256 devices in a mesh: gx: 8 (over z_hi, y), gy: 8 (over x, core), gz: 4 (over z_lo).
Axes of the slice: x: 4, y: 4, z: 8 (z_hi: 2, z_lo: 4; z = z_hi * 4 + z_lo), core: 2. Of those that a mesh axis runs over, the one named last changes fastest.
Arguments:
- gas_state: float32 [5, 64, 128, 512], P(None, 'gx', 'gy', 'gz'), may hold values from -3 to 3, as said below
- parcels: float32 [8192, 5, 128], P(('gx', 'gy', 'gz')), may hold values from -4 to 5, as said below
- parcel_cells: int32 [8192, 128], P(('gx', 'gy', 'gz')), may hold values from 2471 to 20928, as said below
- offsets: float32 [8192, 3, 128], P(('gx', 'gy', 'gz')), may hold values from -0.5 to 0.5
- destination: int32 [8192], P(('gx', 'gy', 'gz')), may hold values from 0 to 26, as said below
- live_blocks: int32 [256], P(('gx', 'gy', 'gz')), may hold values from 4 to 32, as said below
Outputs:
- gas_next: float32 [5, 64, 128, 512], P(None, 'gx', 'gy', 'gz')
- kept: float32 [8192, 5, 128], P(('gx', 'gy', 'gz'))
- arrived: float32 [27648, 5, 128], P(('gx', 'gy', 'gz'))
The draws below stay inside these ranges and needn't reach their ends.
Inputs may be any that keep to these rules, and one draw needn't show every extreme that they name: `gas_state`: field 0 is a vapour fraction within 0 and 0.6, field 1 a temperature within 0.6 and 1.4, fields 2 to 4 velocities. `parcels`: field 0 is a mass within 0.2 and 5, field 1 a temperature within 0.6 and 1.4, fields 2 to 4 velocities. `parcel_cells`: every index is that of an owned cell of the padded brick, 1 to 8, 1 to 16 and 1 to 128 along the three dimensions. Among the blocks of one brick at most 4 name any one destination other than 13; in every draw some brick sends exactly 4 live blocks to one neighbour inside the grid. Destinations of blocks that are not live carry no meaning. Block slots 0 to live_blocks[d] - 1 of brick d are live; in every draw some brick is full.
All inputs are finite; a program needn't handle non-finite values.
Results may differ from the reference program's by a relative error of at most 0.0003.
Values sent between devices are 32-bit elements; how exact they have to be, the bound alone decides.
No kernel may reach another device: no remote copies, remote signals or barrier semaphores. Data moves between devices by JAX's collectives and lax.ppermute only.
A program may use at most 64 MiB of HBM per device.

```python
import math
import jax
import jax.numpy as jnp

CELLS_X = 8
CELLS_Y = 16
CELLS_Z = 128
BLOCKS_DEV = 32
SLOTS = 4
BLOCK_PARCELS = 128
GAS_FIELDS = 5
PARCEL_FIELDS = 5
BRICKS_X = 8
BRICKS_Y = 8
BRICKS_Z = 4
GRID_X = 64
GRID_Y = 128
GRID_Z = 512
BLOCKS = 8192
DEVICES = 256


def draw_gas_state(key, part):
    stochastic_seeds = jax.random.split(key, 3)
    lattice_span = (GRID_X, GRID_Y, GRID_Z)
    steam_concentration = jnp.clip(0.3 + 0.1 * jax.random.normal(stochastic_seeds[0], lattice_span, jnp.float32), 0.0, 0.6)
    parcel_hotness_measure = jnp.clip(1.0 + 0.15 * jax.random.normal(stochastic_seeds[1], lattice_span, jnp.float32), 0.6, 1.4)
    particle_speed_vector = jnp.clip(jax.random.normal(stochastic_seeds[2], (3,) + lattice_span, jnp.float32), -3.0, 3.0)
    return jnp.concatenate([steam_concentration[None], parcel_hotness_measure[None], particle_speed_vector], axis=0)


def draw_parcels(key, part):
    stochastic_seeds = jax.random.split(key, 3)
    lattice_span = (BLOCKS, BLOCK_PARCELS)
    particle_weights_list = jnp.exp(jax.random.uniform(stochastic_seeds[0], lattice_span, jnp.float32, math.log(0.2), math.log(5.0)))
    parcel_hotness_measure = jnp.clip(1.0 + 0.15 * jax.random.normal(stochastic_seeds[1], lattice_span, jnp.float32), 0.6, 1.4)
    particle_speed_vector = jnp.clip(jax.random.normal(stochastic_seeds[2], (BLOCKS, 3, BLOCK_PARCELS), jnp.float32), -4.0, 4.0)
    return jnp.concatenate([particle_weights_list[:, None], parcel_hotness_measure[:, None], particle_speed_vector], axis=1)


def draw_parcel_cells(key, part):
    stochastic_seeds = jax.random.split(key, 5)
    lattice_span = (BLOCKS, BLOCK_PARCELS)
    cell_x = jax.random.randint(stochastic_seeds[0], lattice_span, 1, CELLS_X + 1)
    cell_y = jax.random.randint(stochastic_seeds[1], lattice_span, 1, CELLS_Y + 1)
    cell_z = jax.random.randint(stochastic_seeds[2], lattice_span, 1, CELLS_Z + 1)
    plane_size = (CELLS_Y + 2) * (CELLS_Z + 2)
    result = cell_x * plane_size + cell_y * (CELLS_Z + 2) + cell_z
    upper_row = jax.random.randint(stochastic_seeds[3], (), 0, BLOCKS)
    lower_row = jax.random.randint(stochastic_seeds[4], (), 0, BLOCKS)
    result = result.at[upper_row, 0].set(CELLS_X * plane_size + CELLS_Y * (CELLS_Z + 2) + CELLS_Z)
    result = result.at[lower_row, 1].set(plane_size + CELLS_Z + 3)
    return result.astype(jnp.int32)


def movement(key):
    base_key = jax.random.fold_in(key, 7)
    stochastic_seeds = jax.random.split(base_key, 5)
    bricks = BRICKS_X * BRICKS_Y * BRICKS_Z
    shrink = jax.random.randint(stochastic_seeds[0], (bricks,), 0, 4)
    full_count = jnp.right_shift(jnp.full((bricks,), BLOCKS_DEV, jnp.int32), shrink)
    live_count = full_count - jax.random.randint(stochastic_seeds[1], (bricks,), 0, full_count // 2 + 1)
    live_count = jnp.maximum(live_count, SLOTS)
    busiest = jax.random.randint(stochastic_seeds[2], (), 0, bricks)
    live_count = live_count.at[busiest].set(BLOCKS_DEV)
    target = jax.random.randint(stochastic_seeds[3], (bricks, BLOCKS_DEV), 0, 26)
    target = target + (target >= 13).astype(jnp.int32)
    leaving = jax.random.randint(stochastic_seeds[4], (bricks, BLOCKS_DEV), 0, 10) < 3
    brick_x = busiest // (BRICKS_Y * BRICKS_Z)
    brick_y = busiest // BRICKS_Z % BRICKS_Y
    brick_z = busiest % BRICKS_Z
    forced = jnp.where(brick_x > 0, 0, 2) * 9 + jnp.where(brick_y > 0, 0, 2) * 3 + jnp.where(brick_z > 0, 0, 2)
    forced_rows = (jnp.arange(bricks, dtype=jnp.int32)[:, None] == busiest) & (jnp.arange(BLOCKS_DEV, dtype=jnp.int32)[None, :] < SLOTS)
    target = jnp.where(forced_rows, forced, target)
    leaving = leaving | forced_rows
    one_hot = ((target[:, :, None] == jnp.arange(27, dtype=jnp.int32)[None, None, :]) & leaving[:, :, None]).astype(jnp.int32)
    slot_rank = jnp.sum(jnp.cumsum(one_hot, axis=1) * one_hot, axis=2) - 1
    moving = leaving & (slot_rank < SLOTS)
    dest_grid = jnp.where(moving, target, 13)
    return (live_count.astype(jnp.int32), dest_grid.reshape(-1).astype(jnp.int32))


def draw_destination(key, part):
    return movement(key)[1]


def draw_live_blocks(key, part):
    return movement(key)[0]


def shard_levels(stream_key, dims, cuts, low, largest):
    loudness = 1.0
    for position, blocks in cuts:
        steps = jax.random.uniform(jax.random.fold_in(jax.random.fold_in(stream_key, 6), position), (blocks,), jnp.float32, low / len(cuts), largest / len(cuts))
        loudness = loudness * jnp.repeat(jnp.exp(steps), dims[position] // blocks).reshape((-1,) + (1,) * (len(dims) - 1 - position))
    return loudness


def setup_inputs(seed: int = 0) -> dict:
    key_of = jax.random.split(jax.random.key(seed), 7)
    return {
        "gas_state": draw_gas_state(jax.random.fold_in(key_of[6], 71), 0),
        "parcels": draw_parcels(jax.random.fold_in(key_of[6], 71), 0),
        "parcel_cells": draw_parcel_cells(jax.random.fold_in(key_of[6], 71), 0),
        "offsets": jnp.clip(jax.random.uniform(key_of[3], (BLOCKS, 3, BLOCK_PARCELS), jnp.float32, -0.5, 0.5) * shard_levels(key_of[3], (BLOCKS, 3, BLOCK_PARCELS), ((0, 256),), -0.4, 0.0), -0.5, 0.5),
        "destination": draw_destination(jax.random.fold_in(key_of[6], 71), 0),
        "live_blocks": draw_live_blocks(jax.random.fold_in(key_of[6], 71), 0),
    }


DIFFUSION = (0.06, 0.1, 0.12, 0.12, 0.12)
TIME_STEP = 0.5
COUPLING = 0.5
PHASE_CHANGE_COST = 0.5


def parcel_update(current_condition, local_air_sample):
    particle_weights_list = current_condition[:, 0]
    parcel_hotness_measure = current_condition[:, 1]
    particle_speed_vector = current_condition[:, 2:5]
    relax_time = 0.4 * particle_weights_list ** (2.0 / 3.0)
    keep_velocity = jnp.exp(-TIME_STEP / relax_time)
    residual_heat_content = jnp.exp(-TIME_STEP / (1.5 * relax_time))
    equilibrium_steam_load = 0.4 * jnp.exp(2.0 * (parcel_hotness_measure - 1.0))
    evaporated_share = 1.0 - jnp.exp(-0.3 * jax.nn.softplus(4.0 * (equilibrium_steam_load - local_air_sample[:, 0])))
    evaporated = particle_weights_list * evaporated_share
    ambient_heat_content = local_air_sample[:, 1]
    gas_velocity = local_air_sample[:, 2:5]
    adjusted_heat_content = ambient_heat_content + (parcel_hotness_measure - ambient_heat_content) * residual_heat_content - PHASE_CHANGE_COST * evaporated_share
    velocity_new = gas_velocity + (particle_speed_vector - gas_velocity) * keep_velocity[:, None]
    enthalpy_injection = 0.5 * particle_weights_list * (parcel_hotness_measure - adjusted_heat_content)
    push_source = particle_weights_list[:, None] * (particle_speed_vector - velocity_new)
    updated = jnp.concatenate([(particle_weights_list - evaporated)[:, None], adjusted_heat_content[:, None], velocity_new], axis=1)
    sources = jnp.concatenate([evaporated[:, None], enthalpy_injection[:, None], push_source], axis=1)
    return updated, sources


def laplacian(padded):
    centre = padded[:, 1:-1, 1:-1, 1:-1]
    beside = padded[:, 2:, 1:-1, 1:-1] + padded[:, :-2, 1:-1, 1:-1]
    beside = beside + padded[:, 1:-1, 2:, 1:-1] + padded[:, 1:-1, :-2, 1:-1]
    beside = beside + padded[:, 1:-1, 1:-1, 2:] + padded[:, 1:-1, 1:-1, :-2]
    return beside - 6.0 * centre


def reference(gas_state, parcels, parcel_cells, offsets, destination, live_blocks):
    plane_size = (CELLS_Y + 2) * (CELLS_Z + 2)
    cell_x = parcel_cells // plane_size
    cell_y = (parcel_cells // (CELLS_Z + 2)) % (CELLS_Y + 2)
    cell_z = parcel_cells % (CELLS_Z + 2)
    block_ids = jnp.arange(BLOCKS, dtype=jnp.int32)
    device = block_ids // BLOCKS_DEV
    glob_x = cell_x + ((device // (BRICKS_Y * BRICKS_Z)) * CELLS_X)[:, None]
    glob_y = cell_y + (((device // BRICKS_Z) % BRICKS_Y) * CELLS_Y)[:, None]
    glob_z = cell_z + ((device % BRICKS_Z) * CELLS_Z)[:, None]
    step_sign = jnp.where(offsets >= 0.0, 1, -1).astype(jnp.int32)
    far_share = jnp.abs(offsets)
    near_share = 1.0 - far_share
    padded = jnp.pad(gas_state, ((0, 0), (1, 1), (1, 1), (1, 1)))
    gas_rows = padded.reshape(GAS_FIELDS, -1)
    glob_plane = (GRID_Y + 2) * (GRID_Z + 2)
    weights = []
    indices = []
    for corner in range(8):
        offset_bits = ((corner >> 2) & 1, (corner >> 1) & 1, corner & 1)
        weight = jnp.ones((BLOCKS, BLOCK_PARCELS), jnp.float32)
        for dim_index in range(3):
            weight = weight * (far_share[:, dim_index] if offset_bits[dim_index] else near_share[:, dim_index])
        cell_index = (glob_x + offset_bits[0] * step_sign[:, 0]) * glob_plane
        cell_index = cell_index + (glob_y + offset_bits[1] * step_sign[:, 1]) * (GRID_Z + 2)
        cell_index = cell_index + glob_z + offset_bits[2] * step_sign[:, 2]
        weights.append(weight)
        indices.append(cell_index.astype(jnp.int32))
    local_air_sample = jnp.zeros((BLOCKS, GAS_FIELDS, BLOCK_PARCELS), jnp.float32)
    for weight, cell_index in zip(weights, indices):
        local_air_sample = local_air_sample + weight[:, None] * jnp.moveaxis(gas_rows[:, cell_index], 0, 1)
    updated, sources = parcel_update(parcels, local_air_sample)
    alive_mask = (block_ids % BLOCKS_DEV) < live_blocks[device]
    sources = jnp.where(alive_mask[:, None, None], sources, 0.0)
    moved_sources = jnp.moveaxis(sources, 1, 0)
    deposit = jnp.zeros_like(gas_rows)
    for weight, cell_index in zip(weights, indices):
        deposit = deposit.at[:, cell_index].add(weight[None] * moved_sources)
    deposit = deposit.reshape(padded.shape)
    cell_sources = deposit[:, 1:-1, 1:-1, 1:-1]
    kappa = jnp.array(DIFFUSION, jnp.float32)[:, None, None, None]
    gas_next = gas_state + kappa * laplacian(padded) + COUPLING * cell_sources
    kept = jnp.where((alive_mask & (destination == 13))[:, None, None], updated, 0.0)
    leaving = (alive_mask & (destination != 13)).reshape(DEVICES, BLOCKS_DEV)
    dest_grid = destination.reshape(DEVICES, BLOCKS_DEV)
    one_hot = ((dest_grid[:, :, None] == jnp.arange(27, dtype=jnp.int32)[None, None, :]) & leaving[:, :, None]).astype(jnp.int32)
    slot_rank = jnp.sum(jnp.cumsum(one_hot, axis=1) * one_hot, axis=2) - 1
    slot_index = jnp.where(leaving, dest_grid * SLOTS + slot_rank, 27 * SLOTS).astype(jnp.int32)
    device_rows = jnp.broadcast_to(jnp.arange(DEVICES, dtype=jnp.int32)[:, None], (DEVICES, BLOCKS_DEV))
    outboxes = jnp.zeros((DEVICES, 27 * SLOTS + 1, PARCEL_FIELDS, BLOCK_PARCELS), jnp.float32)
    outboxes = outboxes.at[device_rows, slot_index].set(updated.reshape(DEVICES, BLOCKS_DEV, PARCEL_FIELDS, BLOCK_PARCELS))
    outboxes = outboxes[:, :27 * SLOTS].reshape(BRICKS_X, BRICKS_Y, BRICKS_Z, 3, 3, 3, SLOTS, PARCEL_FIELDS, BLOCK_PARCELS)
    outboxes = jnp.pad(outboxes, ((1, 1), (1, 1), (1, 1), (0, 0), (0, 0), (0, 0), (0, 0), (0, 0), (0, 0)))
    pieces = []
    for first in range(3):
        for second in range(3):
            for third in range(3):
                pieces.append(outboxes[first:first + BRICKS_X, second:second + BRICKS_Y, third:third + BRICKS_Z, 2 - first, 2 - second, 2 - third])
    arrived = jnp.stack(pieces, axis=3).reshape(DEVICES * 27 * SLOTS, PARCEL_FIELDS, BLOCK_PARCELS)
    return gas_next, kept, arrived
```

```python
import jax
import jax.numpy as jnp
from jax import lax
from jax.sharding import PartitionSpec as P

SLOTS = 4


DIFFUSION = (0.06, 0.1, 0.12, 0.12, 0.12)
TIME_STEP = 0.5
COUPLING = 0.5
PHASE_CHANGE_COST = 0.5
GROUP_BLOCKS = 8


def with_halo(block, sides, width):
    for axis, dim in sides:
        count = lax.axis_size(axis)
        forward = [(i, i + 1) for i in range(count - 1)]
        backward = [(target, source) for source, target in forward]
        low = lax.ppermute(
            lax.slice_in_dim(block, block.shape[dim] - width, None, axis=dim), axis, forward
        )
        high = lax.ppermute(lax.slice_in_dim(block, 0, width, axis=dim), axis, backward)
        block = jnp.concatenate([low, block, high], axis=dim)
    return block


def fold_ghosts(block, sides):
    for axis, dim in sides:
        count = lax.axis_size(axis)
        forward = [(i, i + 1) for i in range(count - 1)]
        backward = [(target, source) for source, target in forward]
        span = block.shape[dim]
        below = lax.ppermute(lax.slice_in_dim(block, span - 1, span, axis=dim), axis, forward)
        above = lax.ppermute(lax.slice_in_dim(block, 0, 1, axis=dim), axis, backward)
        inner = lax.slice_in_dim(block, 1, span - 1, axis=dim)
        low_pad = [(0, 0)] * block.ndim
        high_pad = [(0, 0)] * block.ndim
        low_pad[dim] = (0, span - 3)
        high_pad[dim] = (span - 3, 0)
        block = inner + jnp.pad(below, low_pad) + jnp.pad(above, high_pad)
    return block


def parcel_update(current_condition, local_air_sample):
    particle_weights_list = current_condition[:, 0]
    parcel_hotness_measure = current_condition[:, 1]
    particle_speed_vector = current_condition[:, 2:5]
    relax_time = 0.4 * particle_weights_list ** (2.0 / 3.0)
    keep_velocity = jnp.exp(-TIME_STEP / relax_time)
    residual_heat_content = jnp.exp(-TIME_STEP / (1.5 * relax_time))
    equilibrium_steam_load = 0.4 * jnp.exp(2.0 * (parcel_hotness_measure - 1.0))
    evaporated_share = 1.0 - jnp.exp(
        -0.3 * jax.nn.softplus(4.0 * (equilibrium_steam_load - local_air_sample[:, 0]))
    )
    evaporated = particle_weights_list * evaporated_share
    ambient_heat_content = local_air_sample[:, 1]
    gas_velocity = local_air_sample[:, 2:5]
    adjusted_heat_content = (
        ambient_heat_content
        + (parcel_hotness_measure - ambient_heat_content) * residual_heat_content
        - PHASE_CHANGE_COST * evaporated_share
    )
    velocity_new = gas_velocity + (particle_speed_vector - gas_velocity) * keep_velocity[:, None]
    enthalpy_injection = (
        0.5 * particle_weights_list * (parcel_hotness_measure - adjusted_heat_content)
    )
    push_source = particle_weights_list[:, None] * (particle_speed_vector - velocity_new)
    updated = jnp.concatenate(
        [
            (particle_weights_list - evaporated)[:, None],
            adjusted_heat_content[:, None],
            velocity_new,
        ],
        axis=1,
    )
    sources = jnp.concatenate(
        [evaporated[:, None], enthalpy_injection[:, None], push_source], axis=1
    )
    return (updated, sources)


def laplacian(padded):
    centre = padded[:, 1:-1, 1:-1, 1:-1]
    beside = padded[:, 2:, 1:-1, 1:-1] + padded[:, :-2, 1:-1, 1:-1]
    beside = beside + padded[:, 1:-1, 2:, 1:-1] + padded[:, 1:-1, :-2, 1:-1]
    beside = beside + padded[:, 1:-1, 1:-1, 2:] + padded[:, 1:-1, 1:-1, :-2]
    return beside - 6.0 * centre


def local(gas_state, parcels, parcel_cells, offsets, destination, live_blocks):
    fields, size_x, size_y, size_z = gas_state.shape
    blocks, parcel_fields, block_parcels = parcels.shape
    padded = with_halo(gas_state, (("gx", 1), ("gy", 2), ("gz", 3)), 1)
    span_x = size_x + 2
    span_y = size_y + 2
    span_z = size_z + 2
    pair_count = span_x * span_y
    plane_size = span_y * span_z
    table = jnp.transpose(padded.reshape(fields, pair_count, span_z), (1, 0, 2)).reshape(
        pair_count, fields * span_z
    )
    alive_mask = jnp.arange(blocks, dtype=jnp.int32) < live_blocks[0]
    turns = blocks // GROUP_BLOCKS
    rows = GROUP_BLOCKS * block_parcels
    pair_iota = jnp.arange(pair_count, dtype=jnp.int32)
    depth_iota = jnp.arange(span_z, dtype=jnp.int32)

    def group_step(total, item):
        group_parcels, group_cells, group_offsets, group_alive = item
        cells = group_cells.reshape(rows)
        shifts = jnp.transpose(group_offsets, (1, 0, 2)).reshape(3, rows)
        cell_x = cells // plane_size
        cell_y = cells // span_z % span_y
        cell_z = cells % span_z
        step_sign = jnp.where(shifts >= 0.0, 1, -1).astype(jnp.int32)
        far_share = jnp.abs(shifts)
        near_share = 1.0 - far_share
        pair_weights = jnp.zeros((rows, pair_count), jnp.float32)
        for bit_x in range(2):
            for bit_y in range(2):
                share = (far_share[0] if bit_x else near_share[0]) * (
                    far_share[1] if bit_y else near_share[1]
                )
                target = (cell_x + bit_x * step_sign[0]) * span_y + cell_y + bit_y * step_sign[1]
                pair_weights = pair_weights + jnp.where(
                    pair_iota[None, :] == target[:, None], share[:, None], 0.0
                )
        depth_weights = jnp.where(
            depth_iota[None, :] == cell_z[:, None], near_share[2][:, None], 0.0
        )
        depth_weights = depth_weights + jnp.where(
            depth_iota[None, :] == (cell_z + step_sign[2])[:, None], far_share[2][:, None], 0.0
        )
        mixed = jnp.dot(pair_weights, table, precision=lax.Precision.HIGHEST).reshape(
            rows, fields, span_z
        )
        sample = jnp.sum(mixed * depth_weights[:, None, :], axis=2)
        sample_blocks = jnp.transpose(
            sample.reshape(GROUP_BLOCKS, block_parcels, fields), (0, 2, 1)
        )
        updated, sources = parcel_update(group_parcels, sample_blocks)
        sources = jnp.where(group_alive[:, None, None], sources, 0.0)
        source_rows = jnp.transpose(sources, (0, 2, 1)).reshape(rows, fields)
        spread = (source_rows[:, :, None] * depth_weights[:, None, :]).reshape(
            rows, fields * span_z
        )
        total = total + lax.dot_general(
            pair_weights, spread, (((0,), (0,)), ((), ())), precision=lax.Precision.HIGHEST
        )
        return (total, updated)

    inputs = (
        parcels.reshape(turns, GROUP_BLOCKS, parcel_fields, block_parcels),
        parcel_cells.reshape(turns, GROUP_BLOCKS, block_parcels),
        offsets.reshape(turns, GROUP_BLOCKS, 3, block_parcels),
        alive_mask.reshape(turns, GROUP_BLOCKS),
    )
    deposit_rows, updated = lax.scan(
        group_step, jnp.zeros((pair_count, fields * span_z), jnp.float32), inputs
    )
    updated = updated.reshape(blocks, parcel_fields, block_parcels)
    deposit = jnp.transpose(deposit_rows.reshape(span_x, span_y, fields, span_z), (2, 0, 1, 3))
    cell_sources = fold_ghosts(deposit, (("gx", 1), ("gy", 2), ("gz", 3)))
    kappa = jnp.array(DIFFUSION, jnp.float32)[:, None, None, None]
    gas_next = gas_state + kappa * laplacian(padded) + COUPLING * cell_sources
    kept = jnp.where((alive_mask & (destination == 13))[:, None, None], updated, 0.0)
    leaving = alive_mask & (destination != 13)
    one_hot = (
        (destination[:, None] == jnp.arange(27, dtype=jnp.int32)[None, :]) & leaving[:, None]
    ).astype(jnp.int32)
    slot_rank = jnp.sum(jnp.cumsum(one_hot, axis=0) * one_hot, axis=1) - 1
    slot_index = jnp.where(leaving, destination * SLOTS + slot_rank, -1)
    selector = (jnp.arange(27 * SLOTS, dtype=jnp.int32)[:, None] == slot_index[None, :]).astype(
        jnp.float32
    )
    outbox = jnp.dot(selector, updated.reshape(blocks, -1), precision=lax.Precision.HIGHEST)
    outbox = outbox.reshape((3, 3, 3, SLOTS) + parcels.shape[1:])
    widened = with_halo(outbox, (("gx", 0), ("gy", 1), ("gz", 2)), 1)
    arrived_boxes = widened[0::2, 0::2, 0::2]
    arrived = arrived_boxes.reshape((27 * SLOTS,) + parcels.shape[1:])
    return (gas_next, kept, arrived)


def solution(mesh):
    placed = (
        P(None, "gx", "gy", "gz"),
        P(("gx", "gy", "gz"), None, None),
        P(("gx", "gy", "gz"), None),
        P(("gx", "gy", "gz"), None, None),
        P(("gx", "gy", "gz")),
        P(("gx", "gy", "gz")),
    )
    return jax.shard_map(
        local,
        mesh=mesh,
        in_specs=placed,
        out_specs=(
            P(None, "gx", "gy", "gz"),
            P(("gx", "gy", "gz"), None, None),
            P(("gx", "gy", "gz"), None, None),
        ),
        check_vma=False,
    )
```

```python
import jax
import jax.numpy as jnp
from jax import lax
from jax.sharding import PartitionSpec as P
from jax.experimental import pallas as pl
from jax.experimental.pallas import tpu as pltpu

SLOTS = 4


DIFFUSION = (0.06, 0.1, 0.12, 0.12, 0.12)
TIME_STEP = 0.5
COUPLING = 0.5
PHASE_CHANGE_COST = 0.5


def with_halo(block, sides, width):
    for axis, dim in sides:
        count = lax.axis_size(axis)
        forward = [(i, i + 1) for i in range(count - 1)]
        backward = [(target, source) for source, target in forward]
        low = lax.ppermute(
            lax.slice_in_dim(block, block.shape[dim] - width, None, axis=dim), axis, forward
        )
        high = lax.ppermute(lax.slice_in_dim(block, 0, width, axis=dim), axis, backward)
        block = jnp.concatenate([low, block, high], axis=dim)
    return block


def fold_ghosts(block, sides):
    for axis, dim in sides:
        count = lax.axis_size(axis)
        forward = [(i, i + 1) for i in range(count - 1)]
        backward = [(target, source) for source, target in forward]
        span = block.shape[dim]
        below = lax.ppermute(lax.slice_in_dim(block, span - 1, span, axis=dim), axis, forward)
        above = lax.ppermute(lax.slice_in_dim(block, 0, 1, axis=dim), axis, backward)
        inner = lax.slice_in_dim(block, 1, span - 1, axis=dim)
        low_pad = [(0, 0)] * block.ndim
        high_pad = [(0, 0)] * block.ndim
        low_pad[dim] = (0, span - 3)
        high_pad[dim] = (span - 3, 0)
        block = inner + jnp.pad(below, low_pad) + jnp.pad(above, high_pad)
    return block


def parcel_update(current_condition, local_air_sample):
    particle_weights_list = current_condition[:, 0]
    parcel_hotness_measure = current_condition[:, 1]
    particle_speed_vector = current_condition[:, 2:5]
    relax_time = 0.4 * particle_weights_list ** (2.0 / 3.0)
    keep_velocity = jnp.exp(-TIME_STEP / relax_time)
    residual_heat_content = jnp.exp(-TIME_STEP / (1.5 * relax_time))
    equilibrium_steam_load = 0.4 * jnp.exp(2.0 * (parcel_hotness_measure - 1.0))
    evaporated_share = 1.0 - jnp.exp(
        -0.3 * jax.nn.softplus(4.0 * (equilibrium_steam_load - local_air_sample[:, 0]))
    )
    evaporated = particle_weights_list * evaporated_share
    ambient_heat_content = local_air_sample[:, 1]
    gas_velocity = local_air_sample[:, 2:5]
    adjusted_heat_content = (
        ambient_heat_content
        + (parcel_hotness_measure - ambient_heat_content) * residual_heat_content
        - PHASE_CHANGE_COST * evaporated_share
    )
    velocity_new = gas_velocity + (particle_speed_vector - gas_velocity) * keep_velocity[:, None]
    enthalpy_injection = (
        0.5 * particle_weights_list * (parcel_hotness_measure - adjusted_heat_content)
    )
    push_source = particle_weights_list[:, None] * (particle_speed_vector - velocity_new)
    updated = jnp.concatenate(
        [
            (particle_weights_list - evaporated)[:, None],
            adjusted_heat_content[:, None],
            velocity_new,
        ],
        axis=1,
    )
    sources = jnp.concatenate(
        [evaporated[:, None], enthalpy_injection[:, None], push_source], axis=1
    )
    return (updated, sources)


def laplacian(padded):
    centre = padded[:, 1:-1, 1:-1, 1:-1]
    beside = padded[:, 2:, 1:-1, 1:-1] + padded[:, :-2, 1:-1, 1:-1]
    beside = beside + padded[:, 1:-1, 2:, 1:-1] + padded[:, 1:-1, :-2, 1:-1]
    beside = beside + padded[:, 1:-1, 1:-1, 2:] + padded[:, 1:-1, 1:-1, :-2]
    return beside - 6.0 * centre


PAIR_LANES = 256
DEPTH_ROWS = 136


def split_bf16(value):
    high = value.astype(jnp.bfloat16)
    low = (value - high.astype(jnp.float32)).astype(jnp.bfloat16)
    return high, low


def three_pass(a, b, dims):
    a_high, a_low = split_bf16(a)
    b_high, b_low = split_bf16(b)
    out = None
    for x, y in ((a_high, b_high), (a_high, b_low), (a_low, b_high)):
        part = lax.dot_general(x, y, (dims, ((), ())), preferred_element_type=jnp.float32)
        out = part if out is None else out + part
    return out


def coupling_kernel(
    live_ref, table_ref, parcel_ref, pair_ref, pair_share_ref, depth_ref, depth_share_ref,
    factor_ref, updated_ref, deposit_ref,
):
    fields = parcel_ref.shape[1]
    blocks = parcel_ref.shape[0]
    lanes = parcel_ref.shape[2]
    deposit_ref[...] = jnp.zeros(deposit_ref.shape, jnp.float32)
    live = live_ref[0]
    pair_iota = lax.broadcasted_iota(jnp.int32, (PAIR_LANES, lanes), 0)
    depth_iota = lax.broadcasted_iota(jnp.int32, (DEPTH_ROWS, lanes), 0)

    def body(b, carry):
        pair = pair_ref[b]
        pair_share = pair_share_ref[b]
        weights = jnp.zeros((PAIR_LANES, lanes), jnp.float32)
        for c in range(4):
            weights = weights + jnp.where(pair_iota == pair[c:c + 1], pair_share[c:c + 1], 0.0)
        depth = depth_ref[b]
        depth_share = depth_share_ref[b]
        depth_weights = jnp.where(depth_iota == depth[0:1], depth_share[0:1], 0.0)
        depth_weights = depth_weights + jnp.where(
            depth_iota == depth[1:2], depth_share[1:2], 0.0
        )
        mixed = three_pass(table_ref[...], weights, ((1,), (0,)))
        sample = [
            jnp.sum(
                mixed[f * DEPTH_ROWS:(f + 1) * DEPTH_ROWS] * depth_weights, axis=0, keepdims=True
            )
            for f in range(fields)
        ]
        current = parcel_ref[b]
        factors = factor_ref[b]
        mass = current[0:1]
        heat = current[1:2]
        keep_velocity = factors[0:1]
        residual_heat = factors[1:2]
        equilibrium = factors[2:3]
        x = 4.0 * (equilibrium - sample[0])
        soft = jnp.maximum(x, 0.0) + jnp.log1p(jnp.exp(-jnp.abs(x)))
        share = 1.0 - jnp.exp(-0.3 * soft)
        evaporated = mass * share
        ambient = sample[1]
        adjusted = ambient + (heat - ambient) * residual_heat - PHASE_CHANGE_COST * share
        velocity = [
            sample[2 + d] + (current[2 + d:3 + d] - sample[2 + d]) * keep_velocity
            for d in range(3)
        ]
        enthalpy = 0.5 * mass * (heat - adjusted)
        push = [mass * (current[2 + d:3 + d] - velocity[d]) for d in range(3)]
        updated_ref[b] = jnp.concatenate([mass - evaporated, adjusted] + velocity, axis=0)
        alive = b < live
        sources = [jnp.where(alive, s, 0.0) for s in [evaporated, enthalpy] + push]
        spread = jnp.concatenate([s * depth_weights for s in sources], axis=0)
        deposit_ref[...] += three_pass(spread, weights, ((1,), (1,)))
        return carry

    lax.fori_loop(0, blocks, body, 0)


def local(gas_state, parcels, parcel_cells, offsets, destination, live_blocks):
    fields, size_x, size_y, size_z = gas_state.shape
    blocks, parcel_fields, block_parcels = parcels.shape
    padded = with_halo(gas_state, (("gx", 1), ("gy", 2), ("gz", 3)), 1)
    span_x = size_x + 2
    span_y = size_y + 2
    span_z = size_z + 2
    pair_count = span_x * span_y
    plane_size = span_y * span_z
    table = jnp.transpose(padded, (0, 3, 1, 2)).reshape(fields, span_z, pair_count)
    table = jnp.pad(table, ((0, 0), (0, DEPTH_ROWS - span_z), (0, PAIR_LANES - pair_count)))
    table = table.reshape(fields * DEPTH_ROWS, PAIR_LANES)
    alive_mask = jnp.arange(blocks, dtype=jnp.int32) < live_blocks[0]
    cell_x = parcel_cells // plane_size
    cell_y = parcel_cells // span_z % span_y
    cell_z = parcel_cells % span_z
    step_sign = jnp.where(offsets >= 0.0, 1, -1).astype(jnp.int32)
    far_share = jnp.abs(offsets)
    near_share = 1.0 - far_share
    pairs = []
    pair_shares = []
    for bit_x in range(2):
        for bit_y in range(2):
            pair_shares.append(
                (far_share[:, 0] if bit_x else near_share[:, 0])
                * (far_share[:, 1] if bit_y else near_share[:, 1])
            )
            pairs.append(
                (cell_x + bit_x * step_sign[:, 0]) * span_y + cell_y + bit_y * step_sign[:, 1]
            )
    pairs = jnp.stack(pairs, axis=1)
    pair_shares = jnp.stack(pair_shares, axis=1)
    depths = jnp.stack([cell_z, cell_z + step_sign[:, 2]], axis=1)
    depth_shares = jnp.stack([near_share[:, 2], far_share[:, 2]], axis=1)
    relax_time = 0.4 * parcels[:, 0] ** (2.0 / 3.0)
    factors = jnp.stack(
        [
            jnp.exp(-TIME_STEP / relax_time),
            jnp.exp(-TIME_STEP / (1.5 * relax_time)),
            0.4 * jnp.exp(2.0 * (parcels[:, 1] - 1.0)),
        ],
        axis=1,
    )
    vmem = pl.BlockSpec(memory_space=pltpu.VMEM)
    updated, deposit_rows = pl.pallas_call(
        coupling_kernel,
        out_shape=(
            jax.ShapeDtypeStruct(parcels.shape, jnp.float32),
            jax.ShapeDtypeStruct((fields * DEPTH_ROWS, PAIR_LANES), jnp.float32),
        ),
        in_specs=[pl.BlockSpec(memory_space=pltpu.SMEM)] + [vmem] * 7,
        out_specs=(vmem, vmem),
    )(live_blocks, table, parcels, pairs, pair_shares, depths, depth_shares, factors)
    deposit = deposit_rows.reshape(fields, DEPTH_ROWS, PAIR_LANES)[:, :span_z, :pair_count]
    deposit = jnp.transpose(deposit.reshape(fields, span_z, span_x, span_y), (0, 2, 3, 1))
    cell_sources = fold_ghosts(deposit, (("gx", 1), ("gy", 2), ("gz", 3)))
    kappa = jnp.array(DIFFUSION, jnp.float32)[:, None, None, None]
    gas_next = gas_state + kappa * laplacian(padded) + COUPLING * cell_sources
    kept = jnp.where((alive_mask & (destination == 13))[:, None, None], updated, 0.0)
    leaving = alive_mask & (destination != 13)
    one_hot = (
        (destination[:, None] == jnp.arange(27, dtype=jnp.int32)[None, :]) & leaving[:, None]
    ).astype(jnp.int32)
    slot_rank = jnp.sum(jnp.cumsum(one_hot, axis=0) * one_hot, axis=1) - 1
    slot_index = jnp.where(leaving, destination * SLOTS + slot_rank, -1)
    selector = (jnp.arange(27 * SLOTS, dtype=jnp.int32)[:, None] == slot_index[None, :]).astype(
        jnp.float32
    )
    outbox = jnp.dot(selector, updated.reshape(blocks, -1), precision=lax.Precision.HIGHEST)
    outbox = outbox.reshape((3, 3, 3, SLOTS) + parcels.shape[1:])
    widened = with_halo(outbox, (("gx", 0), ("gy", 1), ("gz", 2)), 1)
    arrived_boxes = widened[0::2, 0::2, 0::2]
    arrived = arrived_boxes.reshape((27 * SLOTS,) + parcels.shape[1:])
    return (gas_next, kept, arrived)


def solution(mesh):
    placed = (
        P(None, "gx", "gy", "gz"),
        P(("gx", "gy", "gz"), None, None),
        P(("gx", "gy", "gz"), None),
        P(("gx", "gy", "gz"), None, None),
        P(("gx", "gy", "gz")),
        P(("gx", "gy", "gz")),
    )
    return jax.shard_map(
        local,
        mesh=mesh,
        in_specs=placed,
        out_specs=(
            P(None, "gx", "gy", "gz"),
            P(("gx", "gy", "gz"), None, None),
            P(("gx", "gy", "gz"), None, None),
        ),
        check_vma=False,
    )
```

```python
import jax
import jax.numpy as jnp
from jax import lax
from jax.sharding import PartitionSpec as P
from jax.experimental import pallas as pl
from jax.experimental.pallas import tpu as pltpu

SLOTS = 4


DIFFUSION = (0.06, 0.1, 0.12, 0.12, 0.12)
TIME_STEP = 0.5
COUPLING = 0.5
PHASE_CHANGE_COST = 0.5


def with_halo(block, sides, width):
    for axis, dim in sides:
        count = lax.axis_size(axis)
        forward = [(i, i + 1) for i in range(count - 1)]
        backward = [(target, source) for source, target in forward]
        low = lax.ppermute(
            lax.slice_in_dim(block, block.shape[dim] - width, None, axis=dim), axis, forward
        )
        high = lax.ppermute(lax.slice_in_dim(block, 0, width, axis=dim), axis, backward)
        block = jnp.concatenate([low, block, high], axis=dim)
    return block


def fold_ghosts(block, sides):
    for axis, dim in sides:
        count = lax.axis_size(axis)
        forward = [(i, i + 1) for i in range(count - 1)]
        backward = [(target, source) for source, target in forward]
        span = block.shape[dim]
        below = lax.ppermute(lax.slice_in_dim(block, span - 1, span, axis=dim), axis, forward)
        above = lax.ppermute(lax.slice_in_dim(block, 0, 1, axis=dim), axis, backward)
        inner = lax.slice_in_dim(block, 1, span - 1, axis=dim)
        low_pad = [(0, 0)] * block.ndim
        high_pad = [(0, 0)] * block.ndim
        low_pad[dim] = (0, span - 3)
        high_pad[dim] = (span - 3, 0)
        block = inner + jnp.pad(below, low_pad) + jnp.pad(above, high_pad)
    return block


def pack_rows(parts):
    flat = jnp.concatenate([p.reshape(-1) for p in parts])
    extra = -flat.shape[0] % 128
    return jnp.pad(flat, (0, extra)).reshape(-1, 128)


def unpack_rows(rows, shapes):
    flat = rows.reshape(-1)
    parts = []
    at = 0
    for shape in shapes:
        size = 1
        for n in shape:
            size *= n
        parts.append(flat[at:at + size].reshape(shape))
        at += size
    return parts


def fold_and_widen(block, boxes, sides):
    for axis, dim, box_dim in sides:
        count = lax.axis_size(axis)
        forward = [(i, i + 1) for i in range(count - 1)]
        backward = [(target, source) for source, target in forward]
        span = block.shape[dim]
        width = boxes.shape[box_dim]
        up = [
            lax.slice_in_dim(block, span - 1, span, axis=dim),
            lax.slice_in_dim(boxes, width - 1, width, axis=box_dim),
        ]
        down = [lax.slice_in_dim(block, 0, 1, axis=dim), lax.slice_in_dim(boxes, 0, 1, axis=box_dim)]
        shapes = [p.shape for p in up]
        below = unpack_rows(lax.ppermute(pack_rows(up), axis, forward), shapes)
        above = unpack_rows(lax.ppermute(pack_rows(down), axis, backward), shapes)
        inner = lax.slice_in_dim(block, 1, span - 1, axis=dim)
        low_pad = [(0, 0)] * block.ndim
        high_pad = [(0, 0)] * block.ndim
        low_pad[dim] = (0, span - 3)
        high_pad[dim] = (span - 3, 0)
        block = inner + jnp.pad(below[0], low_pad) + jnp.pad(above[0], high_pad)
        boxes = jnp.concatenate([below[1], boxes, above[1]], axis=box_dim)
    return block, boxes


def parcel_update(current_condition, local_air_sample):
    particle_weights_list = current_condition[:, 0]
    parcel_hotness_measure = current_condition[:, 1]
    particle_speed_vector = current_condition[:, 2:5]
    relax_time = 0.4 * particle_weights_list ** (2.0 / 3.0)
    keep_velocity = jnp.exp(-TIME_STEP / relax_time)
    residual_heat_content = jnp.exp(-TIME_STEP / (1.5 * relax_time))
    equilibrium_steam_load = 0.4 * jnp.exp(2.0 * (parcel_hotness_measure - 1.0))
    evaporated_share = 1.0 - jnp.exp(
        -0.3 * jax.nn.softplus(4.0 * (equilibrium_steam_load - local_air_sample[:, 0]))
    )
    evaporated = particle_weights_list * evaporated_share
    ambient_heat_content = local_air_sample[:, 1]
    gas_velocity = local_air_sample[:, 2:5]
    adjusted_heat_content = (
        ambient_heat_content
        + (parcel_hotness_measure - ambient_heat_content) * residual_heat_content
        - PHASE_CHANGE_COST * evaporated_share
    )
    velocity_new = gas_velocity + (particle_speed_vector - gas_velocity) * keep_velocity[:, None]
    enthalpy_injection = (
        0.5 * particle_weights_list * (parcel_hotness_measure - adjusted_heat_content)
    )
    push_source = particle_weights_list[:, None] * (particle_speed_vector - velocity_new)
    updated = jnp.concatenate(
        [
            (particle_weights_list - evaporated)[:, None],
            adjusted_heat_content[:, None],
            velocity_new,
        ],
        axis=1,
    )
    sources = jnp.concatenate(
        [evaporated[:, None], enthalpy_injection[:, None], push_source], axis=1
    )
    return (updated, sources)


def laplacian(padded):
    centre = padded[:, 1:-1, 1:-1, 1:-1]
    beside = padded[:, 2:, 1:-1, 1:-1] + padded[:, :-2, 1:-1, 1:-1]
    beside = beside + padded[:, 1:-1, 2:, 1:-1] + padded[:, 1:-1, :-2, 1:-1]
    beside = beside + padded[:, 1:-1, 1:-1, 2:] + padded[:, 1:-1, 1:-1, :-2]
    return beside - 6.0 * centre


PAIR_LANES = 256
DEPTH_ROWS = 136


def split_bf16(value):
    high = value.astype(jnp.bfloat16)
    low = (value - high.astype(jnp.float32)).astype(jnp.bfloat16)
    return high, low


def three_pass(a, b, dims):
    a_high, a_low = split_bf16(a)
    b_high, b_low = split_bf16(b)
    out = None
    for x, y in ((a_high, b_high), (a_high, b_low), (a_low, b_high)):
        part = lax.dot_general(x, y, (dims, ((), ())), preferred_element_type=jnp.float32)
        out = part if out is None else out + part
    return out


def coupling_kernel(
    live_ref, table_ref, parcel_ref, pair_ref, pair_share_ref, depth_ref, depth_share_ref,
    factor_ref, updated_ref, deposit_ref,
):
    fields = parcel_ref.shape[1]
    blocks = parcel_ref.shape[0]
    lanes = parcel_ref.shape[2]
    deposit_ref[...] = jnp.zeros(deposit_ref.shape, jnp.float32)
    live = live_ref[0]
    pair_iota = lax.broadcasted_iota(jnp.int32, (PAIR_LANES, lanes), 0)
    depth_iota = lax.broadcasted_iota(jnp.int32, (DEPTH_ROWS, lanes), 0)

    def body(b, carry):
        pair = pair_ref[b]
        pair_share = pair_share_ref[b]
        weights = jnp.zeros((PAIR_LANES, lanes), jnp.float32)
        for c in range(4):
            weights = weights + jnp.where(pair_iota == pair[c:c + 1], pair_share[c:c + 1], 0.0)
        depth = depth_ref[b]
        depth_share = depth_share_ref[b]
        depth_weights = jnp.where(depth_iota == depth[0:1], depth_share[0:1], 0.0)
        depth_weights = depth_weights + jnp.where(
            depth_iota == depth[1:2], depth_share[1:2], 0.0
        )
        mixed = three_pass(table_ref[...], weights, ((1,), (0,)))
        sample = [
            jnp.sum(
                mixed[f * DEPTH_ROWS:(f + 1) * DEPTH_ROWS] * depth_weights, axis=0, keepdims=True
            )
            for f in range(fields)
        ]
        current = parcel_ref[b]
        factors = factor_ref[b]
        mass = current[0:1]
        heat = current[1:2]
        keep_velocity = factors[0:1]
        residual_heat = factors[1:2]
        equilibrium = factors[2:3]
        x = 4.0 * (equilibrium - sample[0])
        soft = jnp.maximum(x, 0.0) + jnp.log1p(jnp.exp(-jnp.abs(x)))
        share = 1.0 - jnp.exp(-0.3 * soft)
        evaporated = mass * share
        ambient = sample[1]
        adjusted = ambient + (heat - ambient) * residual_heat - PHASE_CHANGE_COST * share
        velocity = [
            sample[2 + d] + (current[2 + d:3 + d] - sample[2 + d]) * keep_velocity
            for d in range(3)
        ]
        enthalpy = 0.5 * mass * (heat - adjusted)
        push = [mass * (current[2 + d:3 + d] - velocity[d]) for d in range(3)]
        updated_ref[b] = jnp.concatenate([mass - evaporated, adjusted] + velocity, axis=0)
        alive = b < live
        sources = [jnp.where(alive, s, 0.0) for s in [evaporated, enthalpy] + push]
        spread = jnp.concatenate([s * depth_weights for s in sources], axis=0)
        deposit_ref[...] += three_pass(spread, weights, ((1,), (1,)))
        return carry

    lax.fori_loop(0, blocks, body, 0)


def local(gas_state, parcels, parcel_cells, offsets, destination, live_blocks):
    fields, size_x, size_y, size_z = gas_state.shape
    blocks, parcel_fields, block_parcels = parcels.shape
    padded = with_halo(gas_state, (("gx", 1), ("gy", 2), ("gz", 3)), 1)
    span_x = size_x + 2
    span_y = size_y + 2
    span_z = size_z + 2
    pair_count = span_x * span_y
    plane_size = span_y * span_z
    table = jnp.transpose(padded, (0, 3, 1, 2)).reshape(fields, span_z, pair_count)
    table = jnp.pad(table, ((0, 0), (0, DEPTH_ROWS - span_z), (0, PAIR_LANES - pair_count)))
    table = table.reshape(fields * DEPTH_ROWS, PAIR_LANES)
    alive_mask = jnp.arange(blocks, dtype=jnp.int32) < live_blocks[0]
    cell_x = parcel_cells // plane_size
    cell_y = parcel_cells // span_z % span_y
    cell_z = parcel_cells % span_z
    step_sign = jnp.where(offsets >= 0.0, 1, -1).astype(jnp.int32)
    far_share = jnp.abs(offsets)
    near_share = 1.0 - far_share
    pairs = []
    pair_shares = []
    for bit_x in range(2):
        for bit_y in range(2):
            pair_shares.append(
                (far_share[:, 0] if bit_x else near_share[:, 0])
                * (far_share[:, 1] if bit_y else near_share[:, 1])
            )
            pairs.append(
                (cell_x + bit_x * step_sign[:, 0]) * span_y + cell_y + bit_y * step_sign[:, 1]
            )
    pairs = jnp.stack(pairs, axis=1)
    pair_shares = jnp.stack(pair_shares, axis=1)
    depths = jnp.stack([cell_z, cell_z + step_sign[:, 2]], axis=1)
    depth_shares = jnp.stack([near_share[:, 2], far_share[:, 2]], axis=1)
    relax_time = 0.4 * parcels[:, 0] ** (2.0 / 3.0)
    factors = jnp.stack(
        [
            jnp.exp(-TIME_STEP / relax_time),
            jnp.exp(-TIME_STEP / (1.5 * relax_time)),
            0.4 * jnp.exp(2.0 * (parcels[:, 1] - 1.0)),
        ],
        axis=1,
    )
    vmem = pl.BlockSpec(memory_space=pltpu.VMEM)
    updated, deposit_rows = pl.pallas_call(
        coupling_kernel,
        out_shape=(
            jax.ShapeDtypeStruct(parcels.shape, jnp.float32),
            jax.ShapeDtypeStruct((fields * DEPTH_ROWS, PAIR_LANES), jnp.float32),
        ),
        in_specs=[pl.BlockSpec(memory_space=pltpu.SMEM)] + [vmem] * 7,
        out_specs=(vmem, vmem),
    )(live_blocks, table, parcels, pairs, pair_shares, depths, depth_shares, factors)
    deposit = deposit_rows.reshape(fields, DEPTH_ROWS, PAIR_LANES)[:, :span_z, :pair_count]
    deposit = jnp.transpose(deposit.reshape(fields, span_z, span_x, span_y), (0, 2, 3, 1))
    kept = jnp.where((alive_mask & (destination == 13))[:, None, None], updated, 0.0)
    leaving = alive_mask & (destination != 13)
    one_hot = (
        (destination[:, None] == jnp.arange(27, dtype=jnp.int32)[None, :]) & leaving[:, None]
    ).astype(jnp.int32)
    slot_rank = jnp.sum(jnp.cumsum(one_hot, axis=0) * one_hot, axis=1) - 1
    slot_index = jnp.where(leaving, destination * SLOTS + slot_rank, -1)
    selector = (jnp.arange(27 * SLOTS, dtype=jnp.int32)[:, None] == slot_index[None, :]).astype(
        jnp.float32
    )
    outbox = jnp.dot(selector, updated.reshape(blocks, -1), precision=lax.Precision.HIGHEST)
    outbox = outbox.reshape((3, 3, 3, SLOTS) + parcels.shape[1:])
    cell_sources, widened = fold_and_widen(
        deposit, outbox, (("gx", 1, 0), ("gy", 2, 1), ("gz", 3, 2))
    )
    kappa = jnp.array(DIFFUSION, jnp.float32)[:, None, None, None]
    gas_next = gas_state + kappa * laplacian(padded) + COUPLING * cell_sources
    arrived_boxes = widened[0::2, 0::2, 0::2]
    arrived = arrived_boxes.reshape((27 * SLOTS,) + parcels.shape[1:])
    return (gas_next, kept, arrived)


def solution(mesh):
    placed = (
        P(None, "gx", "gy", "gz"),
        P(("gx", "gy", "gz"), None, None),
        P(("gx", "gy", "gz"), None),
        P(("gx", "gy", "gz"), None, None),
        P(("gx", "gy", "gz")),
        P(("gx", "gy", "gz")),
    )
    return jax.shard_map(
        local,
        mesh=mesh,
        in_specs=placed,
        out_specs=(
            P(None, "gx", "gy", "gz"),
            P(("gx", "gy", "gz"), None, None),
            P(("gx", "gy", "gz"), None, None),
        ),
        check_vma=False,
    )
```

```python
import jax
import jax.numpy as jnp
from jax import lax
from jax.sharding import PartitionSpec as P
from jax.experimental import pallas as pl
from jax.experimental.pallas import tpu as pltpu

SLOTS = 4


DIFFUSION = (0.06, 0.1, 0.12, 0.12, 0.12)
TIME_STEP = 0.5
COUPLING = 0.5
PHASE_CHANGE_COST = 0.5


def with_halo(block, sides, width):
    for axis, dim in sides:
        count = lax.axis_size(axis)
        forward = [(i, i + 1) for i in range(count - 1)]
        backward = [(target, source) for source, target in forward]
        low = lax.ppermute(
            lax.slice_in_dim(block, block.shape[dim] - width, None, axis=dim), axis, forward
        )
        high = lax.ppermute(lax.slice_in_dim(block, 0, width, axis=dim), axis, backward)
        block = jnp.concatenate([low, block, high], axis=dim)
    return block


def fold_ghosts(block, sides):
    for axis, dim in sides:
        count = lax.axis_size(axis)
        forward = [(i, i + 1) for i in range(count - 1)]
        backward = [(target, source) for source, target in forward]
        span = block.shape[dim]
        below = lax.ppermute(lax.slice_in_dim(block, span - 1, span, axis=dim), axis, forward)
        above = lax.ppermute(lax.slice_in_dim(block, 0, 1, axis=dim), axis, backward)
        inner = lax.slice_in_dim(block, 1, span - 1, axis=dim)
        low_pad = [(0, 0)] * block.ndim
        high_pad = [(0, 0)] * block.ndim
        low_pad[dim] = (0, span - 3)
        high_pad[dim] = (span - 3, 0)
        block = inner + jnp.pad(below, low_pad) + jnp.pad(above, high_pad)
    return block


def parcel_update(current_condition, local_air_sample):
    particle_weights_list = current_condition[:, 0]
    parcel_hotness_measure = current_condition[:, 1]
    particle_speed_vector = current_condition[:, 2:5]
    relax_time = 0.4 * particle_weights_list ** (2.0 / 3.0)
    keep_velocity = jnp.exp(-TIME_STEP / relax_time)
    residual_heat_content = jnp.exp(-TIME_STEP / (1.5 * relax_time))
    equilibrium_steam_load = 0.4 * jnp.exp(2.0 * (parcel_hotness_measure - 1.0))
    evaporated_share = 1.0 - jnp.exp(
        -0.3 * jax.nn.softplus(4.0 * (equilibrium_steam_load - local_air_sample[:, 0]))
    )
    evaporated = particle_weights_list * evaporated_share
    ambient_heat_content = local_air_sample[:, 1]
    gas_velocity = local_air_sample[:, 2:5]
    adjusted_heat_content = (
        ambient_heat_content
        + (parcel_hotness_measure - ambient_heat_content) * residual_heat_content
        - PHASE_CHANGE_COST * evaporated_share
    )
    velocity_new = gas_velocity + (particle_speed_vector - gas_velocity) * keep_velocity[:, None]
    enthalpy_injection = (
        0.5 * particle_weights_list * (parcel_hotness_measure - adjusted_heat_content)
    )
    push_source = particle_weights_list[:, None] * (particle_speed_vector - velocity_new)
    updated = jnp.concatenate(
        [
            (particle_weights_list - evaporated)[:, None],
            adjusted_heat_content[:, None],
            velocity_new,
        ],
        axis=1,
    )
    sources = jnp.concatenate(
        [evaporated[:, None], enthalpy_injection[:, None], push_source], axis=1
    )
    return (updated, sources)


def laplacian(padded):
    centre = padded[:, 1:-1, 1:-1, 1:-1]
    beside = padded[:, 2:, 1:-1, 1:-1] + padded[:, :-2, 1:-1, 1:-1]
    beside = beside + padded[:, 1:-1, 2:, 1:-1] + padded[:, 1:-1, :-2, 1:-1]
    beside = beside + padded[:, 1:-1, 1:-1, 2:] + padded[:, 1:-1, 1:-1, :-2]
    return beside - 6.0 * centre


PAIR_LANES = 256
DEPTH_ROWS = 136


def split_bf16(value):
    high = value.astype(jnp.bfloat16)
    low = (value - high.astype(jnp.float32)).astype(jnp.bfloat16)
    return high, low


def three_pass(a, b, dims):
    a_high, a_low = split_bf16(a)
    b_high, b_low = split_bf16(b)
    out = None
    for x, y in ((a_high, b_high), (a_high, b_low), (a_low, b_high)):
        part = lax.dot_general(x, y, (dims, ((), ())), preferred_element_type=jnp.float32)
        out = part if out is None else out + part
    return out


GROUP = 4


def coupling_kernel(
    live_ref, dest_ref, table_ref, parcel_ref, pair_ref, pair_share_ref,
    depth_ref, depth_share_ref, factor_ref, kept_ref, outbox_ref, deposit_ref,
    weight_scr, depth_scr, spread_scr, updated_scr, count_scr, table_high_ref, table_low_ref,
):
    fields = parcel_ref.shape[1]
    blocks = parcel_ref.shape[0]
    lanes = parcel_ref.shape[2]
    deposit_ref[...] = jnp.zeros(deposit_ref.shape, jnp.float32)
    table_high, table_low = split_bf16(table_ref[...])
    table_high_ref[...] = table_high
    table_low_ref[...] = table_low
    live = live_ref[0]
    pair_iota = lax.broadcasted_iota(jnp.int32, (PAIR_LANES, lanes), 0)
    depth_iota = lax.broadcasted_iota(jnp.int32, (DEPTH_ROWS, lanes), 0)

    def group(g, carry):
        for j in range(GROUP):
            b = g * GROUP + j
            pair = pair_ref[b]
            pair_share = pair_share_ref[b]
            weights = jnp.zeros((PAIR_LANES, lanes), jnp.float32)
            for c in range(4):
                weights = weights + jnp.where(pair_iota == pair[c:c + 1], pair_share[c:c + 1], 0.0)
            weight_scr[:, j * lanes:(j + 1) * lanes] = weights
            depth = depth_ref[b]
            depth_share = depth_share_ref[b]
            depth_weights = jnp.where(depth_iota == depth[0:1], depth_share[0:1], 0.0)
            depth_weights = depth_weights + jnp.where(
                depth_iota == depth[1:2], depth_share[1:2], 0.0
            )
            depth_scr[:, j * lanes:(j + 1) * lanes] = depth_weights
        weight_high, weight_low = split_bf16(weight_scr[...])
        table_high = table_high_ref[...]
        mixed = (
            jnp.dot(table_high, weight_high, preferred_element_type=jnp.float32)
            + jnp.dot(table_high, weight_low, preferred_element_type=jnp.float32)
            + jnp.dot(table_low_ref[...], weight_high, preferred_element_type=jnp.float32)
        )
        for j in range(GROUP):
            b = g * GROUP + j
            depth_weights = depth_scr[:, j * lanes:(j + 1) * lanes]
            sample = [
                jnp.sum(
                    mixed[f * DEPTH_ROWS:(f + 1) * DEPTH_ROWS, j * lanes:(j + 1) * lanes]
                    * depth_weights,
                    axis=0,
                    keepdims=True,
                )
                for f in range(fields)
            ]
            current = parcel_ref[b]
            factors = factor_ref[b]
            mass = current[0:1]
            heat = current[1:2]
            keep_velocity = factors[0:1]
            residual_heat = factors[1:2]
            equilibrium = factors[2:3]
            x = 4.0 * (equilibrium - sample[0])
            soft = jnp.maximum(x, 0.0) + jnp.log1p(jnp.exp(-jnp.abs(x)))
            share = 1.0 - jnp.exp(-0.3 * soft)
            evaporated = mass * share
            ambient = sample[1]
            adjusted = ambient + (heat - ambient) * residual_heat - PHASE_CHANGE_COST * share
            velocity = [
                sample[2 + d] + (current[2 + d:3 + d] - sample[2 + d]) * keep_velocity
                for d in range(3)
            ]
            enthalpy = 0.5 * mass * (heat - adjusted)
            push = [mass * (current[2 + d:3 + d] - velocity[d]) for d in range(3)]
            updated_scr[b] = jnp.concatenate([mass - evaporated, adjusted] + velocity, axis=0)
            alive = b < live
            sources = [jnp.where(alive, s, 0.0) for s in [evaporated, enthalpy] + push]
            spread_scr[:, j * lanes:(j + 1) * lanes] = jnp.concatenate(
                [s * depth_weights for s in sources], axis=0
            )
        spread_high, spread_low = split_bf16(spread_scr[...])
        dims = (((1,), (1,)), ((), ()))
        deposit_ref[...] += (
            lax.dot_general(spread_high, weight_high, dims, preferred_element_type=jnp.float32)
            + lax.dot_general(spread_high, weight_low, dims, preferred_element_type=jnp.float32)
            + lax.dot_general(spread_low, weight_high, dims, preferred_element_type=jnp.float32)
        )
        return carry

    lax.fori_loop(0, blocks // GROUP, group, 0)

    kept_ref[...] = jnp.zeros(kept_ref.shape, jnp.float32)
    outbox_ref[...] = jnp.zeros(outbox_ref.shape, jnp.float32)
    for d in range(27):
        count_scr[d] = 0

    def route(b, carry):
        d = jnp.minimum(jnp.maximum(dest_ref[b], 0), 26)
        alive = b < live

        @pl.when(alive & (d == 13))
        def _():
            kept_ref[b] = updated_scr[b]

        rank = count_scr[d]

        @pl.when(alive & (d != 13) & (rank < SLOTS))
        def _():
            outbox_ref[d * SLOTS + rank] = updated_scr[b]
            count_scr[d] = rank + 1

        return carry

    lax.fori_loop(0, blocks, route, 0)


def local(gas_state, parcels, parcel_cells, offsets, destination, live_blocks):
    fields, size_x, size_y, size_z = gas_state.shape
    blocks, parcel_fields, block_parcels = parcels.shape
    padded = with_halo(gas_state, (("gx", 1), ("gy", 2), ("gz", 3)), 1)
    span_x = size_x + 2
    span_y = size_y + 2
    span_z = size_z + 2
    pair_count = span_x * span_y
    plane_size = span_y * span_z
    table = jnp.transpose(padded, (0, 3, 1, 2)).reshape(fields, span_z, pair_count)
    table = jnp.pad(table, ((0, 0), (0, DEPTH_ROWS - span_z), (0, PAIR_LANES - pair_count)))
    table = table.reshape(fields * DEPTH_ROWS, PAIR_LANES)
    cell_x = parcel_cells // plane_size
    cell_y = parcel_cells // span_z % span_y
    cell_z = parcel_cells % span_z
    step_sign = jnp.where(offsets >= 0.0, 1, -1).astype(jnp.int32)
    far_share = jnp.abs(offsets)
    near_share = 1.0 - far_share
    pairs = []
    pair_shares = []
    for bit_x in range(2):
        for bit_y in range(2):
            pair_shares.append(
                (far_share[:, 0] if bit_x else near_share[:, 0])
                * (far_share[:, 1] if bit_y else near_share[:, 1])
            )
            pairs.append(
                (cell_x + bit_x * step_sign[:, 0]) * span_y + cell_y + bit_y * step_sign[:, 1]
            )
    pairs = jnp.stack(pairs, axis=1)
    pair_shares = jnp.stack(pair_shares, axis=1)
    depths = jnp.stack([cell_z, cell_z + step_sign[:, 2]], axis=1)
    depth_shares = jnp.stack([near_share[:, 2], far_share[:, 2]], axis=1)
    relax_time = 0.4 * parcels[:, 0] ** (2.0 / 3.0)
    factors = jnp.stack(
        [
            jnp.exp(-TIME_STEP / relax_time),
            jnp.exp(-TIME_STEP / (1.5 * relax_time)),
            0.4 * jnp.exp(2.0 * (parcels[:, 1] - 1.0)),
        ],
        axis=1,
    )
    vmem = pl.BlockSpec(memory_space=pltpu.VMEM)
    smem = pl.BlockSpec(memory_space=pltpu.SMEM)
    lanes = GROUP * block_parcels
    kept, outbox, deposit_rows = pl.pallas_call(
        coupling_kernel,
        out_shape=(
            jax.ShapeDtypeStruct(parcels.shape, jnp.float32),
            jax.ShapeDtypeStruct((27 * SLOTS,) + parcels.shape[1:], jnp.float32),
            jax.ShapeDtypeStruct((fields * DEPTH_ROWS, PAIR_LANES), jnp.float32),
        ),
        in_specs=[smem, smem] + [vmem] * 7,
        out_specs=(vmem, vmem, vmem),
        scratch_shapes=[
            pltpu.VMEM((PAIR_LANES, lanes), jnp.float32),
            pltpu.VMEM((DEPTH_ROWS, lanes), jnp.float32),
            pltpu.VMEM((fields * DEPTH_ROWS, lanes), jnp.float32),
            pltpu.VMEM(parcels.shape, jnp.float32),
            pltpu.SMEM((32,), jnp.int32),
            pltpu.VMEM(table.shape, jnp.bfloat16),
            pltpu.VMEM(table.shape, jnp.bfloat16),
        ],
    )(
        live_blocks, destination, table, parcels, pairs, pair_shares, depths,
        depth_shares, factors,
    )
    deposit = deposit_rows.reshape(fields, DEPTH_ROWS, PAIR_LANES)[:, :span_z, :pair_count]
    deposit = jnp.transpose(deposit.reshape(fields, span_z, span_x, span_y), (0, 2, 3, 1))
    cell_sources = fold_ghosts(deposit, (("gx", 1), ("gy", 2), ("gz", 3)))
    kappa = jnp.array(DIFFUSION, jnp.float32)[:, None, None, None]
    gas_next = gas_state + kappa * laplacian(padded) + COUPLING * cell_sources
    outbox = outbox.reshape((3, 3, 3, SLOTS) + parcels.shape[1:])
    widened = with_halo(outbox, (("gx", 0), ("gy", 1), ("gz", 2)), 1)
    arrived_boxes = widened[0::2, 0::2, 0::2]
    arrived = arrived_boxes.reshape((27 * SLOTS,) + parcels.shape[1:])
    return (gas_next, kept, arrived)


def solution(mesh):
    placed = (
        P(None, "gx", "gy", "gz"),
        P(("gx", "gy", "gz"), None, None),
        P(("gx", "gy", "gz"), None),
        P(("gx", "gy", "gz"), None, None),
        P(("gx", "gy", "gz")),
        P(("gx", "gy", "gz")),
    )
    return jax.shard_map(
        local,
        mesh=mesh,
        in_specs=placed,
        out_specs=(
            P(None, "gx", "gy", "gz"),
            P(("gx", "gy", "gz"), None, None),
            P(("gx", "gy", "gz"), None, None),
        ),
        check_vma=False,
    )
```

```python
import functools

import jax
import jax.numpy as jnp
from jax import lax
from jax.sharding import PartitionSpec as P
from jax.experimental import pallas as pl
from jax.experimental.pallas import tpu as pltpu

SLOTS = 4


DIFFUSION = (0.06, 0.1, 0.12, 0.12, 0.12)
TIME_STEP = 0.5
COUPLING = 0.5
PHASE_CHANGE_COST = 0.5


def with_halo(block, sides, width):
    for axis, dim in sides:
        count = lax.axis_size(axis)
        forward = [(i, i + 1) for i in range(count - 1)]
        backward = [(target, source) for source, target in forward]
        low = lax.ppermute(
            lax.slice_in_dim(block, block.shape[dim] - width, None, axis=dim), axis, forward
        )
        high = lax.ppermute(lax.slice_in_dim(block, 0, width, axis=dim), axis, backward)
        block = jnp.concatenate([low, block, high], axis=dim)
    return block


def fold_ghosts(block, sides):
    for axis, dim in sides:
        count = lax.axis_size(axis)
        forward = [(i, i + 1) for i in range(count - 1)]
        backward = [(target, source) for source, target in forward]
        span = block.shape[dim]
        below = lax.ppermute(lax.slice_in_dim(block, span - 1, span, axis=dim), axis, forward)
        above = lax.ppermute(lax.slice_in_dim(block, 0, 1, axis=dim), axis, backward)
        inner = lax.slice_in_dim(block, 1, span - 1, axis=dim)
        low_pad = [(0, 0)] * block.ndim
        high_pad = [(0, 0)] * block.ndim
        low_pad[dim] = (0, span - 3)
        high_pad[dim] = (span - 3, 0)
        block = inner + jnp.pad(below, low_pad) + jnp.pad(above, high_pad)
    return block


def parcel_update(current_condition, local_air_sample):
    particle_weights_list = current_condition[:, 0]
    parcel_hotness_measure = current_condition[:, 1]
    particle_speed_vector = current_condition[:, 2:5]
    relax_time = 0.4 * particle_weights_list ** (2.0 / 3.0)
    keep_velocity = jnp.exp(-TIME_STEP / relax_time)
    residual_heat_content = jnp.exp(-TIME_STEP / (1.5 * relax_time))
    equilibrium_steam_load = 0.4 * jnp.exp(2.0 * (parcel_hotness_measure - 1.0))
    evaporated_share = 1.0 - jnp.exp(
        -0.3 * jax.nn.softplus(4.0 * (equilibrium_steam_load - local_air_sample[:, 0]))
    )
    evaporated = particle_weights_list * evaporated_share
    ambient_heat_content = local_air_sample[:, 1]
    gas_velocity = local_air_sample[:, 2:5]
    adjusted_heat_content = (
        ambient_heat_content
        + (parcel_hotness_measure - ambient_heat_content) * residual_heat_content
        - PHASE_CHANGE_COST * evaporated_share
    )
    velocity_new = gas_velocity + (particle_speed_vector - gas_velocity) * keep_velocity[:, None]
    enthalpy_injection = (
        0.5 * particle_weights_list * (parcel_hotness_measure - adjusted_heat_content)
    )
    push_source = particle_weights_list[:, None] * (particle_speed_vector - velocity_new)
    updated = jnp.concatenate(
        [
            (particle_weights_list - evaporated)[:, None],
            adjusted_heat_content[:, None],
            velocity_new,
        ],
        axis=1,
    )
    sources = jnp.concatenate(
        [evaporated[:, None], enthalpy_injection[:, None], push_source], axis=1
    )
    return (updated, sources)


def laplacian(padded):
    centre = padded[:, 1:-1, 1:-1, 1:-1]
    beside = padded[:, 2:, 1:-1, 1:-1] + padded[:, :-2, 1:-1, 1:-1]
    beside = beside + padded[:, 1:-1, 2:, 1:-1] + padded[:, 1:-1, :-2, 1:-1]
    beside = beside + padded[:, 1:-1, 1:-1, 2:] + padded[:, 1:-1, 1:-1, :-2]
    return beside - 6.0 * centre


PAIR_LANES = 256
DEPTH_ROWS = 136


def split_bf16(value):
    high = value.astype(jnp.bfloat16)
    low = (value - high.astype(jnp.float32)).astype(jnp.bfloat16)
    return high, low


def three_pass(a, b, dims):
    a_high, a_low = split_bf16(a)
    b_high, b_low = split_bf16(b)
    out = None
    for x, y in ((a_high, b_high), (a_high, b_low), (a_low, b_high)):
        part = lax.dot_general(x, y, (dims, ((), ())), preferred_element_type=jnp.float32)
        out = part if out is None else out + part
    return out


GROUP = 4


def coupling_kernel(
    live_ref, dest_ref, table_ref, parcel_ref, cell_ref, offset_ref, factor_ref,
    kept_ref, outbox_ref, deposit_ref,
    weight_scr, depth_scr, spread_scr, updated_scr, count_scr, table_high_ref, table_low_ref,
    *, span_y, span_z,
):
    fields = parcel_ref.shape[0]
    blocks = parcel_ref.shape[1]
    lanes = parcel_ref.shape[2]
    plane_size = span_y * span_z
    deposit_ref[...] = jnp.zeros(deposit_ref.shape, jnp.float32)
    table_high, table_low = split_bf16(table_ref[...])
    table_high_ref[...] = table_high
    table_low_ref[...] = table_low
    live = live_ref[0]
    pair_iota = lax.broadcasted_iota(jnp.int32, (PAIR_LANES, lanes), 0)
    depth_iota = lax.broadcasted_iota(jnp.int32, (DEPTH_ROWS, lanes), 0)

    def group(g, carry):
        first = pl.multiple_of(g * GROUP, GROUP)
        cells = cell_ref[pl.ds(first, GROUP), :]
        offsets = offset_ref[:, pl.ds(first, GROUP), :]
        parcels = parcel_ref[:, pl.ds(first, GROUP), :]
        factors = factor_ref[:, pl.ds(first, GROUP), :]
        flat = cells.astype(jnp.float32) + 0.5
        cell_x = jnp.floor(flat * (1.0 / plane_size))
        rest = flat - cell_x * plane_size
        cell_y = jnp.floor(rest * (1.0 / span_z))
        cell_z = (rest - cell_y * span_z).astype(jnp.int32)
        cell_x = cell_x.astype(jnp.int32)
        cell_y = cell_y.astype(jnp.int32)
        step_sign = jnp.where(offsets >= 0.0, 1, -1).astype(jnp.int32)
        far_share = jnp.abs(offsets)
        near_share = 1.0 - far_share
        for j in range(GROUP):
            weights = jnp.zeros((PAIR_LANES, lanes), jnp.float32)
            for bit_x in range(2):
                for bit_y in range(2):
                    share = (far_share[0, j:j + 1] if bit_x else near_share[0, j:j + 1]) * (
                        far_share[1, j:j + 1] if bit_y else near_share[1, j:j + 1]
                    )
                    target = (
                        (cell_x[j:j + 1] + bit_x * step_sign[0, j:j + 1]) * span_y
                        + cell_y[j:j + 1]
                        + bit_y * step_sign[1, j:j + 1]
                    )
                    weights = weights + jnp.where(pair_iota == target, share, 0.0)
            weight_scr[:, j * lanes:(j + 1) * lanes] = weights
            depth_weights = jnp.where(
                depth_iota == cell_z[j:j + 1], near_share[2, j:j + 1], 0.0
            ) + jnp.where(
                depth_iota == cell_z[j:j + 1] + step_sign[2, j:j + 1], far_share[2, j:j + 1], 0.0
            )
            depth_scr[:, j * lanes:(j + 1) * lanes] = depth_weights
        weight_high, weight_low = split_bf16(weight_scr[...])
        table_high = table_high_ref[...]
        mixed = (
            jnp.dot(table_high, weight_high, preferred_element_type=jnp.float32)
            + jnp.dot(table_high, weight_low, preferred_element_type=jnp.float32)
            + jnp.dot(table_low_ref[...], weight_high, preferred_element_type=jnp.float32)
        )
        for j in range(GROUP):
            b = first + j
            depth_weights = depth_scr[:, j * lanes:(j + 1) * lanes]
            sample = [
                jnp.sum(
                    mixed[f * DEPTH_ROWS:(f + 1) * DEPTH_ROWS, j * lanes:(j + 1) * lanes]
                    * depth_weights,
                    axis=0,
                    keepdims=True,
                )
                for f in range(fields)
            ]
            mass = parcels[0, j:j + 1]
            heat = parcels[1, j:j + 1]
            keep_velocity = factors[0, j:j + 1]
            residual_heat = factors[1, j:j + 1]
            equilibrium = factors[2, j:j + 1]
            x = 4.0 * (equilibrium - sample[0])
            soft = jnp.maximum(x, 0.0) + jnp.log1p(jnp.exp(-jnp.abs(x)))
            share = 1.0 - jnp.exp(-0.3 * soft)
            evaporated = mass * share
            ambient = sample[1]
            adjusted = ambient + (heat - ambient) * residual_heat - PHASE_CHANGE_COST * share
            velocity = [
                sample[2 + d] + (parcels[2 + d, j:j + 1] - sample[2 + d]) * keep_velocity
                for d in range(3)
            ]
            enthalpy = 0.5 * mass * (heat - adjusted)
            push = [mass * (parcels[2 + d, j:j + 1] - velocity[d]) for d in range(3)]
            rows = [mass - evaporated, adjusted] + velocity
            for f in range(fields):
                updated_scr[f, pl.ds(b, 1), :] = rows[f]
            alive = b < live
            sources = [jnp.where(alive, s, 0.0) for s in [evaporated, enthalpy] + push]
            spread_scr[:, j * lanes:(j + 1) * lanes] = jnp.concatenate(
                [s * depth_weights for s in sources], axis=0
            )
        spread_high, spread_low = split_bf16(spread_scr[...])
        dims = (((1,), (1,)), ((), ()))
        deposit_ref[...] += (
            lax.dot_general(spread_high, weight_high, dims, preferred_element_type=jnp.float32)
            + lax.dot_general(spread_high, weight_low, dims, preferred_element_type=jnp.float32)
            + lax.dot_general(spread_low, weight_high, dims, preferred_element_type=jnp.float32)
        )
        return carry

    lax.fori_loop(0, blocks // GROUP, group, 0)

    kept_ref[...] = jnp.zeros(kept_ref.shape, jnp.float32)
    outbox_ref[...] = jnp.zeros(outbox_ref.shape, jnp.float32)
    for d in range(27):
        count_scr[d] = 0

    def route(b, carry):
        d = jnp.minimum(jnp.maximum(dest_ref[b], 0), 26)
        alive = b < live

        @pl.when(alive & (d == 13))
        def _():
            kept_ref[:, pl.ds(b, 1), :] = updated_scr[:, pl.ds(b, 1), :]

        rank = count_scr[d]

        @pl.when(alive & (d != 13) & (rank < SLOTS))
        def _():
            outbox_ref[:, pl.ds(d * SLOTS + rank, 1), :] = updated_scr[:, pl.ds(b, 1), :]
            count_scr[d] = rank + 1

        return carry

    lax.fori_loop(0, blocks, route, 0)


def local(gas_state, parcels, parcel_cells, offsets, destination, live_blocks):
    fields, size_x, size_y, size_z = gas_state.shape
    blocks, parcel_fields, block_parcels = parcels.shape
    padded = with_halo(gas_state, (("gx", 1), ("gy", 2), ("gz", 3)), 1)
    span_x = size_x + 2
    span_y = size_y + 2
    span_z = size_z + 2
    pair_count = span_x * span_y
    plane_size = span_y * span_z
    table = jnp.transpose(padded, (0, 3, 1, 2)).reshape(fields, span_z, pair_count)
    table = jnp.pad(table, ((0, 0), (0, DEPTH_ROWS - span_z), (0, PAIR_LANES - pair_count)))
    table = table.reshape(fields * DEPTH_ROWS, PAIR_LANES)
    parcel_rows = jnp.transpose(parcels, (1, 0, 2))
    offset_rows = jnp.transpose(offsets, (1, 0, 2))
    relax_time = 0.4 * parcel_rows[0] ** (2.0 / 3.0)
    factors = jnp.stack(
        [
            jnp.exp(-TIME_STEP / relax_time),
            jnp.exp(-TIME_STEP / (1.5 * relax_time)),
            0.4 * jnp.exp(2.0 * (parcel_rows[1] - 1.0)),
        ],
        axis=0,
    )
    vmem = pl.BlockSpec(memory_space=pltpu.VMEM)
    smem = pl.BlockSpec(memory_space=pltpu.SMEM)
    lanes = GROUP * block_parcels
    kept_rows, outbox_rows, deposit_rows = pl.pallas_call(
        functools.partial(coupling_kernel, span_y=span_y, span_z=span_z),
        out_shape=(
            jax.ShapeDtypeStruct(parcel_rows.shape, jnp.float32),
            jax.ShapeDtypeStruct((parcel_fields, 27 * SLOTS, block_parcels), jnp.float32),
            jax.ShapeDtypeStruct((fields * DEPTH_ROWS, PAIR_LANES), jnp.float32),
        ),
        in_specs=[smem, smem] + [vmem] * 5,
        out_specs=(vmem, vmem, vmem),
        scratch_shapes=[
            pltpu.VMEM((PAIR_LANES, lanes), jnp.float32),
            pltpu.VMEM((DEPTH_ROWS, lanes), jnp.float32),
            pltpu.VMEM((fields * DEPTH_ROWS, lanes), jnp.float32),
            pltpu.VMEM(parcel_rows.shape, jnp.float32),
            pltpu.SMEM((32,), jnp.int32),
            pltpu.VMEM(table.shape, jnp.bfloat16),
            pltpu.VMEM(table.shape, jnp.bfloat16),
        ],
    )(live_blocks, destination, table, parcel_rows, parcel_cells, offset_rows, factors)
    kept = jnp.transpose(kept_rows, (1, 0, 2))
    deposit = deposit_rows.reshape(fields, DEPTH_ROWS, PAIR_LANES)[:, :span_z, :pair_count]
    deposit = jnp.transpose(deposit.reshape(fields, span_z, span_x, span_y), (0, 2, 3, 1))
    cell_sources = fold_ghosts(deposit, (("gx", 1), ("gy", 2), ("gz", 3)))
    kappa = jnp.array(DIFFUSION, jnp.float32)[:, None, None, None]
    gas_next = gas_state + kappa * laplacian(padded) + COUPLING * cell_sources
    outbox = outbox_rows.reshape((parcel_fields, 3, 3, 3, SLOTS, block_parcels))
    widened = with_halo(outbox, (("gx", 1), ("gy", 2), ("gz", 3)), 1)
    arrived_boxes = widened[:, 0::2, 0::2, 0::2]
    arrived = jnp.transpose(
        arrived_boxes.reshape((parcel_fields, 27 * SLOTS, block_parcels)), (1, 0, 2)
    )
    return (gas_next, kept, arrived)


def solution(mesh):
    placed = (
        P(None, "gx", "gy", "gz"),
        P(("gx", "gy", "gz"), None, None),
        P(("gx", "gy", "gz"), None),
        P(("gx", "gy", "gz"), None, None),
        P(("gx", "gy", "gz")),
        P(("gx", "gy", "gz")),
    )
    return jax.shard_map(
        local,
        mesh=mesh,
        in_specs=placed,
        out_specs=(
            P(None, "gx", "gy", "gz"),
            P(("gx", "gy", "gz"), None, None),
            P(("gx", "gy", "gz"), None, None),
        ),
        check_vma=False,
    )
```

```python
import functools

import jax
import jax.numpy as jnp
from jax import lax
from jax.sharding import PartitionSpec as P
from jax.experimental import pallas as pl
from jax.experimental.pallas import tpu as pltpu

SLOTS = 4


DIFFUSION = (0.06, 0.1, 0.12, 0.12, 0.12)
TIME_STEP = 0.5
COUPLING = 0.5
PHASE_CHANGE_COST = 0.5


def with_halo(block, sides, width):
    for axis, dim in sides:
        count = lax.axis_size(axis)
        forward = [(i, i + 1) for i in range(count - 1)]
        backward = [(target, source) for source, target in forward]
        low = lax.ppermute(
            lax.slice_in_dim(block, block.shape[dim] - width, None, axis=dim), axis, forward
        )
        high = lax.ppermute(lax.slice_in_dim(block, 0, width, axis=dim), axis, backward)
        block = jnp.concatenate([low, block, high], axis=dim)
    return block


def fold_ghosts(block, sides):
    for axis, dim in sides:
        count = lax.axis_size(axis)
        forward = [(i, i + 1) for i in range(count - 1)]
        backward = [(target, source) for source, target in forward]
        span = block.shape[dim]
        below = lax.ppermute(lax.slice_in_dim(block, span - 1, span, axis=dim), axis, forward)
        above = lax.ppermute(lax.slice_in_dim(block, 0, 1, axis=dim), axis, backward)
        inner = lax.slice_in_dim(block, 1, span - 1, axis=dim)
        low_pad = [(0, 0)] * block.ndim
        high_pad = [(0, 0)] * block.ndim
        low_pad[dim] = (0, span - 3)
        high_pad[dim] = (span - 3, 0)
        block = inner + jnp.pad(below, low_pad) + jnp.pad(above, high_pad)
    return block


def parcel_update(current_condition, local_air_sample):
    particle_weights_list = current_condition[:, 0]
    parcel_hotness_measure = current_condition[:, 1]
    particle_speed_vector = current_condition[:, 2:5]
    relax_time = 0.4 * particle_weights_list ** (2.0 / 3.0)
    keep_velocity = jnp.exp(-TIME_STEP / relax_time)
    residual_heat_content = jnp.exp(-TIME_STEP / (1.5 * relax_time))
    equilibrium_steam_load = 0.4 * jnp.exp(2.0 * (parcel_hotness_measure - 1.0))
    evaporated_share = 1.0 - jnp.exp(
        -0.3 * jax.nn.softplus(4.0 * (equilibrium_steam_load - local_air_sample[:, 0]))
    )
    evaporated = particle_weights_list * evaporated_share
    ambient_heat_content = local_air_sample[:, 1]
    gas_velocity = local_air_sample[:, 2:5]
    adjusted_heat_content = (
        ambient_heat_content
        + (parcel_hotness_measure - ambient_heat_content) * residual_heat_content
        - PHASE_CHANGE_COST * evaporated_share
    )
    velocity_new = gas_velocity + (particle_speed_vector - gas_velocity) * keep_velocity[:, None]
    enthalpy_injection = (
        0.5 * particle_weights_list * (parcel_hotness_measure - adjusted_heat_content)
    )
    push_source = particle_weights_list[:, None] * (particle_speed_vector - velocity_new)
    updated = jnp.concatenate(
        [
            (particle_weights_list - evaporated)[:, None],
            adjusted_heat_content[:, None],
            velocity_new,
        ],
        axis=1,
    )
    sources = jnp.concatenate(
        [evaporated[:, None], enthalpy_injection[:, None], push_source], axis=1
    )
    return (updated, sources)


def laplacian(padded):
    centre = padded[:, 1:-1, 1:-1, 1:-1]
    beside = padded[:, 2:, 1:-1, 1:-1] + padded[:, :-2, 1:-1, 1:-1]
    beside = beside + padded[:, 1:-1, 2:, 1:-1] + padded[:, 1:-1, :-2, 1:-1]
    beside = beside + padded[:, 1:-1, 1:-1, 2:] + padded[:, 1:-1, 1:-1, :-2]
    return beside - 6.0 * centre


PAIR_LANES = 256
DEPTH_ROWS = 136


def split_bf16(value):
    high = value.astype(jnp.bfloat16)
    low = (value - high.astype(jnp.float32)).astype(jnp.bfloat16)
    return high, low


def three_pass(a, b, dims):
    a_high, a_low = split_bf16(a)
    b_high, b_low = split_bf16(b)
    out = None
    for x, y in ((a_high, b_high), (a_high, b_low), (a_low, b_high)):
        part = lax.dot_general(x, y, (dims, ((), ())), preferred_element_type=jnp.float32)
        out = part if out is None else out + part
    return out


GROUP = 8


def coupling_kernel(
    live_ref, dest_ref, table_ref, parcel_ref, cell_ref, offset_ref, factor_ref,
    kept_ref, outbox_ref, deposit_ref,
    weight_scr, depth_scr, spread_scr, updated_scr, count_scr, table_high_ref, table_low_ref,
    *, span_y, span_z,
):
    fields = parcel_ref.shape[0]
    blocks = parcel_ref.shape[1]
    lanes = parcel_ref.shape[2]
    plane_size = span_y * span_z
    deposit_ref[...] = jnp.zeros(deposit_ref.shape, jnp.float32)
    table_high, table_low = split_bf16(table_ref[...])
    table_high_ref[...] = table_high
    table_low_ref[...] = table_low
    live = live_ref[0]
    pair_iota = lax.broadcasted_iota(jnp.int32, (PAIR_LANES, lanes), 0)
    depth_iota = lax.broadcasted_iota(jnp.int32, (DEPTH_ROWS, lanes), 0)

    def group(g, carry):
        first = pl.multiple_of(g * GROUP, GROUP)
        cells = cell_ref[pl.ds(first, GROUP), :]
        offsets = offset_ref[:, pl.ds(first, GROUP), :]
        parcels = parcel_ref[:, pl.ds(first, GROUP), :]
        factors = factor_ref[:, pl.ds(first, GROUP), :]
        flat = cells.astype(jnp.float32) + 0.5
        cell_x = jnp.floor(flat * (1.0 / plane_size))
        rest = flat - cell_x * plane_size
        cell_y = jnp.floor(rest * (1.0 / span_z))
        cell_z = (rest - cell_y * span_z).astype(jnp.int32)
        cell_x = cell_x.astype(jnp.int32)
        cell_y = cell_y.astype(jnp.int32)
        step_sign = jnp.where(offsets >= 0.0, 1, -1).astype(jnp.int32)
        far_share = jnp.abs(offsets)
        near_share = 1.0 - far_share
        for j in range(GROUP):
            weights = jnp.zeros((PAIR_LANES, lanes), jnp.float32)
            for bit_x in range(2):
                for bit_y in range(2):
                    share = (far_share[0, j:j + 1] if bit_x else near_share[0, j:j + 1]) * (
                        far_share[1, j:j + 1] if bit_y else near_share[1, j:j + 1]
                    )
                    target = (
                        (cell_x[j:j + 1] + bit_x * step_sign[0, j:j + 1]) * span_y
                        + cell_y[j:j + 1]
                        + bit_y * step_sign[1, j:j + 1]
                    )
                    weights = weights + jnp.where(pair_iota == target, share, 0.0)
            weight_scr[:, j * lanes:(j + 1) * lanes] = weights
            depth_weights = jnp.where(
                depth_iota == cell_z[j:j + 1], near_share[2, j:j + 1], 0.0
            ) + jnp.where(
                depth_iota == cell_z[j:j + 1] + step_sign[2, j:j + 1], far_share[2, j:j + 1], 0.0
            )
            depth_scr[:, j * lanes:(j + 1) * lanes] = depth_weights
        weight_high, weight_low = split_bf16(weight_scr[...])
        table_high = table_high_ref[...]
        mixed = (
            jnp.dot(table_high, weight_high, preferred_element_type=jnp.float32)
            + jnp.dot(table_high, weight_low, preferred_element_type=jnp.float32)
            + jnp.dot(table_low_ref[...], weight_high, preferred_element_type=jnp.float32)
        )
        for j in range(GROUP):
            b = first + j
            depth_weights = depth_scr[:, j * lanes:(j + 1) * lanes]
            sample = [
                jnp.sum(
                    mixed[f * DEPTH_ROWS:(f + 1) * DEPTH_ROWS, j * lanes:(j + 1) * lanes]
                    * depth_weights,
                    axis=0,
                    keepdims=True,
                )
                for f in range(fields)
            ]
            mass = parcels[0, j:j + 1]
            heat = parcels[1, j:j + 1]
            keep_velocity = factors[0, j:j + 1]
            residual_heat = factors[1, j:j + 1]
            equilibrium = factors[2, j:j + 1]
            x = 4.0 * (equilibrium - sample[0])
            soft = jnp.maximum(x, 0.0) + jnp.log1p(jnp.exp(-jnp.abs(x)))
            share = 1.0 - jnp.exp(-0.3 * soft)
            evaporated = mass * share
            ambient = sample[1]
            adjusted = ambient + (heat - ambient) * residual_heat - PHASE_CHANGE_COST * share
            velocity = [
                sample[2 + d] + (parcels[2 + d, j:j + 1] - sample[2 + d]) * keep_velocity
                for d in range(3)
            ]
            enthalpy = 0.5 * mass * (heat - adjusted)
            push = [mass * (parcels[2 + d, j:j + 1] - velocity[d]) for d in range(3)]
            rows = [mass - evaporated, adjusted] + velocity
            for f in range(fields):
                updated_scr[f, pl.ds(b, 1), :] = rows[f]
            alive = b < live
            sources = [jnp.where(alive, s, 0.0) for s in [evaporated, enthalpy] + push]
            spread_scr[:, j * lanes:(j + 1) * lanes] = jnp.concatenate(
                [s * depth_weights for s in sources], axis=0
            )
        spread_high, spread_low = split_bf16(spread_scr[...])
        dims = (((1,), (1,)), ((), ()))
        deposit_ref[...] += (
            lax.dot_general(spread_high, weight_high, dims, preferred_element_type=jnp.float32)
            + lax.dot_general(spread_high, weight_low, dims, preferred_element_type=jnp.float32)
            + lax.dot_general(spread_low, weight_high, dims, preferred_element_type=jnp.float32)
        )
        return carry

    lax.fori_loop(0, blocks // GROUP, group, 0)

    kept_ref[...] = jnp.zeros(kept_ref.shape, jnp.float32)
    outbox_ref[...] = jnp.zeros(outbox_ref.shape, jnp.float32)
    for d in range(27):
        count_scr[d] = 0

    def route(b, carry):
        d = jnp.minimum(jnp.maximum(dest_ref[b], 0), 26)
        alive = b < live

        @pl.when(alive & (d == 13))
        def _():
            kept_ref[:, pl.ds(b, 1), :] = updated_scr[:, pl.ds(b, 1), :]

        rank = count_scr[d]

        @pl.when(alive & (d != 13) & (rank < SLOTS))
        def _():
            outbox_ref[:, pl.ds(d * SLOTS + rank, 1), :] = updated_scr[:, pl.ds(b, 1), :]
            count_scr[d] = rank + 1

        return carry

    lax.fori_loop(0, blocks, route, 0)


def local(gas_state, parcels, parcel_cells, offsets, destination, live_blocks):
    fields, size_x, size_y, size_z = gas_state.shape
    blocks, parcel_fields, block_parcels = parcels.shape
    padded = with_halo(gas_state, (("gx", 1), ("gy", 2), ("gz", 3)), 1)
    span_x = size_x + 2
    span_y = size_y + 2
    span_z = size_z + 2
    pair_count = span_x * span_y
    plane_size = span_y * span_z
    table = jnp.transpose(padded, (0, 3, 1, 2)).reshape(fields, span_z, pair_count)
    table = jnp.pad(table, ((0, 0), (0, DEPTH_ROWS - span_z), (0, PAIR_LANES - pair_count)))
    table = table.reshape(fields * DEPTH_ROWS, PAIR_LANES)
    parcel_rows = jnp.transpose(parcels, (1, 0, 2))
    offset_rows = jnp.transpose(offsets, (1, 0, 2))
    relax_time = 0.4 * parcel_rows[0] ** (2.0 / 3.0)
    factors = jnp.stack(
        [
            jnp.exp(-TIME_STEP / relax_time),
            jnp.exp(-TIME_STEP / (1.5 * relax_time)),
            0.4 * jnp.exp(2.0 * (parcel_rows[1] - 1.0)),
        ],
        axis=0,
    )
    vmem = pl.BlockSpec(memory_space=pltpu.VMEM)
    smem = pl.BlockSpec(memory_space=pltpu.SMEM)
    lanes = GROUP * block_parcels
    kept_rows, outbox_rows, deposit_rows = pl.pallas_call(
        functools.partial(coupling_kernel, span_y=span_y, span_z=span_z),
        out_shape=(
            jax.ShapeDtypeStruct(parcel_rows.shape, jnp.float32),
            jax.ShapeDtypeStruct((parcel_fields, 27 * SLOTS, block_parcels), jnp.float32),
            jax.ShapeDtypeStruct((fields * DEPTH_ROWS, PAIR_LANES), jnp.float32),
        ),
        in_specs=[smem, smem] + [vmem] * 5,
        out_specs=(vmem, vmem, vmem),
        scratch_shapes=[
            pltpu.VMEM((PAIR_LANES, lanes), jnp.float32),
            pltpu.VMEM((DEPTH_ROWS, lanes), jnp.float32),
            pltpu.VMEM((fields * DEPTH_ROWS, lanes), jnp.float32),
            pltpu.VMEM(parcel_rows.shape, jnp.float32),
            pltpu.SMEM((32,), jnp.int32),
            pltpu.VMEM(table.shape, jnp.bfloat16),
            pltpu.VMEM(table.shape, jnp.bfloat16),
        ],
    )(live_blocks, destination, table, parcel_rows, parcel_cells, offset_rows, factors)
    kept = jnp.transpose(kept_rows, (1, 0, 2))
    deposit = deposit_rows.reshape(fields, DEPTH_ROWS, PAIR_LANES)[:, :span_z, :pair_count]
    deposit = jnp.transpose(deposit.reshape(fields, span_z, span_x, span_y), (0, 2, 3, 1))
    cell_sources = fold_ghosts(deposit, (("gx", 1), ("gy", 2), ("gz", 3)))
    kappa = jnp.array(DIFFUSION, jnp.float32)[:, None, None, None]
    gas_next = gas_state + kappa * laplacian(padded) + COUPLING * cell_sources
    outbox = outbox_rows.reshape((parcel_fields, 3, 3, 3, SLOTS, block_parcels))
    widened = with_halo(outbox, (("gx", 1), ("gy", 2), ("gz", 3)), 1)
    arrived_boxes = widened[:, 0::2, 0::2, 0::2]
    arrived = jnp.transpose(
        arrived_boxes.reshape((parcel_fields, 27 * SLOTS, block_parcels)), (1, 0, 2)
    )
    return (gas_next, kept, arrived)


def solution(mesh):
    placed = (
        P(None, "gx", "gy", "gz"),
        P(("gx", "gy", "gz"), None, None),
        P(("gx", "gy", "gz"), None),
        P(("gx", "gy", "gz"), None, None),
        P(("gx", "gy", "gz")),
        P(("gx", "gy", "gz")),
    )
    return jax.shard_map(
        local,
        mesh=mesh,
        in_specs=placed,
        out_specs=(
            P(None, "gx", "gy", "gz"),
            P(("gx", "gy", "gz"), None, None),
            P(("gx", "gy", "gz"), None, None),
        ),
        check_vma=False,
    )
```

```python
import functools

import jax
import jax.numpy as jnp
from jax import lax
from jax.sharding import PartitionSpec as P
from jax.experimental import pallas as pl
from jax.experimental.pallas import tpu as pltpu

SLOTS = 4


DIFFUSION = (0.06, 0.1, 0.12, 0.12, 0.12)
TIME_STEP = 0.5
COUPLING = 0.5
PHASE_CHANGE_COST = 0.5


def with_halo(block, sides, width):
    for axis, dim in sides:
        count = lax.axis_size(axis)
        forward = [(i, i + 1) for i in range(count - 1)]
        backward = [(target, source) for source, target in forward]
        low = lax.ppermute(
            lax.slice_in_dim(block, block.shape[dim] - width, None, axis=dim), axis, forward
        )
        high = lax.ppermute(lax.slice_in_dim(block, 0, width, axis=dim), axis, backward)
        block = jnp.concatenate([low, block, high], axis=dim)
    return block


def fold_ghosts(block, sides):
    for axis, dim in sides:
        count = lax.axis_size(axis)
        forward = [(i, i + 1) for i in range(count - 1)]
        backward = [(target, source) for source, target in forward]
        span = block.shape[dim]
        below = lax.ppermute(lax.slice_in_dim(block, span - 1, span, axis=dim), axis, forward)
        above = lax.ppermute(lax.slice_in_dim(block, 0, 1, axis=dim), axis, backward)
        inner = lax.slice_in_dim(block, 1, span - 1, axis=dim)
        low_pad = [(0, 0)] * block.ndim
        high_pad = [(0, 0)] * block.ndim
        low_pad[dim] = (0, span - 3)
        high_pad[dim] = (span - 3, 0)
        block = inner + jnp.pad(below, low_pad) + jnp.pad(above, high_pad)
    return block


def exchange_rows(deposit, boxes, axis, dim, rows):
    count = lax.axis_size(axis)
    forward = [(i, i + 1) for i in range(count - 1)]
    backward = [(target, source) for source, target in forward]
    span = deposit.shape[dim]
    width = boxes.shape[-1]
    last = lax.index_in_dim(deposit, span - 1, dim, keepdims=False).reshape(-1, width)
    first = lax.index_in_dim(deposit, 0, dim, keepdims=False).reshape(-1, width)
    box_last = lax.index_in_dim(boxes, boxes.shape[dim] - 1, dim, keepdims=False)
    box_first = lax.index_in_dim(boxes, 0, dim, keepdims=False)
    up = jnp.concatenate([last, box_last.reshape(-1, width)], axis=0)
    down = jnp.concatenate([first, box_first.reshape(-1, width)], axis=0)
    below = lax.ppermute(up, axis, forward)
    above = lax.ppermute(down, axis, backward)
    layer = lax.index_in_dim(deposit, 0, dim, keepdims=True).shape
    face = lax.index_in_dim(boxes, 0, dim, keepdims=True).shape
    inner = lax.slice_in_dim(deposit, 1, span - 1, axis=dim)
    low_pad = [(0, 0)] * deposit.ndim
    high_pad = [(0, 0)] * deposit.ndim
    low_pad[dim] = (0, span - 3)
    high_pad[dim] = (span - 3, 0)
    deposit = (
        inner
        + jnp.pad(below[:rows].reshape(layer), low_pad)
        + jnp.pad(above[:rows].reshape(layer), high_pad)
    )
    boxes = jnp.concatenate(
        [below[rows:].reshape(face), boxes, above[rows:].reshape(face)], axis=dim
    )
    return deposit, boxes


def parcel_update(current_condition, local_air_sample):
    particle_weights_list = current_condition[:, 0]
    parcel_hotness_measure = current_condition[:, 1]
    particle_speed_vector = current_condition[:, 2:5]
    relax_time = 0.4 * particle_weights_list ** (2.0 / 3.0)
    keep_velocity = jnp.exp(-TIME_STEP / relax_time)
    residual_heat_content = jnp.exp(-TIME_STEP / (1.5 * relax_time))
    equilibrium_steam_load = 0.4 * jnp.exp(2.0 * (parcel_hotness_measure - 1.0))
    evaporated_share = 1.0 - jnp.exp(
        -0.3 * jax.nn.softplus(4.0 * (equilibrium_steam_load - local_air_sample[:, 0]))
    )
    evaporated = particle_weights_list * evaporated_share
    ambient_heat_content = local_air_sample[:, 1]
    gas_velocity = local_air_sample[:, 2:5]
    adjusted_heat_content = (
        ambient_heat_content
        + (parcel_hotness_measure - ambient_heat_content) * residual_heat_content
        - PHASE_CHANGE_COST * evaporated_share
    )
    velocity_new = gas_velocity + (particle_speed_vector - gas_velocity) * keep_velocity[:, None]
    enthalpy_injection = (
        0.5 * particle_weights_list * (parcel_hotness_measure - adjusted_heat_content)
    )
    push_source = particle_weights_list[:, None] * (particle_speed_vector - velocity_new)
    updated = jnp.concatenate(
        [
            (particle_weights_list - evaporated)[:, None],
            adjusted_heat_content[:, None],
            velocity_new,
        ],
        axis=1,
    )
    sources = jnp.concatenate(
        [evaporated[:, None], enthalpy_injection[:, None], push_source], axis=1
    )
    return (updated, sources)


def laplacian(padded):
    centre = padded[:, 1:-1, 1:-1, 1:-1]
    beside = padded[:, 2:, 1:-1, 1:-1] + padded[:, :-2, 1:-1, 1:-1]
    beside = beside + padded[:, 1:-1, 2:, 1:-1] + padded[:, 1:-1, :-2, 1:-1]
    beside = beside + padded[:, 1:-1, 1:-1, 2:] + padded[:, 1:-1, 1:-1, :-2]
    return beside - 6.0 * centre


PAIR_LANES = 256
DEPTH_ROWS = 136


def split_bf16(value):
    high = value.astype(jnp.bfloat16)
    low = (value - high.astype(jnp.float32)).astype(jnp.bfloat16)
    return high, low


def three_pass(a, b, dims):
    a_high, a_low = split_bf16(a)
    b_high, b_low = split_bf16(b)
    out = None
    for x, y in ((a_high, b_high), (a_high, b_low), (a_low, b_high)):
        part = lax.dot_general(x, y, (dims, ((), ())), preferred_element_type=jnp.float32)
        out = part if out is None else out + part
    return out


GROUP = 8


def coupling_kernel(
    live_ref, dest_ref, table_ref, parcel_ref, cell_ref, offset_ref, factor_ref,
    kept_ref, outbox_ref, deposit_ref,
    weight_scr, depth_scr, spread_scr, updated_scr, count_scr, table_high_ref, table_low_ref,
    *, span_y, span_z, stride,
):
    fields = parcel_ref.shape[0]
    blocks = parcel_ref.shape[1]
    lanes = parcel_ref.shape[2]
    plane_size = span_y * span_z
    deposit_ref[...] = jnp.zeros(deposit_ref.shape, jnp.float32)
    table_high, table_low = split_bf16(table_ref[...])
    table_high_ref[...] = table_high
    table_low_ref[...] = table_low
    live = live_ref[0]
    pair_iota = lax.broadcasted_iota(jnp.int32, (PAIR_LANES, lanes), 0)
    depth_iota = lax.broadcasted_iota(jnp.int32, (DEPTH_ROWS, lanes), 0)

    def group(g, carry):
        first = pl.multiple_of(g * GROUP, GROUP)
        cells = cell_ref[pl.ds(first, GROUP), :]
        offsets = offset_ref[:, pl.ds(first, GROUP), :]
        parcels = parcel_ref[:, pl.ds(first, GROUP), :]
        factors = factor_ref[:, pl.ds(first, GROUP), :]
        flat = cells.astype(jnp.float32) + 0.5
        cell_x = jnp.floor(flat * (1.0 / plane_size))
        rest = flat - cell_x * plane_size
        cell_y = jnp.floor(rest * (1.0 / span_z))
        cell_z = (rest - cell_y * span_z).astype(jnp.int32)
        cell_x = cell_x.astype(jnp.int32)
        cell_y = cell_y.astype(jnp.int32)
        step_sign = jnp.where(offsets >= 0.0, 1, -1).astype(jnp.int32)
        far_share = jnp.abs(offsets)
        near_share = 1.0 - far_share
        for j in range(GROUP):
            weights = jnp.zeros((PAIR_LANES, lanes), jnp.float32)
            for bit_x in range(2):
                for bit_y in range(2):
                    share = (far_share[0, j:j + 1] if bit_x else near_share[0, j:j + 1]) * (
                        far_share[1, j:j + 1] if bit_y else near_share[1, j:j + 1]
                    )
                    target = (
                        (cell_x[j:j + 1] + bit_x * step_sign[0, j:j + 1]) * stride
                        + cell_y[j:j + 1]
                        + bit_y * step_sign[1, j:j + 1]
                    )
                    weights = weights + jnp.where(pair_iota == target, share, 0.0)
            weight_scr[:, j * lanes:(j + 1) * lanes] = weights
            depth_weights = jnp.where(
                depth_iota == cell_z[j:j + 1], near_share[2, j:j + 1], 0.0
            ) + jnp.where(
                depth_iota == cell_z[j:j + 1] + step_sign[2, j:j + 1], far_share[2, j:j + 1], 0.0
            )
            depth_scr[:, j * lanes:(j + 1) * lanes] = depth_weights
        weight_high, weight_low = split_bf16(weight_scr[...])
        table_high = table_high_ref[...]
        mixed = (
            jnp.dot(table_high, weight_high, preferred_element_type=jnp.float32)
            + jnp.dot(table_high, weight_low, preferred_element_type=jnp.float32)
            + jnp.dot(table_low_ref[...], weight_high, preferred_element_type=jnp.float32)
        )
        for j in range(GROUP):
            b = first + j
            depth_weights = depth_scr[:, j * lanes:(j + 1) * lanes]
            sample = [
                jnp.sum(
                    mixed[f * DEPTH_ROWS:(f + 1) * DEPTH_ROWS, j * lanes:(j + 1) * lanes]
                    * depth_weights,
                    axis=0,
                    keepdims=True,
                )
                for f in range(fields)
            ]
            mass = parcels[0, j:j + 1]
            heat = parcels[1, j:j + 1]
            keep_velocity = factors[0, j:j + 1]
            residual_heat = factors[1, j:j + 1]
            equilibrium = factors[2, j:j + 1]
            x = 4.0 * (equilibrium - sample[0])
            soft = jnp.maximum(x, 0.0) + jnp.log1p(jnp.exp(-jnp.abs(x)))
            share = 1.0 - jnp.exp(-0.3 * soft)
            evaporated = mass * share
            ambient = sample[1]
            adjusted = ambient + (heat - ambient) * residual_heat - PHASE_CHANGE_COST * share
            velocity = [
                sample[2 + d] + (parcels[2 + d, j:j + 1] - sample[2 + d]) * keep_velocity
                for d in range(3)
            ]
            enthalpy = 0.5 * mass * (heat - adjusted)
            push = [mass * (parcels[2 + d, j:j + 1] - velocity[d]) for d in range(3)]
            rows = [mass - evaporated, adjusted] + velocity
            for f in range(fields):
                updated_scr[f, pl.ds(b, 1), :] = rows[f]
            alive = b < live
            sources = [jnp.where(alive, s, 0.0) for s in [evaporated, enthalpy] + push]
            spread_scr[:, j * lanes:(j + 1) * lanes] = jnp.concatenate(
                [s * depth_weights for s in sources], axis=0
            )
        spread_high, spread_low = split_bf16(spread_scr[...])
        dims = (((1,), (1,)), ((), ()))
        deposit_ref[...] += (
            lax.dot_general(weight_high, spread_high, dims, preferred_element_type=jnp.float32)
            + lax.dot_general(weight_low, spread_high, dims, preferred_element_type=jnp.float32)
            + lax.dot_general(weight_high, spread_low, dims, preferred_element_type=jnp.float32)
        )
        return carry

    lax.fori_loop(0, blocks // GROUP, group, 0)

    kept_ref[...] = jnp.zeros(kept_ref.shape, jnp.float32)
    outbox_ref[...] = jnp.zeros(outbox_ref.shape, jnp.float32)
    for d in range(27):
        count_scr[d] = 0

    def route(b, carry):
        d = jnp.minimum(jnp.maximum(dest_ref[b], 0), 26)
        alive = b < live

        @pl.when(alive & (d == 13))
        def _():
            kept_ref[:, pl.ds(b, 1), :] = updated_scr[:, pl.ds(b, 1), :]

        rank = count_scr[d]

        @pl.when(alive & (d != 13) & (rank < SLOTS))
        def _():
            for f in range(fields):
                outbox_ref[d * SLOTS + rank, :, f * lanes:(f + 1) * lanes] = updated_scr[
                    f, pl.ds(b, 1), :
                ]
            count_scr[d] = rank + 1

        return carry

    lax.fori_loop(0, blocks, route, 0)


def local(gas_state, parcels, parcel_cells, offsets, destination, live_blocks):
    fields, size_x, size_y, size_z = gas_state.shape
    blocks, parcel_fields, block_parcels = parcels.shape
    padded = with_halo(gas_state, (("gx", 1), ("gy", 2), ("gz", 3)), 1)
    span_x = size_x + 2
    span_y = size_y + 2
    span_z = size_z + 2
    pair_count = span_x * span_y
    plane_size = span_y * span_z
    stride = -(-span_y // 8) * 8
    pair_count = span_x * stride
    table = jnp.pad(padded, ((0, 0), (0, 0), (0, stride - span_y), (0, 0)))
    table = jnp.transpose(table, (0, 3, 1, 2)).reshape(fields, span_z, pair_count)
    table = jnp.pad(table, ((0, 0), (0, DEPTH_ROWS - span_z), (0, PAIR_LANES - pair_count)))
    table = table.reshape(fields * DEPTH_ROWS, PAIR_LANES)
    parcel_rows = jnp.transpose(parcels, (1, 0, 2))
    offset_rows = jnp.transpose(offsets, (1, 0, 2))
    relax_time = 0.4 * parcel_rows[0] ** (2.0 / 3.0)
    factors = jnp.stack(
        [
            jnp.exp(-TIME_STEP / relax_time),
            jnp.exp(-TIME_STEP / (1.5 * relax_time)),
            0.4 * jnp.exp(2.0 * (parcel_rows[1] - 1.0)),
        ],
        axis=0,
    )
    vmem = pl.BlockSpec(memory_space=pltpu.VMEM)
    smem = pl.BlockSpec(memory_space=pltpu.SMEM)
    lanes = GROUP * block_parcels
    kept_rows, outbox_rows, deposit_rows = pl.pallas_call(
        functools.partial(coupling_kernel, span_y=span_y, span_z=span_z, stride=stride),
        out_shape=(
            jax.ShapeDtypeStruct(parcel_rows.shape, jnp.float32),
            jax.ShapeDtypeStruct((27 * SLOTS, 1, fields * DEPTH_ROWS), jnp.float32),
            jax.ShapeDtypeStruct((PAIR_LANES, fields * DEPTH_ROWS), jnp.float32),
        ),
        in_specs=[smem, smem] + [vmem] * 5,
        out_specs=(vmem, vmem, vmem),
        scratch_shapes=[
            pltpu.VMEM((PAIR_LANES, lanes), jnp.float32),
            pltpu.VMEM((DEPTH_ROWS, lanes), jnp.float32),
            pltpu.VMEM((fields * DEPTH_ROWS, lanes), jnp.float32),
            pltpu.VMEM(parcel_rows.shape, jnp.float32),
            pltpu.SMEM((32,), jnp.int32),
            pltpu.VMEM(table.shape, jnp.bfloat16),
            pltpu.VMEM(table.shape, jnp.bfloat16),
        ],
    )(live_blocks, destination, table, parcel_rows, parcel_cells, offset_rows, factors)
    kept = jnp.transpose(kept_rows, (1, 0, 2))
    width = fields * DEPTH_ROWS
    deposit = deposit_rows[:pair_count].reshape(span_x, stride, width)
    boxes = outbox_rows.reshape(3, 9 * SLOTS, width)
    deposit, boxes = exchange_rows(deposit, boxes, "gx", 0, stride)
    boxes = boxes.reshape(boxes.shape[0], 3, 3 * SLOTS, width)
    deposit, boxes = exchange_rows(deposit[:, :span_y], boxes, "gy", 1, size_x)
    deposit = deposit.reshape(size_x, size_y, fields, DEPTH_ROWS)
    boxes = boxes.reshape(boxes.shape[:2] + (3, SLOTS, width))
    plane = size_x * size_y * fields
    count = lax.axis_size("gz")
    forward = [(i, i + 1) for i in range(count - 1)]
    backward = [(target, source) for source, target in forward]
    up = jnp.concatenate(
        [
            jnp.pad(deposit[..., span_z - 1].reshape(1, plane), ((0, 0), (0, width - plane))),
            boxes[:, :, 2].reshape(-1, width),
        ],
        axis=0,
    )
    down = jnp.concatenate(
        [
            jnp.pad(deposit[..., 0].reshape(1, plane), ((0, 0), (0, width - plane))),
            boxes[:, :, 0].reshape(-1, width),
        ],
        axis=0,
    )
    below = lax.ppermute(up, "gz", forward)
    above = lax.ppermute(down, "gz", backward)
    owned = deposit[..., 1:span_z - 1]
    owned = owned + jnp.pad(
        below[0, :plane].reshape(size_x, size_y, fields, 1), ((0, 0), (0, 0), (0, 0), (0, size_z - 1))
    )
    owned = owned + jnp.pad(
        above[0, :plane].reshape(size_x, size_y, fields, 1), ((0, 0), (0, 0), (0, 0), (size_z - 1, 0))
    )
    cell_sources = jnp.transpose(owned, (2, 0, 1, 3))
    face = boxes.shape[:2] + (1, SLOTS, width)
    boxes = jnp.concatenate(
        [below[1:].reshape(face), boxes, above[1:].reshape(face)], axis=2
    )
    kappa = jnp.array(DIFFUSION, jnp.float32)[:, None, None, None]
    gas_next = gas_state + kappa * laplacian(padded) + COUPLING * cell_sources
    arrived_boxes = boxes[0::2, 0::2, 0::2][..., :parcel_fields * block_parcels]
    arrived = arrived_boxes.reshape((27 * SLOTS, parcel_fields, block_parcels))
    return (gas_next, kept, arrived)


def solution(mesh):
    placed = (
        P(None, "gx", "gy", "gz"),
        P(("gx", "gy", "gz"), None, None),
        P(("gx", "gy", "gz"), None),
        P(("gx", "gy", "gz"), None, None),
        P(("gx", "gy", "gz")),
        P(("gx", "gy", "gz")),
    )
    return jax.shard_map(
        local,
        mesh=mesh,
        in_specs=placed,
        out_specs=(
            P(None, "gx", "gy", "gz"),
            P(("gx", "gy", "gz"), None, None),
            P(("gx", "gy", "gz"), None, None),
        ),
        check_vma=False,
    )
```

```python
import functools

import jax
import jax.numpy as jnp
from jax import lax
from jax.sharding import PartitionSpec as P
from jax.experimental import pallas as pl
from jax.experimental.pallas import tpu as pltpu

SLOTS = 4


DIFFUSION = (0.06, 0.1, 0.12, 0.12, 0.12)
TIME_STEP = 0.5
COUPLING = 0.5
PHASE_CHANGE_COST = 0.5


def with_halo(block, sides, width):
    for axis, dim in sides:
        count = lax.axis_size(axis)
        forward = [(i, i + 1) for i in range(count - 1)]
        backward = [(target, source) for source, target in forward]
        low = lax.ppermute(
            lax.slice_in_dim(block, block.shape[dim] - width, None, axis=dim), axis, forward
        )
        high = lax.ppermute(lax.slice_in_dim(block, 0, width, axis=dim), axis, backward)
        block = jnp.concatenate([low, block, high], axis=dim)
    return block


def fold_ghosts(block, sides):
    for axis, dim in sides:
        count = lax.axis_size(axis)
        forward = [(i, i + 1) for i in range(count - 1)]
        backward = [(target, source) for source, target in forward]
        span = block.shape[dim]
        below = lax.ppermute(lax.slice_in_dim(block, span - 1, span, axis=dim), axis, forward)
        above = lax.ppermute(lax.slice_in_dim(block, 0, 1, axis=dim), axis, backward)
        inner = lax.slice_in_dim(block, 1, span - 1, axis=dim)
        low_pad = [(0, 0)] * block.ndim
        high_pad = [(0, 0)] * block.ndim
        low_pad[dim] = (0, span - 3)
        high_pad[dim] = (span - 3, 0)
        block = inner + jnp.pad(below, low_pad) + jnp.pad(above, high_pad)
    return block


def parcel_update(current_condition, local_air_sample):
    particle_weights_list = current_condition[:, 0]
    parcel_hotness_measure = current_condition[:, 1]
    particle_speed_vector = current_condition[:, 2:5]
    relax_time = 0.4 * particle_weights_list ** (2.0 / 3.0)
    keep_velocity = jnp.exp(-TIME_STEP / relax_time)
    residual_heat_content = jnp.exp(-TIME_STEP / (1.5 * relax_time))
    equilibrium_steam_load = 0.4 * jnp.exp(2.0 * (parcel_hotness_measure - 1.0))
    evaporated_share = 1.0 - jnp.exp(
        -0.3 * jax.nn.softplus(4.0 * (equilibrium_steam_load - local_air_sample[:, 0]))
    )
    evaporated = particle_weights_list * evaporated_share
    ambient_heat_content = local_air_sample[:, 1]
    gas_velocity = local_air_sample[:, 2:5]
    adjusted_heat_content = (
        ambient_heat_content
        + (parcel_hotness_measure - ambient_heat_content) * residual_heat_content
        - PHASE_CHANGE_COST * evaporated_share
    )
    velocity_new = gas_velocity + (particle_speed_vector - gas_velocity) * keep_velocity[:, None]
    enthalpy_injection = (
        0.5 * particle_weights_list * (parcel_hotness_measure - adjusted_heat_content)
    )
    push_source = particle_weights_list[:, None] * (particle_speed_vector - velocity_new)
    updated = jnp.concatenate(
        [
            (particle_weights_list - evaporated)[:, None],
            adjusted_heat_content[:, None],
            velocity_new,
        ],
        axis=1,
    )
    sources = jnp.concatenate(
        [evaporated[:, None], enthalpy_injection[:, None], push_source], axis=1
    )
    return (updated, sources)


def laplacian(padded):
    centre = padded[:, 1:-1, 1:-1, 1:-1]
    beside = padded[:, 2:, 1:-1, 1:-1] + padded[:, :-2, 1:-1, 1:-1]
    beside = beside + padded[:, 1:-1, 2:, 1:-1] + padded[:, 1:-1, :-2, 1:-1]
    beside = beside + padded[:, 1:-1, 1:-1, 2:] + padded[:, 1:-1, 1:-1, :-2]
    return beside - 6.0 * centre


PAIR_LANES = 256
DEPTH_ROWS = 136


def split_bf16(value):
    high = value.astype(jnp.bfloat16)
    low = (value - high.astype(jnp.float32)).astype(jnp.bfloat16)
    return high, low


def three_pass(a, b, dims):
    a_high, a_low = split_bf16(a)
    b_high, b_low = split_bf16(b)
    out = None
    for x, y in ((a_high, b_high), (a_high, b_low), (a_low, b_high)):
        part = lax.dot_general(x, y, (dims, ((), ())), preferred_element_type=jnp.float32)
        out = part if out is None else out + part
    return out


GROUP = 8


def coupling_kernel(
    live_ref, dest_ref, table_ref, parcel_ref, cell_ref, offset_ref, factor_ref,
    kept_ref, outbox_ref, deposit_ref,
    weight_scr, depth_scr, spread_scr, updated_scr, count_scr, table_high_ref, table_low_ref,
    *, span_y, span_z, stride,
):
    fields = parcel_ref.shape[0]
    blocks = parcel_ref.shape[1]
    lanes = parcel_ref.shape[2]
    plane_size = span_y * span_z
    deposit_ref[...] = jnp.zeros(deposit_ref.shape, jnp.float32)
    table_high, table_low = split_bf16(table_ref[...])
    table_high_ref[...] = table_high
    table_low_ref[...] = table_low
    live = live_ref[0]
    pair_iota = lax.broadcasted_iota(jnp.int32, (PAIR_LANES, lanes), 0)
    depth_iota = lax.broadcasted_iota(jnp.int32, (DEPTH_ROWS, lanes), 0)

    def group(g, carry):
        first = pl.multiple_of(g * GROUP, GROUP)
        cells = cell_ref[pl.ds(first, GROUP), :]
        offsets = offset_ref[:, pl.ds(first, GROUP), :]
        parcels = parcel_ref[:, pl.ds(first, GROUP), :]
        factors = factor_ref[:, pl.ds(first, GROUP), :]
        flat = cells.astype(jnp.float32) + 0.5
        cell_x = jnp.floor(flat * (1.0 / plane_size))
        rest = flat - cell_x * plane_size
        cell_y = jnp.floor(rest * (1.0 / span_z))
        cell_z = (rest - cell_y * span_z).astype(jnp.int32)
        cell_x = cell_x.astype(jnp.int32)
        cell_y = cell_y.astype(jnp.int32)
        step_sign = jnp.where(offsets >= 0.0, 1, -1).astype(jnp.int32)
        far_share = jnp.abs(offsets)
        near_share = 1.0 - far_share
        for j in range(GROUP):
            weights = jnp.zeros((PAIR_LANES, lanes), jnp.float32)
            for bit_x in range(2):
                for bit_y in range(2):
                    share = (far_share[0, j:j + 1] if bit_x else near_share[0, j:j + 1]) * (
                        far_share[1, j:j + 1] if bit_y else near_share[1, j:j + 1]
                    )
                    target = (
                        (cell_x[j:j + 1] + bit_x * step_sign[0, j:j + 1]) * stride
                        + cell_y[j:j + 1]
                        + bit_y * step_sign[1, j:j + 1]
                    )
                    weights = weights + jnp.where(pair_iota == target, share, 0.0)
            weight_scr[:, j * lanes:(j + 1) * lanes] = weights
            depth_weights = jnp.where(
                depth_iota == cell_z[j:j + 1], near_share[2, j:j + 1], 0.0
            ) + jnp.where(
                depth_iota == cell_z[j:j + 1] + step_sign[2, j:j + 1], far_share[2, j:j + 1], 0.0
            )
            depth_scr[:, j * lanes:(j + 1) * lanes] = depth_weights
        weight_high, weight_low = split_bf16(weight_scr[...])
        table_high = table_high_ref[...]
        mixed = (
            jnp.dot(table_high, weight_high, preferred_element_type=jnp.float32)
            + jnp.dot(table_high, weight_low, preferred_element_type=jnp.float32)
            + jnp.dot(table_low_ref[...], weight_high, preferred_element_type=jnp.float32)
        )
        for j in range(GROUP):
            b = first + j
            depth_weights = depth_scr[:, j * lanes:(j + 1) * lanes]
            sample = [
                jnp.sum(
                    mixed[f * DEPTH_ROWS:(f + 1) * DEPTH_ROWS, j * lanes:(j + 1) * lanes]
                    * depth_weights,
                    axis=0,
                    keepdims=True,
                )
                for f in range(fields)
            ]
            mass = parcels[0, j:j + 1]
            heat = parcels[1, j:j + 1]
            keep_velocity = factors[0, j:j + 1]
            residual_heat = factors[1, j:j + 1]
            equilibrium = factors[2, j:j + 1]
            x = 4.0 * (equilibrium - sample[0])
            soft = jnp.maximum(x, 0.0) + jnp.log1p(jnp.exp(-jnp.abs(x)))
            share = 1.0 - jnp.exp(-0.3 * soft)
            evaporated = mass * share
            ambient = sample[1]
            adjusted = ambient + (heat - ambient) * residual_heat - PHASE_CHANGE_COST * share
            velocity = [
                sample[2 + d] + (parcels[2 + d, j:j + 1] - sample[2 + d]) * keep_velocity
                for d in range(3)
            ]
            enthalpy = 0.5 * mass * (heat - adjusted)
            push = [mass * (parcels[2 + d, j:j + 1] - velocity[d]) for d in range(3)]
            rows = [mass - evaporated, adjusted] + velocity
            for f in range(fields):
                updated_scr[f, pl.ds(b, 1), :] = rows[f]
            alive = b < live
            sources = [jnp.where(alive, s, 0.0) for s in [evaporated, enthalpy] + push]
            spread_scr[:, j * lanes:(j + 1) * lanes] = jnp.concatenate(
                [s * depth_weights for s in sources], axis=0
            )
        spread_high, spread_low = split_bf16(spread_scr[...])
        dims = (((1,), (1,)), ((), ()))
        deposit_ref[...] += (
            lax.dot_general(weight_high, spread_high, dims, preferred_element_type=jnp.float32)
            + lax.dot_general(weight_low, spread_high, dims, preferred_element_type=jnp.float32)
            + lax.dot_general(weight_high, spread_low, dims, preferred_element_type=jnp.float32)
        )
        return carry

    lax.fori_loop(0, blocks // GROUP, group, 0)

    kept_ref[...] = jnp.zeros(kept_ref.shape, jnp.float32)
    outbox_ref[...] = jnp.zeros(outbox_ref.shape, jnp.float32)
    for d in range(27):
        count_scr[d] = 0

    def route(b, carry):
        d = jnp.minimum(jnp.maximum(dest_ref[b], 0), 26)
        alive = b < live

        @pl.when(alive & (d == 13))
        def _():
            kept_ref[:, pl.ds(b, 1), :] = updated_scr[:, pl.ds(b, 1), :]

        rank = count_scr[d]

        @pl.when(alive & (d != 13) & (rank < SLOTS))
        def _():
            outbox_ref[:, pl.ds(d * SLOTS + rank, 1), :] = updated_scr[:, pl.ds(b, 1), :]
            count_scr[d] = rank + 1

        return carry

    lax.fori_loop(0, blocks, route, 0)


def local(gas_state, parcels, parcel_cells, offsets, destination, live_blocks):
    fields, size_x, size_y, size_z = gas_state.shape
    blocks, parcel_fields, block_parcels = parcels.shape
    padded = with_halo(gas_state, (("gx", 1), ("gy", 2), ("gz", 3)), 1)
    span_x = size_x + 2
    span_y = size_y + 2
    span_z = size_z + 2
    pair_count = span_x * span_y
    plane_size = span_y * span_z
    stride = -(-span_y // 8) * 8
    pair_count = span_x * stride
    table = jnp.pad(padded, ((0, 0), (0, 0), (0, stride - span_y), (0, 0)))
    table = jnp.transpose(table, (0, 3, 1, 2)).reshape(fields, span_z, pair_count)
    table = jnp.pad(table, ((0, 0), (0, DEPTH_ROWS - span_z), (0, PAIR_LANES - pair_count)))
    table = table.reshape(fields * DEPTH_ROWS, PAIR_LANES)
    parcel_rows = jnp.transpose(parcels, (1, 0, 2))
    offset_rows = jnp.transpose(offsets, (1, 0, 2))
    relax_time = 0.4 * parcel_rows[0] ** (2.0 / 3.0)
    factors = jnp.stack(
        [
            jnp.exp(-TIME_STEP / relax_time),
            jnp.exp(-TIME_STEP / (1.5 * relax_time)),
            0.4 * jnp.exp(2.0 * (parcel_rows[1] - 1.0)),
        ],
        axis=0,
    )
    vmem = pl.BlockSpec(memory_space=pltpu.VMEM)
    smem = pl.BlockSpec(memory_space=pltpu.SMEM)
    lanes = GROUP * block_parcels
    kept_rows, outbox_rows, deposit_rows = pl.pallas_call(
        functools.partial(coupling_kernel, span_y=span_y, span_z=span_z, stride=stride),
        out_shape=(
            jax.ShapeDtypeStruct(parcel_rows.shape, jnp.float32),
            jax.ShapeDtypeStruct((parcel_fields, 27 * SLOTS, block_parcels), jnp.float32),
            jax.ShapeDtypeStruct((PAIR_LANES, fields * DEPTH_ROWS), jnp.float32),
        ),
        in_specs=[smem, smem] + [vmem] * 5,
        out_specs=(vmem, vmem, vmem),
        scratch_shapes=[
            pltpu.VMEM((PAIR_LANES, lanes), jnp.float32),
            pltpu.VMEM((DEPTH_ROWS, lanes), jnp.float32),
            pltpu.VMEM((fields * DEPTH_ROWS, lanes), jnp.float32),
            pltpu.VMEM(parcel_rows.shape, jnp.float32),
            pltpu.SMEM((32,), jnp.int32),
            pltpu.VMEM(table.shape, jnp.bfloat16),
            pltpu.VMEM(table.shape, jnp.bfloat16),
        ],
    )(live_blocks, destination, table, parcel_rows, parcel_cells, offset_rows, factors)
    kept = jnp.transpose(kept_rows, (1, 0, 2))
    deposit = deposit_rows[:pair_count].reshape(span_x, stride, fields, DEPTH_ROWS)
    deposit = jnp.transpose(deposit[:, :span_y, :, :span_z], (2, 0, 1, 3))
    cell_sources = fold_ghosts(deposit, (("gx", 1), ("gy", 2), ("gz", 3)))
    kappa = jnp.array(DIFFUSION, jnp.float32)[:, None, None, None]
    gas_next = gas_state + kappa * laplacian(padded) + COUPLING * cell_sources
    outbox = outbox_rows.reshape((parcel_fields, 3, 3, 3, SLOTS, block_parcels))
    widened = with_halo(outbox, (("gx", 1), ("gy", 2), ("gz", 3)), 1)
    arrived_boxes = widened[:, 0::2, 0::2, 0::2]
    arrived = jnp.transpose(
        arrived_boxes.reshape((parcel_fields, 27 * SLOTS, block_parcels)), (1, 0, 2)
    )
    return (gas_next, kept, arrived)


def solution(mesh):
    placed = (
        P(None, "gx", "gy", "gz"),
        P(("gx", "gy", "gz"), None, None),
        P(("gx", "gy", "gz"), None),
        P(("gx", "gy", "gz"), None, None),
        P(("gx", "gy", "gz")),
        P(("gx", "gy", "gz")),
    )
    return jax.shard_map(
        local,
        mesh=mesh,
        in_specs=placed,
        out_specs=(
            P(None, "gx", "gy", "gz"),
            P(("gx", "gy", "gz"), None, None),
            P(("gx", "gy", "gz"), None, None),
        ),
        check_vma=False,
    )
```

```python
import functools

import jax
import jax.numpy as jnp
from jax import lax
from jax.sharding import PartitionSpec as P
from jax.experimental import pallas as pl
from jax.experimental.pallas import tpu as pltpu

SLOTS = 4


DIFFUSION = (0.06, 0.1, 0.12, 0.12, 0.12)
TIME_STEP = 0.5
COUPLING = 0.5
PHASE_CHANGE_COST = 0.5


def with_halo(block, sides, width):
    for axis, dim in sides:
        count = lax.axis_size(axis)
        forward = [(i, i + 1) for i in range(count - 1)]
        backward = [(target, source) for source, target in forward]
        low = lax.ppermute(
            lax.slice_in_dim(block, block.shape[dim] - width, None, axis=dim), axis, forward
        )
        high = lax.ppermute(lax.slice_in_dim(block, 0, width, axis=dim), axis, backward)
        block = jnp.concatenate([low, block, high], axis=dim)
    return block


def fold_ghosts(block, sides):
    for axis, dim in sides:
        count = lax.axis_size(axis)
        forward = [(i, i + 1) for i in range(count - 1)]
        backward = [(target, source) for source, target in forward]
        span = block.shape[dim]
        below = lax.ppermute(lax.slice_in_dim(block, span - 1, span, axis=dim), axis, forward)
        above = lax.ppermute(lax.slice_in_dim(block, 0, 1, axis=dim), axis, backward)
        inner = lax.slice_in_dim(block, 1, span - 1, axis=dim)
        low_pad = [(0, 0)] * block.ndim
        high_pad = [(0, 0)] * block.ndim
        low_pad[dim] = (0, span - 3)
        high_pad[dim] = (span - 3, 0)
        block = inner + jnp.pad(below, low_pad) + jnp.pad(above, high_pad)
    return block


def fold_and_widen(block, boxes, sides):
    for axis, dim, box_dim in sides:
        count = lax.axis_size(axis)
        forward = [(i, i + 1) for i in range(count - 1)]
        backward = [(target, source) for source, target in forward]
        span = block.shape[dim]
        width = boxes.shape[box_dim]
        sends = lax.optimization_barrier(
            (
                lax.slice_in_dim(block, span - 1, span, axis=dim),
                lax.slice_in_dim(block, 0, 1, axis=dim),
                lax.slice_in_dim(boxes, width - 1, width, axis=box_dim),
                lax.slice_in_dim(boxes, 0, 1, axis=box_dim),
            )
        )
        below, above, box_below, box_above = lax.optimization_barrier(
            (
                lax.ppermute(sends[0], axis, forward),
                lax.ppermute(sends[1], axis, backward),
                lax.ppermute(sends[2], axis, forward),
                lax.ppermute(sends[3], axis, backward),
            )
        )
        inner = lax.slice_in_dim(block, 1, span - 1, axis=dim)
        low_pad = [(0, 0)] * block.ndim
        high_pad = [(0, 0)] * block.ndim
        low_pad[dim] = (0, span - 3)
        high_pad[dim] = (span - 3, 0)
        block = inner + jnp.pad(below, low_pad) + jnp.pad(above, high_pad)
        boxes = jnp.concatenate([box_below, boxes, box_above], axis=box_dim)
    return block, boxes


def parcel_update(current_condition, local_air_sample):
    particle_weights_list = current_condition[:, 0]
    parcel_hotness_measure = current_condition[:, 1]
    particle_speed_vector = current_condition[:, 2:5]
    relax_time = 0.4 * particle_weights_list ** (2.0 / 3.0)
    keep_velocity = jnp.exp(-TIME_STEP / relax_time)
    residual_heat_content = jnp.exp(-TIME_STEP / (1.5 * relax_time))
    equilibrium_steam_load = 0.4 * jnp.exp(2.0 * (parcel_hotness_measure - 1.0))
    evaporated_share = 1.0 - jnp.exp(
        -0.3 * jax.nn.softplus(4.0 * (equilibrium_steam_load - local_air_sample[:, 0]))
    )
    evaporated = particle_weights_list * evaporated_share
    ambient_heat_content = local_air_sample[:, 1]
    gas_velocity = local_air_sample[:, 2:5]
    adjusted_heat_content = (
        ambient_heat_content
        + (parcel_hotness_measure - ambient_heat_content) * residual_heat_content
        - PHASE_CHANGE_COST * evaporated_share
    )
    velocity_new = gas_velocity + (particle_speed_vector - gas_velocity) * keep_velocity[:, None]
    enthalpy_injection = (
        0.5 * particle_weights_list * (parcel_hotness_measure - adjusted_heat_content)
    )
    push_source = particle_weights_list[:, None] * (particle_speed_vector - velocity_new)
    updated = jnp.concatenate(
        [
            (particle_weights_list - evaporated)[:, None],
            adjusted_heat_content[:, None],
            velocity_new,
        ],
        axis=1,
    )
    sources = jnp.concatenate(
        [evaporated[:, None], enthalpy_injection[:, None], push_source], axis=1
    )
    return (updated, sources)


def laplacian(padded):
    centre = padded[:, 1:-1, 1:-1, 1:-1]
    beside = padded[:, 2:, 1:-1, 1:-1] + padded[:, :-2, 1:-1, 1:-1]
    beside = beside + padded[:, 1:-1, 2:, 1:-1] + padded[:, 1:-1, :-2, 1:-1]
    beside = beside + padded[:, 1:-1, 1:-1, 2:] + padded[:, 1:-1, 1:-1, :-2]
    return beside - 6.0 * centre


PAIR_LANES = 256
DEPTH_ROWS = 136


def split_bf16(value):
    high = value.astype(jnp.bfloat16)
    low = (value - high.astype(jnp.float32)).astype(jnp.bfloat16)
    return high, low


def three_pass(a, b, dims):
    a_high, a_low = split_bf16(a)
    b_high, b_low = split_bf16(b)
    out = None
    for x, y in ((a_high, b_high), (a_high, b_low), (a_low, b_high)):
        part = lax.dot_general(x, y, (dims, ((), ())), preferred_element_type=jnp.float32)
        out = part if out is None else out + part
    return out


GROUP = 8


def coupling_kernel(
    live_ref, dest_ref, table_ref, parcel_ref, cell_ref, offset_ref, factor_ref,
    kept_ref, outbox_ref, deposit_ref,
    weight_scr, depth_scr, spread_scr, updated_scr, count_scr, table_high_ref, table_low_ref,
    *, span_y, span_z,
):
    fields = parcel_ref.shape[0]
    blocks = parcel_ref.shape[1]
    lanes = parcel_ref.shape[2]
    plane_size = span_y * span_z
    deposit_ref[...] = jnp.zeros(deposit_ref.shape, jnp.float32)
    table_high, table_low = split_bf16(table_ref[...])
    table_high_ref[...] = table_high
    table_low_ref[...] = table_low
    live = live_ref[0]
    pair_iota = lax.broadcasted_iota(jnp.int32, (PAIR_LANES, lanes), 0)
    depth_iota = lax.broadcasted_iota(jnp.int32, (DEPTH_ROWS, lanes), 0)

    def group(g, carry):
        first = pl.multiple_of(g * GROUP, GROUP)
        cells = cell_ref[pl.ds(first, GROUP), :]
        offsets = offset_ref[:, pl.ds(first, GROUP), :]
        parcels = parcel_ref[:, pl.ds(first, GROUP), :]
        factors = factor_ref[:, pl.ds(first, GROUP), :]
        flat = cells.astype(jnp.float32) + 0.5
        cell_x = jnp.floor(flat * (1.0 / plane_size))
        rest = flat - cell_x * plane_size
        cell_y = jnp.floor(rest * (1.0 / span_z))
        cell_z = (rest - cell_y * span_z).astype(jnp.int32)
        cell_x = cell_x.astype(jnp.int32)
        cell_y = cell_y.astype(jnp.int32)
        step_sign = jnp.where(offsets >= 0.0, 1, -1).astype(jnp.int32)
        far_share = jnp.abs(offsets)
        near_share = 1.0 - far_share
        for j in range(GROUP):
            weights = jnp.zeros((PAIR_LANES, lanes), jnp.float32)
            for bit_x in range(2):
                for bit_y in range(2):
                    share = (far_share[0, j:j + 1] if bit_x else near_share[0, j:j + 1]) * (
                        far_share[1, j:j + 1] if bit_y else near_share[1, j:j + 1]
                    )
                    target = (
                        (cell_x[j:j + 1] + bit_x * step_sign[0, j:j + 1]) * span_y
                        + cell_y[j:j + 1]
                        + bit_y * step_sign[1, j:j + 1]
                    )
                    weights = weights + jnp.where(pair_iota == target, share, 0.0)
            weight_scr[:, j * lanes:(j + 1) * lanes] = weights
            depth_weights = jnp.where(
                depth_iota == cell_z[j:j + 1], near_share[2, j:j + 1], 0.0
            ) + jnp.where(
                depth_iota == cell_z[j:j + 1] + step_sign[2, j:j + 1], far_share[2, j:j + 1], 0.0
            )
            depth_scr[:, j * lanes:(j + 1) * lanes] = depth_weights
        weight_high, weight_low = split_bf16(weight_scr[...])
        table_high = table_high_ref[...]
        mixed = (
            jnp.dot(table_high, weight_high, preferred_element_type=jnp.float32)
            + jnp.dot(table_high, weight_low, preferred_element_type=jnp.float32)
            + jnp.dot(table_low_ref[...], weight_high, preferred_element_type=jnp.float32)
        )
        for j in range(GROUP):
            b = first + j
            depth_weights = depth_scr[:, j * lanes:(j + 1) * lanes]
            sample = [
                jnp.sum(
                    mixed[f * DEPTH_ROWS:(f + 1) * DEPTH_ROWS, j * lanes:(j + 1) * lanes]
                    * depth_weights,
                    axis=0,
                    keepdims=True,
                )
                for f in range(fields)
            ]
            mass = parcels[0, j:j + 1]
            heat = parcels[1, j:j + 1]
            keep_velocity = factors[0, j:j + 1]
            residual_heat = factors[1, j:j + 1]
            equilibrium = factors[2, j:j + 1]
            x = 4.0 * (equilibrium - sample[0])
            soft = jnp.maximum(x, 0.0) + jnp.log1p(jnp.exp(-jnp.abs(x)))
            share = 1.0 - jnp.exp(-0.3 * soft)
            evaporated = mass * share
            ambient = sample[1]
            adjusted = ambient + (heat - ambient) * residual_heat - PHASE_CHANGE_COST * share
            velocity = [
                sample[2 + d] + (parcels[2 + d, j:j + 1] - sample[2 + d]) * keep_velocity
                for d in range(3)
            ]
            enthalpy = 0.5 * mass * (heat - adjusted)
            push = [mass * (parcels[2 + d, j:j + 1] - velocity[d]) for d in range(3)]
            rows = [mass - evaporated, adjusted] + velocity
            for f in range(fields):
                updated_scr[f, pl.ds(b, 1), :] = rows[f]
            alive = b < live
            sources = [jnp.where(alive, s, 0.0) for s in [evaporated, enthalpy] + push]
            spread_scr[:, j * lanes:(j + 1) * lanes] = jnp.concatenate(
                [s * depth_weights for s in sources], axis=0
            )
        spread_high, spread_low = split_bf16(spread_scr[...])
        dims = (((1,), (1,)), ((), ()))
        deposit_ref[...] += (
            lax.dot_general(spread_high, weight_high, dims, preferred_element_type=jnp.float32)
            + lax.dot_general(spread_high, weight_low, dims, preferred_element_type=jnp.float32)
            + lax.dot_general(spread_low, weight_high, dims, preferred_element_type=jnp.float32)
        )
        return carry

    lax.fori_loop(0, blocks // GROUP, group, 0)

    kept_ref[...] = jnp.zeros(kept_ref.shape, jnp.float32)
    outbox_ref[...] = jnp.zeros(outbox_ref.shape, jnp.float32)
    for d in range(27):
        count_scr[d] = 0

    def route(b, carry):
        d = jnp.minimum(jnp.maximum(dest_ref[b], 0), 26)
        alive = b < live

        @pl.when(alive & (d == 13))
        def _():
            kept_ref[:, pl.ds(b, 1), :] = updated_scr[:, pl.ds(b, 1), :]

        rank = count_scr[d]

        @pl.when(alive & (d != 13) & (rank < SLOTS))
        def _():
            outbox_ref[:, pl.ds(d * SLOTS + rank, 1), :] = updated_scr[:, pl.ds(b, 1), :]
            count_scr[d] = rank + 1

        return carry

    lax.fori_loop(0, blocks, route, 0)


def local(gas_state, parcels, parcel_cells, offsets, destination, live_blocks):
    fields, size_x, size_y, size_z = gas_state.shape
    blocks, parcel_fields, block_parcels = parcels.shape
    padded = with_halo(gas_state, (("gx", 1), ("gy", 2), ("gz", 3)), 1)
    span_x = size_x + 2
    span_y = size_y + 2
    span_z = size_z + 2
    pair_count = span_x * span_y
    plane_size = span_y * span_z
    table = jnp.transpose(padded, (0, 3, 1, 2)).reshape(fields, span_z, pair_count)
    table = jnp.pad(table, ((0, 0), (0, DEPTH_ROWS - span_z), (0, PAIR_LANES - pair_count)))
    table = table.reshape(fields * DEPTH_ROWS, PAIR_LANES)
    parcel_rows = jnp.transpose(parcels, (1, 0, 2))
    offset_rows = jnp.transpose(offsets, (1, 0, 2))
    relax_time = 0.4 * parcel_rows[0] ** (2.0 / 3.0)
    factors = jnp.stack(
        [
            jnp.exp(-TIME_STEP / relax_time),
            jnp.exp(-TIME_STEP / (1.5 * relax_time)),
            0.4 * jnp.exp(2.0 * (parcel_rows[1] - 1.0)),
        ],
        axis=0,
    )
    vmem = pl.BlockSpec(memory_space=pltpu.VMEM)
    smem = pl.BlockSpec(memory_space=pltpu.SMEM)
    lanes = GROUP * block_parcels
    kept_rows, outbox_rows, deposit_rows = pl.pallas_call(
        functools.partial(coupling_kernel, span_y=span_y, span_z=span_z),
        out_shape=(
            jax.ShapeDtypeStruct(parcel_rows.shape, jnp.float32),
            jax.ShapeDtypeStruct((parcel_fields, 27 * SLOTS, block_parcels), jnp.float32),
            jax.ShapeDtypeStruct((fields * DEPTH_ROWS, PAIR_LANES), jnp.float32),
        ),
        in_specs=[smem, smem] + [vmem] * 5,
        out_specs=(vmem, vmem, vmem),
        scratch_shapes=[
            pltpu.VMEM((PAIR_LANES, lanes), jnp.float32),
            pltpu.VMEM((DEPTH_ROWS, lanes), jnp.float32),
            pltpu.VMEM((fields * DEPTH_ROWS, lanes), jnp.float32),
            pltpu.VMEM(parcel_rows.shape, jnp.float32),
            pltpu.SMEM((32,), jnp.int32),
            pltpu.VMEM(table.shape, jnp.bfloat16),
            pltpu.VMEM(table.shape, jnp.bfloat16),
        ],
    )(live_blocks, destination, table, parcel_rows, parcel_cells, offset_rows, factors)
    kept = jnp.transpose(kept_rows, (1, 0, 2))
    deposit = deposit_rows.reshape(fields, DEPTH_ROWS, PAIR_LANES)[:, :span_z, :pair_count]
    deposit = jnp.transpose(deposit.reshape(fields, span_z, span_x, span_y), (0, 2, 3, 1))
    outbox = outbox_rows.reshape((parcel_fields, 3, 3, 3, SLOTS, block_parcels))
    cell_sources, widened = fold_and_widen(
        deposit, outbox, (("gx", 1, 1), ("gy", 2, 2), ("gz", 3, 3))
    )
    kappa = jnp.array(DIFFUSION, jnp.float32)[:, None, None, None]
    gas_next = gas_state + kappa * laplacian(padded) + COUPLING * cell_sources
    arrived_boxes = widened[:, 0::2, 0::2, 0::2]
    arrived = jnp.transpose(
        arrived_boxes.reshape((parcel_fields, 27 * SLOTS, block_parcels)), (1, 0, 2)
    )
    return (gas_next, kept, arrived)


def solution(mesh):
    placed = (
        P(None, "gx", "gy", "gz"),
        P(("gx", "gy", "gz"), None, None),
        P(("gx", "gy", "gz"), None),
        P(("gx", "gy", "gz"), None, None),
        P(("gx", "gy", "gz")),
        P(("gx", "gy", "gz")),
    )
    return jax.shard_map(
        local,
        mesh=mesh,
        in_specs=placed,
        out_specs=(
            P(None, "gx", "gy", "gz"),
            P(("gx", "gy", "gz"), None, None),
            P(("gx", "gy", "gz"), None, None),
        ),
        check_vma=False,
    )
```

```python
import functools

import jax
import jax.numpy as jnp
from jax import lax
from jax.sharding import PartitionSpec as P
from jax.experimental import pallas as pl
from jax.experimental.pallas import tpu as pltpu

SLOTS = 4


DIFFUSION = (0.06, 0.1, 0.12, 0.12, 0.12)
TIME_STEP = 0.5
COUPLING = 0.5
PHASE_CHANGE_COST = 0.5


def with_halo(block, sides, width):
    for axis, dim in sides:
        count = lax.axis_size(axis)
        forward = [(i, i + 1) for i in range(count - 1)]
        backward = [(target, source) for source, target in forward]
        low = lax.ppermute(
            lax.slice_in_dim(block, block.shape[dim] - width, None, axis=dim), axis, forward
        )
        high = lax.ppermute(lax.slice_in_dim(block, 0, width, axis=dim), axis, backward)
        block = jnp.concatenate([low, block, high], axis=dim)
    return block


def fold_ghosts(block, sides):
    for axis, dim in sides:
        count = lax.axis_size(axis)
        forward = [(i, i + 1) for i in range(count - 1)]
        backward = [(target, source) for source, target in forward]
        span = block.shape[dim]
        below = lax.ppermute(lax.slice_in_dim(block, span - 1, span, axis=dim), axis, forward)
        above = lax.ppermute(lax.slice_in_dim(block, 0, 1, axis=dim), axis, backward)
        inner = lax.slice_in_dim(block, 1, span - 1, axis=dim)
        low_pad = [(0, 0)] * block.ndim
        high_pad = [(0, 0)] * block.ndim
        low_pad[dim] = (0, span - 3)
        high_pad[dim] = (span - 3, 0)
        block = inner + jnp.pad(below, low_pad) + jnp.pad(above, high_pad)
    return block


def fold_and_widen(block, boxes, sides):
    for axis, dim in sides:
        count = lax.axis_size(axis)
        forward = [(i, i + 1) for i in range(count - 1)]
        backward = [(target, source) for source, target in forward]
        span = block.shape[dim]
        width = boxes.shape[dim]
        fields = block.shape[0]
        lanes = block.shape[-1]
        layer = lax.index_in_dim(block, 0, dim, keepdims=True).shape
        face = lax.index_in_dim(boxes, 0, dim, keepdims=True).shape
        rows = 1
        for n in layer[1:-1]:
            rows *= n

        def payload(block_layer, box_face):
            return jnp.concatenate(
                [block_layer.reshape(fields, -1, lanes), box_face.reshape(fields, -1, lanes)],
                axis=1,
            )

        up = payload(
            lax.slice_in_dim(block, span - 1, span, axis=dim),
            lax.slice_in_dim(boxes, width - 1, width, axis=dim),
        )
        down = payload(lax.slice_in_dim(block, 0, 1, axis=dim), lax.slice_in_dim(boxes, 0, 1, axis=dim))
        below = lax.ppermute(up, axis, forward)
        above = lax.ppermute(down, axis, backward)
        inner = lax.slice_in_dim(block, 1, span - 1, axis=dim)
        low_pad = [(0, 0)] * block.ndim
        high_pad = [(0, 0)] * block.ndim
        low_pad[dim] = (0, span - 3)
        high_pad[dim] = (span - 3, 0)
        block = (
            inner
            + jnp.pad(below[:, :rows].reshape(layer), low_pad)
            + jnp.pad(above[:, :rows].reshape(layer), high_pad)
        )
        boxes = jnp.concatenate(
            [below[:, rows:].reshape(face), boxes, above[:, rows:].reshape(face)], axis=dim
        )
    return block, boxes


def parcel_update(current_condition, local_air_sample):
    particle_weights_list = current_condition[:, 0]
    parcel_hotness_measure = current_condition[:, 1]
    particle_speed_vector = current_condition[:, 2:5]
    relax_time = 0.4 * particle_weights_list ** (2.0 / 3.0)
    keep_velocity = jnp.exp(-TIME_STEP / relax_time)
    residual_heat_content = jnp.exp(-TIME_STEP / (1.5 * relax_time))
    equilibrium_steam_load = 0.4 * jnp.exp(2.0 * (parcel_hotness_measure - 1.0))
    evaporated_share = 1.0 - jnp.exp(
        -0.3 * jax.nn.softplus(4.0 * (equilibrium_steam_load - local_air_sample[:, 0]))
    )
    evaporated = particle_weights_list * evaporated_share
    ambient_heat_content = local_air_sample[:, 1]
    gas_velocity = local_air_sample[:, 2:5]
    adjusted_heat_content = (
        ambient_heat_content
        + (parcel_hotness_measure - ambient_heat_content) * residual_heat_content
        - PHASE_CHANGE_COST * evaporated_share
    )
    velocity_new = gas_velocity + (particle_speed_vector - gas_velocity) * keep_velocity[:, None]
    enthalpy_injection = (
        0.5 * particle_weights_list * (parcel_hotness_measure - adjusted_heat_content)
    )
    push_source = particle_weights_list[:, None] * (particle_speed_vector - velocity_new)
    updated = jnp.concatenate(
        [
            (particle_weights_list - evaporated)[:, None],
            adjusted_heat_content[:, None],
            velocity_new,
        ],
        axis=1,
    )
    sources = jnp.concatenate(
        [evaporated[:, None], enthalpy_injection[:, None], push_source], axis=1
    )
    return (updated, sources)


def laplacian(padded):
    centre = padded[:, 1:-1, 1:-1, 1:-1]
    beside = padded[:, 2:, 1:-1, 1:-1] + padded[:, :-2, 1:-1, 1:-1]
    beside = beside + padded[:, 1:-1, 2:, 1:-1] + padded[:, 1:-1, :-2, 1:-1]
    beside = beside + padded[:, 1:-1, 1:-1, 2:] + padded[:, 1:-1, 1:-1, :-2]
    return beside - 6.0 * centre


PAIR_LANES = 256
DEPTH_ROWS = 136


def split_bf16(value):
    high = value.astype(jnp.bfloat16)
    low = (value - high.astype(jnp.float32)).astype(jnp.bfloat16)
    return high, low


def three_pass(a, b, dims):
    a_high, a_low = split_bf16(a)
    b_high, b_low = split_bf16(b)
    out = None
    for x, y in ((a_high, b_high), (a_high, b_low), (a_low, b_high)):
        part = lax.dot_general(x, y, (dims, ((), ())), preferred_element_type=jnp.float32)
        out = part if out is None else out + part
    return out


GROUP = 8


def coupling_kernel(
    live_ref, dest_ref, table_ref, parcel_ref, cell_ref, offset_ref, factor_ref,
    kept_ref, outbox_ref, deposit_ref,
    weight_scr, depth_scr, spread_scr, updated_scr, count_scr, table_high_ref, table_low_ref,
    *, span_y, span_z,
):
    fields = parcel_ref.shape[0]
    blocks = parcel_ref.shape[1]
    lanes = parcel_ref.shape[2]
    plane_size = span_y * span_z
    deposit_ref[...] = jnp.zeros(deposit_ref.shape, jnp.float32)
    table_high, table_low = split_bf16(table_ref[...])
    table_high_ref[...] = table_high
    table_low_ref[...] = table_low
    live = live_ref[0]
    pair_iota = lax.broadcasted_iota(jnp.int32, (PAIR_LANES, lanes), 0)
    depth_iota = lax.broadcasted_iota(jnp.int32, (DEPTH_ROWS, lanes), 0)

    def group(g, carry):
        first = pl.multiple_of(g * GROUP, GROUP)
        cells = cell_ref[pl.ds(first, GROUP), :]
        offsets = offset_ref[:, pl.ds(first, GROUP), :]
        parcels = parcel_ref[:, pl.ds(first, GROUP), :]
        factors = factor_ref[:, pl.ds(first, GROUP), :]
        flat = cells.astype(jnp.float32) + 0.5
        cell_x = jnp.floor(flat * (1.0 / plane_size))
        rest = flat - cell_x * plane_size
        cell_y = jnp.floor(rest * (1.0 / span_z))
        cell_z = (rest - cell_y * span_z).astype(jnp.int32)
        cell_x = cell_x.astype(jnp.int32)
        cell_y = cell_y.astype(jnp.int32)
        step_sign = jnp.where(offsets >= 0.0, 1, -1).astype(jnp.int32)
        far_share = jnp.abs(offsets)
        near_share = 1.0 - far_share
        for j in range(GROUP):
            weights = jnp.zeros((PAIR_LANES, lanes), jnp.float32)
            for bit_x in range(2):
                for bit_y in range(2):
                    share = (far_share[0, j:j + 1] if bit_x else near_share[0, j:j + 1]) * (
                        far_share[1, j:j + 1] if bit_y else near_share[1, j:j + 1]
                    )
                    target = (
                        (cell_x[j:j + 1] + bit_x * step_sign[0, j:j + 1]) * span_y
                        + cell_y[j:j + 1]
                        + bit_y * step_sign[1, j:j + 1]
                    )
                    weights = weights + jnp.where(pair_iota == target, share, 0.0)
            weight_scr[:, j * lanes:(j + 1) * lanes] = weights
            depth_weights = jnp.where(
                depth_iota == cell_z[j:j + 1], near_share[2, j:j + 1], 0.0
            ) + jnp.where(
                depth_iota == cell_z[j:j + 1] + step_sign[2, j:j + 1], far_share[2, j:j + 1], 0.0
            )
            depth_scr[:, j * lanes:(j + 1) * lanes] = depth_weights
        weight_high, weight_low = split_bf16(weight_scr[...])
        table_high = table_high_ref[...]
        mixed = (
            jnp.dot(table_high, weight_high, preferred_element_type=jnp.float32)
            + jnp.dot(table_high, weight_low, preferred_element_type=jnp.float32)
            + jnp.dot(table_low_ref[...], weight_high, preferred_element_type=jnp.float32)
        )
        for j in range(GROUP):
            b = first + j
            depth_weights = depth_scr[:, j * lanes:(j + 1) * lanes]
            sample = [
                jnp.sum(
                    mixed[f * DEPTH_ROWS:(f + 1) * DEPTH_ROWS, j * lanes:(j + 1) * lanes]
                    * depth_weights,
                    axis=0,
                    keepdims=True,
                )
                for f in range(fields)
            ]
            mass = parcels[0, j:j + 1]
            heat = parcels[1, j:j + 1]
            keep_velocity = factors[0, j:j + 1]
            residual_heat = factors[1, j:j + 1]
            equilibrium = factors[2, j:j + 1]
            x = 4.0 * (equilibrium - sample[0])
            soft = jnp.maximum(x, 0.0) + jnp.log1p(jnp.exp(-jnp.abs(x)))
            share = 1.0 - jnp.exp(-0.3 * soft)
            evaporated = mass * share
            ambient = sample[1]
            adjusted = ambient + (heat - ambient) * residual_heat - PHASE_CHANGE_COST * share
            velocity = [
                sample[2 + d] + (parcels[2 + d, j:j + 1] - sample[2 + d]) * keep_velocity
                for d in range(3)
            ]
            enthalpy = 0.5 * mass * (heat - adjusted)
            push = [mass * (parcels[2 + d, j:j + 1] - velocity[d]) for d in range(3)]
            rows = [mass - evaporated, adjusted] + velocity
            for f in range(fields):
                updated_scr[f, pl.ds(b, 1), :] = rows[f]
            alive = b < live
            sources = [jnp.where(alive, s, 0.0) for s in [evaporated, enthalpy] + push]
            spread_scr[:, j * lanes:(j + 1) * lanes] = jnp.concatenate(
                [s * depth_weights for s in sources], axis=0
            )
        spread_high, spread_low = split_bf16(spread_scr[...])
        dims = (((1,), (1,)), ((), ()))
        deposit_ref[...] += (
            lax.dot_general(spread_high, weight_high, dims, preferred_element_type=jnp.float32)
            + lax.dot_general(spread_high, weight_low, dims, preferred_element_type=jnp.float32)
            + lax.dot_general(spread_low, weight_high, dims, preferred_element_type=jnp.float32)
        )
        return carry

    lax.fori_loop(0, blocks // GROUP, group, 0)

    kept_ref[...] = jnp.zeros(kept_ref.shape, jnp.float32)
    outbox_ref[...] = jnp.zeros(outbox_ref.shape, jnp.float32)
    for d in range(27):
        count_scr[d] = 0

    def route(b, carry):
        d = jnp.minimum(jnp.maximum(dest_ref[b], 0), 26)
        alive = b < live

        @pl.when(alive & (d == 13))
        def _():
            kept_ref[:, pl.ds(b, 1), :] = updated_scr[:, pl.ds(b, 1), :]

        rank = count_scr[d]

        @pl.when(alive & (d != 13) & (rank < SLOTS))
        def _():
            outbox_ref[:, pl.ds(d * SLOTS + rank, 1), :] = updated_scr[:, pl.ds(b, 1), :]
            count_scr[d] = rank + 1

        return carry

    lax.fori_loop(0, blocks, route, 0)


def local(gas_state, parcels, parcel_cells, offsets, destination, live_blocks):
    fields, size_x, size_y, size_z = gas_state.shape
    blocks, parcel_fields, block_parcels = parcels.shape
    padded = with_halo(gas_state, (("gx", 1), ("gy", 2), ("gz", 3)), 1)
    span_x = size_x + 2
    span_y = size_y + 2
    span_z = size_z + 2
    pair_count = span_x * span_y
    plane_size = span_y * span_z
    table = jnp.transpose(padded, (0, 3, 1, 2)).reshape(fields, span_z, pair_count)
    table = jnp.pad(table, ((0, 0), (0, DEPTH_ROWS - span_z), (0, PAIR_LANES - pair_count)))
    table = table.reshape(fields * DEPTH_ROWS, PAIR_LANES)
    parcel_rows = jnp.transpose(parcels, (1, 0, 2))
    offset_rows = jnp.transpose(offsets, (1, 0, 2))
    relax_time = 0.4 * parcel_rows[0] ** (2.0 / 3.0)
    factors = jnp.stack(
        [
            jnp.exp(-TIME_STEP / relax_time),
            jnp.exp(-TIME_STEP / (1.5 * relax_time)),
            0.4 * jnp.exp(2.0 * (parcel_rows[1] - 1.0)),
        ],
        axis=0,
    )
    vmem = pl.BlockSpec(memory_space=pltpu.VMEM)
    smem = pl.BlockSpec(memory_space=pltpu.SMEM)
    lanes = GROUP * block_parcels
    kept_rows, outbox_rows, deposit_rows = pl.pallas_call(
        functools.partial(coupling_kernel, span_y=span_y, span_z=span_z),
        out_shape=(
            jax.ShapeDtypeStruct(parcel_rows.shape, jnp.float32),
            jax.ShapeDtypeStruct((parcel_fields, 27 * SLOTS, block_parcels), jnp.float32),
            jax.ShapeDtypeStruct((fields * DEPTH_ROWS, PAIR_LANES), jnp.float32),
        ),
        in_specs=[smem, smem] + [vmem] * 5,
        out_specs=(vmem, vmem, vmem),
        scratch_shapes=[
            pltpu.VMEM((PAIR_LANES, lanes), jnp.float32),
            pltpu.VMEM((DEPTH_ROWS, lanes), jnp.float32),
            pltpu.VMEM((fields * DEPTH_ROWS, lanes), jnp.float32),
            pltpu.VMEM(parcel_rows.shape, jnp.float32),
            pltpu.SMEM((32,), jnp.int32),
            pltpu.VMEM(table.shape, jnp.bfloat16),
            pltpu.VMEM(table.shape, jnp.bfloat16),
        ],
    )(live_blocks, destination, table, parcel_rows, parcel_cells, offset_rows, factors)
    kept = jnp.transpose(kept_rows, (1, 0, 2))
    deposit = deposit_rows.reshape(fields, DEPTH_ROWS, PAIR_LANES)[:, :span_z, :pair_count]
    deposit = jnp.transpose(deposit.reshape(fields, span_z, span_x, span_y), (0, 2, 3, 1))
    boxes = jnp.pad(outbox_rows, ((0, 0), (0, 0), (0, span_z - block_parcels)))
    boxes = boxes.reshape((parcel_fields, 3, 3, 3, SLOTS, span_z))
    deposit, boxes = fold_and_widen(deposit, boxes, (("gx", 1), ("gy", 2)))
    cell_sources = fold_ghosts(deposit, (("gz", 3),))
    kappa = jnp.array(DIFFUSION, jnp.float32)[:, None, None, None]
    gas_next = gas_state + kappa * laplacian(padded) + COUPLING * cell_sources
    widened = with_halo(boxes, (("gz", 3),), 1)
    arrived_boxes = widened[:, 0::2, 0::2, 0::2, :, :block_parcels]
    arrived = jnp.transpose(
        arrived_boxes.reshape((parcel_fields, 27 * SLOTS, block_parcels)), (1, 0, 2)
    )
    return (gas_next, kept, arrived)


def solution(mesh):
    placed = (
        P(None, "gx", "gy", "gz"),
        P(("gx", "gy", "gz"), None, None),
        P(("gx", "gy", "gz"), None),
        P(("gx", "gy", "gz"), None, None),
        P(("gx", "gy", "gz")),
        P(("gx", "gy", "gz")),
    )
    return jax.shard_map(
        local,
        mesh=mesh,
        in_specs=placed,
        out_specs=(
            P(None, "gx", "gy", "gz"),
            P(("gx", "gy", "gz"), None, None),
            P(("gx", "gy", "gz"), None, None),
        ),
        check_vma=False,
    )
```

```python
import functools

import jax
import jax.numpy as jnp
from jax import lax
from jax.sharding import PartitionSpec as P
from jax.experimental import pallas as pl
from jax.experimental.pallas import tpu as pltpu

SLOTS = 4


DIFFUSION = (0.06, 0.1, 0.12, 0.12, 0.12)
TIME_STEP = 0.5
COUPLING = 0.5
PHASE_CHANGE_COST = 0.5


def with_halo(block, sides, width):
    for axis, dim in sides:
        count = lax.axis_size(axis)
        forward = [(i, i + 1) for i in range(count - 1)]
        backward = [(target, source) for source, target in forward]
        low = lax.ppermute(
            lax.slice_in_dim(block, block.shape[dim] - width, None, axis=dim), axis, forward
        )
        high = lax.ppermute(lax.slice_in_dim(block, 0, width, axis=dim), axis, backward)
        block = jnp.concatenate([low, block, high], axis=dim)
    return block


def fold_ghosts(block, sides):
    for axis, dim in sides:
        count = lax.axis_size(axis)
        forward = [(i, i + 1) for i in range(count - 1)]
        backward = [(target, source) for source, target in forward]
        span = block.shape[dim]
        below = lax.ppermute(lax.slice_in_dim(block, span - 1, span, axis=dim), axis, forward)
        above = lax.ppermute(lax.slice_in_dim(block, 0, 1, axis=dim), axis, backward)
        inner = lax.slice_in_dim(block, 1, span - 1, axis=dim)
        low_pad = [(0, 0)] * block.ndim
        high_pad = [(0, 0)] * block.ndim
        low_pad[dim] = (0, span - 3)
        high_pad[dim] = (span - 3, 0)
        block = inner + jnp.pad(below, low_pad) + jnp.pad(above, high_pad)
    return block


def parcel_update(current_condition, local_air_sample):
    particle_weights_list = current_condition[:, 0]
    parcel_hotness_measure = current_condition[:, 1]
    particle_speed_vector = current_condition[:, 2:5]
    relax_time = 0.4 * particle_weights_list ** (2.0 / 3.0)
    keep_velocity = jnp.exp(-TIME_STEP / relax_time)
    residual_heat_content = jnp.exp(-TIME_STEP / (1.5 * relax_time))
    equilibrium_steam_load = 0.4 * jnp.exp(2.0 * (parcel_hotness_measure - 1.0))
    evaporated_share = 1.0 - jnp.exp(
        -0.3 * jax.nn.softplus(4.0 * (equilibrium_steam_load - local_air_sample[:, 0]))
    )
    evaporated = particle_weights_list * evaporated_share
    ambient_heat_content = local_air_sample[:, 1]
    gas_velocity = local_air_sample[:, 2:5]
    adjusted_heat_content = (
        ambient_heat_content
        + (parcel_hotness_measure - ambient_heat_content) * residual_heat_content
        - PHASE_CHANGE_COST * evaporated_share
    )
    velocity_new = gas_velocity + (particle_speed_vector - gas_velocity) * keep_velocity[:, None]
    enthalpy_injection = (
        0.5 * particle_weights_list * (parcel_hotness_measure - adjusted_heat_content)
    )
    push_source = particle_weights_list[:, None] * (particle_speed_vector - velocity_new)
    updated = jnp.concatenate(
        [
            (particle_weights_list - evaporated)[:, None],
            adjusted_heat_content[:, None],
            velocity_new,
        ],
        axis=1,
    )
    sources = jnp.concatenate(
        [evaporated[:, None], enthalpy_injection[:, None], push_source], axis=1
    )
    return (updated, sources)


def laplacian(padded):
    centre = padded[:, 1:-1, 1:-1, 1:-1]
    beside = padded[:, 2:, 1:-1, 1:-1] + padded[:, :-2, 1:-1, 1:-1]
    beside = beside + padded[:, 1:-1, 2:, 1:-1] + padded[:, 1:-1, :-2, 1:-1]
    beside = beside + padded[:, 1:-1, 1:-1, 2:] + padded[:, 1:-1, 1:-1, :-2]
    return beside - 6.0 * centre


PAIR_LANES = 256
DEPTH_ROWS = 136


def split_bf16(value):
    high = value.astype(jnp.bfloat16)
    low = (value - high.astype(jnp.float32)).astype(jnp.bfloat16)
    return high, low


def three_pass(a, b, dims):
    a_high, a_low = split_bf16(a)
    b_high, b_low = split_bf16(b)
    out = None
    for x, y in ((a_high, b_high), (a_high, b_low), (a_low, b_high)):
        part = lax.dot_general(x, y, (dims, ((), ())), preferred_element_type=jnp.float32)
        out = part if out is None else out + part
    return out


GROUP = 8


def coupling_kernel(
    live_ref, dest_ref, table_ref, parcel_ref, cell_ref, offset_ref, factor_ref,
    kept_ref, outbox_ref, deposit_ref,
    weight_scr, depth_scr, spread_scr, updated_scr, count_scr, table_high_ref, table_low_ref,
    total_scr, *, span_y, span_z,
):
    fields = parcel_ref.shape[0]
    blocks = parcel_ref.shape[1]
    lanes = parcel_ref.shape[2]
    plane_size = span_y * span_z
    total_scr[...] = jnp.zeros(total_scr.shape, jnp.float32)
    table_high, table_low = split_bf16(table_ref[...])
    table_high_ref[...] = table_high
    table_low_ref[...] = table_low
    live = live_ref[0]
    pair_iota = lax.broadcasted_iota(jnp.int32, (PAIR_LANES, lanes), 0)
    depth_iota = lax.broadcasted_iota(jnp.int32, (DEPTH_ROWS, lanes), 0)

    def group(g, carry):
        first = pl.multiple_of(g * GROUP, GROUP)
        cells = cell_ref[pl.ds(first, GROUP), :]
        offsets = offset_ref[:, pl.ds(first, GROUP), :]
        parcels = parcel_ref[:, pl.ds(first, GROUP), :]
        factors = factor_ref[:, pl.ds(first, GROUP), :]
        flat = cells.astype(jnp.float32) + 0.5
        cell_x = jnp.floor(flat * (1.0 / plane_size))
        rest = flat - cell_x * plane_size
        cell_y = jnp.floor(rest * (1.0 / span_z))
        cell_z = (rest - cell_y * span_z).astype(jnp.int32)
        cell_x = cell_x.astype(jnp.int32)
        cell_y = cell_y.astype(jnp.int32)
        step_sign = jnp.where(offsets >= 0.0, 1, -1).astype(jnp.int32)
        far_share = jnp.abs(offsets)
        near_share = 1.0 - far_share
        for j in range(GROUP):
            weights = jnp.zeros((PAIR_LANES, lanes), jnp.float32)
            for bit_x in range(2):
                for bit_y in range(2):
                    share = (far_share[0, j:j + 1] if bit_x else near_share[0, j:j + 1]) * (
                        far_share[1, j:j + 1] if bit_y else near_share[1, j:j + 1]
                    )
                    target = (
                        (cell_x[j:j + 1] + bit_x * step_sign[0, j:j + 1]) * span_y
                        + cell_y[j:j + 1]
                        + bit_y * step_sign[1, j:j + 1]
                    )
                    weights = weights + jnp.where(pair_iota == target, share, 0.0)
            weight_scr[:, j * lanes:(j + 1) * lanes] = weights
            depth_weights = jnp.where(
                depth_iota == cell_z[j:j + 1], near_share[2, j:j + 1], 0.0
            ) + jnp.where(
                depth_iota == cell_z[j:j + 1] + step_sign[2, j:j + 1], far_share[2, j:j + 1], 0.0
            )
            depth_scr[:, j * lanes:(j + 1) * lanes] = depth_weights
        weight_high, weight_low = split_bf16(weight_scr[...])
        table_high = table_high_ref[...]
        mixed = (
            jnp.dot(table_high, weight_high, preferred_element_type=jnp.float32)
            + jnp.dot(table_high, weight_low, preferred_element_type=jnp.float32)
            + jnp.dot(table_low_ref[...], weight_high, preferred_element_type=jnp.float32)
        )
        for j in range(GROUP):
            b = first + j
            depth_weights = depth_scr[:, j * lanes:(j + 1) * lanes]
            sample = [
                jnp.sum(
                    mixed[f * DEPTH_ROWS:(f + 1) * DEPTH_ROWS, j * lanes:(j + 1) * lanes]
                    * depth_weights,
                    axis=0,
                    keepdims=True,
                )
                for f in range(fields)
            ]
            mass = parcels[0, j:j + 1]
            heat = parcels[1, j:j + 1]
            keep_velocity = factors[0, j:j + 1]
            residual_heat = factors[1, j:j + 1]
            equilibrium = factors[2, j:j + 1]
            x = 4.0 * (equilibrium - sample[0])
            soft = jnp.maximum(x, 0.0) + jnp.log1p(jnp.exp(-jnp.abs(x)))
            share = 1.0 - jnp.exp(-0.3 * soft)
            evaporated = mass * share
            ambient = sample[1]
            adjusted = ambient + (heat - ambient) * residual_heat - PHASE_CHANGE_COST * share
            velocity = [
                sample[2 + d] + (parcels[2 + d, j:j + 1] - sample[2 + d]) * keep_velocity
                for d in range(3)
            ]
            enthalpy = 0.5 * mass * (heat - adjusted)
            push = [mass * (parcels[2 + d, j:j + 1] - velocity[d]) for d in range(3)]
            rows = [mass - evaporated, adjusted] + velocity
            for f in range(fields):
                updated_scr[f, pl.ds(b, 1), :] = rows[f]
            alive = b < live
            sources = [jnp.where(alive, s, 0.0) for s in [evaporated, enthalpy] + push]
            spread_scr[:, j * lanes:(j + 1) * lanes] = jnp.concatenate(
                [s * depth_weights for s in sources], axis=0
            )
        spread_high, spread_low = split_bf16(spread_scr[...])
        dims = (((1,), (1,)), ((), ()))
        total_scr[...] += (
            lax.dot_general(weight_high, spread_high, dims, preferred_element_type=jnp.float32)
            + lax.dot_general(weight_low, spread_high, dims, preferred_element_type=jnp.float32)
            + lax.dot_general(weight_high, spread_low, dims, preferred_element_type=jnp.float32)
        )
        return carry

    lax.fori_loop(0, blocks // GROUP, group, 0)
    deposit_ref[...] = total_scr[...].T

    kept_ref[...] = jnp.zeros(kept_ref.shape, jnp.float32)
    outbox_ref[...] = jnp.zeros(outbox_ref.shape, jnp.float32)
    for d in range(27):
        count_scr[d] = 0

    def route(b, carry):
        d = jnp.minimum(jnp.maximum(dest_ref[b], 0), 26)
        alive = b < live

        @pl.when(alive & (d == 13))
        def _():
            kept_ref[:, pl.ds(b, 1), :] = updated_scr[:, pl.ds(b, 1), :]

        rank = count_scr[d]

        @pl.when(alive & (d != 13) & (rank < SLOTS))
        def _():
            outbox_ref[:, pl.ds(d * SLOTS + rank, 1), :] = updated_scr[:, pl.ds(b, 1), :]
            count_scr[d] = rank + 1

        return carry

    lax.fori_loop(0, blocks, route, 0)


def local(gas_state, parcels, parcel_cells, offsets, destination, live_blocks):
    fields, size_x, size_y, size_z = gas_state.shape
    blocks, parcel_fields, block_parcels = parcels.shape
    padded = with_halo(gas_state, (("gx", 1), ("gy", 2), ("gz", 3)), 1)
    span_x = size_x + 2
    span_y = size_y + 2
    span_z = size_z + 2
    pair_count = span_x * span_y
    plane_size = span_y * span_z
    table = jnp.transpose(padded, (0, 3, 1, 2)).reshape(fields, span_z, pair_count)
    table = jnp.pad(table, ((0, 0), (0, DEPTH_ROWS - span_z), (0, PAIR_LANES - pair_count)))
    table = table.reshape(fields * DEPTH_ROWS, PAIR_LANES)
    parcel_rows = jnp.transpose(parcels, (1, 0, 2))
    offset_rows = jnp.transpose(offsets, (1, 0, 2))
    relax_time = 0.4 * parcel_rows[0] ** (2.0 / 3.0)
    factors = jnp.stack(
        [
            jnp.exp(-TIME_STEP / relax_time),
            jnp.exp(-TIME_STEP / (1.5 * relax_time)),
            0.4 * jnp.exp(2.0 * (parcel_rows[1] - 1.0)),
        ],
        axis=0,
    )
    vmem = pl.BlockSpec(memory_space=pltpu.VMEM)
    smem = pl.BlockSpec(memory_space=pltpu.SMEM)
    lanes = GROUP * block_parcels
    kept_rows, outbox_rows, deposit_rows = pl.pallas_call(
        functools.partial(coupling_kernel, span_y=span_y, span_z=span_z),
        out_shape=(
            jax.ShapeDtypeStruct(parcel_rows.shape, jnp.float32),
            jax.ShapeDtypeStruct((parcel_fields, 27 * SLOTS, block_parcels), jnp.float32),
            jax.ShapeDtypeStruct((fields * DEPTH_ROWS, PAIR_LANES), jnp.float32),
        ),
        in_specs=[smem, smem] + [vmem] * 5,
        out_specs=(vmem, vmem, vmem),
        scratch_shapes=[
            pltpu.VMEM((PAIR_LANES, lanes), jnp.float32),
            pltpu.VMEM((DEPTH_ROWS, lanes), jnp.float32),
            pltpu.VMEM((fields * DEPTH_ROWS, lanes), jnp.float32),
            pltpu.VMEM(parcel_rows.shape, jnp.float32),
            pltpu.SMEM((32,), jnp.int32),
            pltpu.VMEM(table.shape, jnp.bfloat16),
            pltpu.VMEM(table.shape, jnp.bfloat16),
            pltpu.VMEM((PAIR_LANES, fields * DEPTH_ROWS), jnp.float32),
        ],
    )(live_blocks, destination, table, parcel_rows, parcel_cells, offset_rows, factors)
    kept = jnp.transpose(kept_rows, (1, 0, 2))
    deposit = deposit_rows.reshape(fields, DEPTH_ROWS, PAIR_LANES)[:, :span_z, :pair_count]
    deposit = jnp.transpose(deposit.reshape(fields, span_z, span_x, span_y), (0, 2, 3, 1))
    cell_sources = fold_ghosts(deposit, (("gx", 1), ("gy", 2), ("gz", 3)))
    kappa = jnp.array(DIFFUSION, jnp.float32)[:, None, None, None]
    gas_next = gas_state + kappa * laplacian(padded) + COUPLING * cell_sources
    outbox = outbox_rows.reshape((parcel_fields, 3, 3, 3, SLOTS, block_parcels))
    widened = with_halo(outbox, (("gx", 1), ("gy", 2), ("gz", 3)), 1)
    arrived_boxes = widened[:, 0::2, 0::2, 0::2]
    arrived = jnp.transpose(
        arrived_boxes.reshape((parcel_fields, 27 * SLOTS, block_parcels)), (1, 0, 2)
    )
    return (gas_next, kept, arrived)


def solution(mesh):
    placed = (
        P(None, "gx", "gy", "gz"),
        P(("gx", "gy", "gz"), None, None),
        P(("gx", "gy", "gz"), None),
        P(("gx", "gy", "gz"), None, None),
        P(("gx", "gy", "gz")),
        P(("gx", "gy", "gz")),
    )
    return jax.shard_map(
        local,
        mesh=mesh,
        in_specs=placed,
        out_specs=(
            P(None, "gx", "gy", "gz"),
            P(("gx", "gy", "gz"), None, None),
            P(("gx", "gy", "gz"), None, None),
        ),
        check_vma=False,
    )
```

```python
import functools

import jax
import jax.numpy as jnp
from jax import lax
from jax.sharding import PartitionSpec as P
from jax.experimental import pallas as pl
from jax.experimental.pallas import tpu as pltpu

SLOTS = 4


DIFFUSION = (0.06, 0.1, 0.12, 0.12, 0.12)
TIME_STEP = 0.5
COUPLING = 0.5
PHASE_CHANGE_COST = 0.5


def with_halo(block, sides, width):
    for axis, dim in sides:
        count = lax.axis_size(axis)
        forward = [(i, i + 1) for i in range(count - 1)]
        backward = [(target, source) for source, target in forward]
        low = lax.ppermute(
            lax.slice_in_dim(block, block.shape[dim] - width, None, axis=dim), axis, forward
        )
        high = lax.ppermute(lax.slice_in_dim(block, 0, width, axis=dim), axis, backward)
        block = jnp.concatenate([low, block, high], axis=dim)
    return block


def fold_ghosts(block, sides):
    for axis, dim in sides:
        count = lax.axis_size(axis)
        forward = [(i, i + 1) for i in range(count - 1)]
        backward = [(target, source) for source, target in forward]
        span = block.shape[dim]
        below = lax.ppermute(lax.slice_in_dim(block, span - 1, span, axis=dim), axis, forward)
        above = lax.ppermute(lax.slice_in_dim(block, 0, 1, axis=dim), axis, backward)
        inner = lax.slice_in_dim(block, 1, span - 1, axis=dim)
        low_pad = [(0, 0)] * block.ndim
        high_pad = [(0, 0)] * block.ndim
        low_pad[dim] = (0, span - 3)
        high_pad[dim] = (span - 3, 0)
        block = inner + jnp.pad(below, low_pad) + jnp.pad(above, high_pad)
    return block


def parcel_update(current_condition, local_air_sample):
    particle_weights_list = current_condition[:, 0]
    parcel_hotness_measure = current_condition[:, 1]
    particle_speed_vector = current_condition[:, 2:5]
    relax_time = 0.4 * particle_weights_list ** (2.0 / 3.0)
    keep_velocity = jnp.exp(-TIME_STEP / relax_time)
    residual_heat_content = jnp.exp(-TIME_STEP / (1.5 * relax_time))
    equilibrium_steam_load = 0.4 * jnp.exp(2.0 * (parcel_hotness_measure - 1.0))
    evaporated_share = 1.0 - jnp.exp(
        -0.3 * jax.nn.softplus(4.0 * (equilibrium_steam_load - local_air_sample[:, 0]))
    )
    evaporated = particle_weights_list * evaporated_share
    ambient_heat_content = local_air_sample[:, 1]
    gas_velocity = local_air_sample[:, 2:5]
    adjusted_heat_content = (
        ambient_heat_content
        + (parcel_hotness_measure - ambient_heat_content) * residual_heat_content
        - PHASE_CHANGE_COST * evaporated_share
    )
    velocity_new = gas_velocity + (particle_speed_vector - gas_velocity) * keep_velocity[:, None]
    enthalpy_injection = (
        0.5 * particle_weights_list * (parcel_hotness_measure - adjusted_heat_content)
    )
    push_source = particle_weights_list[:, None] * (particle_speed_vector - velocity_new)
    updated = jnp.concatenate(
        [
            (particle_weights_list - evaporated)[:, None],
            adjusted_heat_content[:, None],
            velocity_new,
        ],
        axis=1,
    )
    sources = jnp.concatenate(
        [evaporated[:, None], enthalpy_injection[:, None], push_source], axis=1
    )
    return (updated, sources)


def laplacian(padded):
    centre = padded[:, 1:-1, 1:-1, 1:-1]
    beside = padded[:, 2:, 1:-1, 1:-1] + padded[:, :-2, 1:-1, 1:-1]
    beside = beside + padded[:, 1:-1, 2:, 1:-1] + padded[:, 1:-1, :-2, 1:-1]
    beside = beside + padded[:, 1:-1, 1:-1, 2:] + padded[:, 1:-1, 1:-1, :-2]
    return beside - 6.0 * centre


PAIR_LANES = 256
DEPTH_ROWS = 136


def split_bf16(value):
    high = value.astype(jnp.bfloat16)
    low = (value - high.astype(jnp.float32)).astype(jnp.bfloat16)
    return high, low


def three_pass(a, b, dims):
    a_high, a_low = split_bf16(a)
    b_high, b_low = split_bf16(b)
    out = None
    for x, y in ((a_high, b_high), (a_high, b_low), (a_low, b_high)):
        part = lax.dot_general(x, y, (dims, ((), ())), preferred_element_type=jnp.float32)
        out = part if out is None else out + part
    return out


GROUP = 8


def coupling_kernel(
    live_ref, dest_ref, table_ref, parcel_ref, cell_ref, offset_ref, factor_ref,
    kept_ref, outbox_ref, deposit_ref,
    weight_scr, depth_scr, spread_scr, updated_scr, count_scr, table_high_ref, table_low_ref,
    total_scr, stack_scr, weight_rows_scr, spread_rows_scr, *, span_y, span_z,
):
    fields = parcel_ref.shape[0]
    blocks = parcel_ref.shape[1]
    lanes = parcel_ref.shape[2]
    plane_size = span_y * span_z
    total_scr[...] = jnp.zeros(total_scr.shape, jnp.float32)
    table_high, table_low = split_bf16(table_ref[...])
    stack_scr[:, 0:PAIR_LANES] = table_high
    stack_scr[:, PAIR_LANES:2 * PAIR_LANES] = table_high
    stack_scr[:, 2 * PAIR_LANES:3 * PAIR_LANES] = table_low
    live = live_ref[0]
    pair_iota = lax.broadcasted_iota(jnp.int32, (PAIR_LANES, lanes), 0)
    depth_iota = lax.broadcasted_iota(jnp.int32, (DEPTH_ROWS, lanes), 0)

    def group(g, carry):
        first = pl.multiple_of(g * GROUP, GROUP)
        cells = cell_ref[pl.ds(first, GROUP), :]
        offsets = offset_ref[:, pl.ds(first, GROUP), :]
        parcels = parcel_ref[:, pl.ds(first, GROUP), :]
        factors = factor_ref[:, pl.ds(first, GROUP), :]
        flat = cells.astype(jnp.float32) + 0.5
        cell_x = jnp.floor(flat * (1.0 / plane_size))
        rest = flat - cell_x * plane_size
        cell_y = jnp.floor(rest * (1.0 / span_z))
        cell_z = (rest - cell_y * span_z).astype(jnp.int32)
        cell_x = cell_x.astype(jnp.int32)
        cell_y = cell_y.astype(jnp.int32)
        step_sign = jnp.where(offsets >= 0.0, 1, -1).astype(jnp.int32)
        far_share = jnp.abs(offsets)
        near_share = 1.0 - far_share
        for j in range(GROUP):
            weights = jnp.zeros((PAIR_LANES, lanes), jnp.float32)
            for bit_x in range(2):
                for bit_y in range(2):
                    share = (far_share[0, j:j + 1] if bit_x else near_share[0, j:j + 1]) * (
                        far_share[1, j:j + 1] if bit_y else near_share[1, j:j + 1]
                    )
                    target = (
                        (cell_x[j:j + 1] + bit_x * step_sign[0, j:j + 1]) * span_y
                        + cell_y[j:j + 1]
                        + bit_y * step_sign[1, j:j + 1]
                    )
                    weights = weights + jnp.where(pair_iota == target, share, 0.0)
            weight_scr[:, j * lanes:(j + 1) * lanes] = weights
            depth_weights = jnp.where(
                depth_iota == cell_z[j:j + 1], near_share[2, j:j + 1], 0.0
            ) + jnp.where(
                depth_iota == cell_z[j:j + 1] + step_sign[2, j:j + 1], far_share[2, j:j + 1], 0.0
            )
            depth_scr[:, j * lanes:(j + 1) * lanes] = depth_weights
        weight_high, weight_low = split_bf16(weight_scr[...])
        width = GROUP * lanes
        weight_rows_scr[0:PAIR_LANES, :] = weight_high
        weight_rows_scr[PAIR_LANES:2 * PAIR_LANES, :] = weight_low
        weight_rows_scr[2 * PAIR_LANES:3 * PAIR_LANES, :] = weight_high
        mixed = jnp.dot(stack_scr[...], weight_rows_scr[...], preferred_element_type=jnp.float32)
        for j in range(GROUP):
            b = first + j
            depth_weights = depth_scr[:, j * lanes:(j + 1) * lanes]
            sample = [
                jnp.sum(
                    mixed[f * DEPTH_ROWS:(f + 1) * DEPTH_ROWS, j * lanes:(j + 1) * lanes]
                    * depth_weights,
                    axis=0,
                    keepdims=True,
                )
                for f in range(fields)
            ]
            mass = parcels[0, j:j + 1]
            heat = parcels[1, j:j + 1]
            keep_velocity = factors[0, j:j + 1]
            residual_heat = factors[1, j:j + 1]
            equilibrium = factors[2, j:j + 1]
            x = 4.0 * (equilibrium - sample[0])
            soft = jnp.maximum(x, 0.0) + jnp.log1p(jnp.exp(-jnp.abs(x)))
            share = 1.0 - jnp.exp(-0.3 * soft)
            evaporated = mass * share
            ambient = sample[1]
            adjusted = ambient + (heat - ambient) * residual_heat - PHASE_CHANGE_COST * share
            velocity = [
                sample[2 + d] + (parcels[2 + d, j:j + 1] - sample[2 + d]) * keep_velocity
                for d in range(3)
            ]
            enthalpy = 0.5 * mass * (heat - adjusted)
            push = [mass * (parcels[2 + d, j:j + 1] - velocity[d]) for d in range(3)]
            rows = [mass - evaporated, adjusted] + velocity
            for f in range(fields):
                updated_scr[f, pl.ds(b, 1), :] = rows[f]
            alive = b < live
            sources = [jnp.where(alive, s, 0.0) for s in [evaporated, enthalpy] + push]
            spread_scr[:, j * lanes:(j + 1) * lanes] = jnp.concatenate(
                [s * depth_weights for s in sources], axis=0
            )
        spread_high, spread_low = split_bf16(spread_scr[...])
        spread_rows_scr[:, 0:width] = spread_high
        spread_rows_scr[:, width:2 * width] = spread_high
        spread_rows_scr[:, 2 * width:3 * width] = spread_low
        weight_cols = jnp.concatenate([weight_high, weight_low, weight_high], axis=1)
        dims = (((1,), (1,)), ((), ()))
        total_scr[...] += lax.dot_general(
            weight_cols, spread_rows_scr[...], dims, preferred_element_type=jnp.float32
        )
        return carry

    lax.fori_loop(0, blocks // GROUP, group, 0)
    deposit_ref[...] = total_scr[...].T

    kept_ref[...] = jnp.zeros(kept_ref.shape, jnp.float32)
    outbox_ref[...] = jnp.zeros(outbox_ref.shape, jnp.float32)
    for d in range(27):
        count_scr[d] = 0

    def route(b, carry):
        d = jnp.minimum(jnp.maximum(dest_ref[b], 0), 26)
        alive = b < live

        @pl.when(alive & (d == 13))
        def _():
            kept_ref[:, pl.ds(b, 1), :] = updated_scr[:, pl.ds(b, 1), :]

        rank = count_scr[d]

        @pl.when(alive & (d != 13) & (rank < SLOTS))
        def _():
            outbox_ref[:, pl.ds(d * SLOTS + rank, 1), :] = updated_scr[:, pl.ds(b, 1), :]
            count_scr[d] = rank + 1

        return carry

    lax.fori_loop(0, blocks, route, 0)


def local(gas_state, parcels, parcel_cells, offsets, destination, live_blocks):
    fields, size_x, size_y, size_z = gas_state.shape
    blocks, parcel_fields, block_parcels = parcels.shape
    padded = with_halo(gas_state, (("gx", 1), ("gy", 2), ("gz", 3)), 1)
    span_x = size_x + 2
    span_y = size_y + 2
    span_z = size_z + 2
    pair_count = span_x * span_y
    plane_size = span_y * span_z
    table = jnp.transpose(padded, (0, 3, 1, 2)).reshape(fields, span_z, pair_count)
    table = jnp.pad(table, ((0, 0), (0, DEPTH_ROWS - span_z), (0, PAIR_LANES - pair_count)))
    table = table.reshape(fields * DEPTH_ROWS, PAIR_LANES)
    parcel_rows = jnp.transpose(parcels, (1, 0, 2))
    offset_rows = jnp.transpose(offsets, (1, 0, 2))
    relax_time = 0.4 * parcel_rows[0] ** (2.0 / 3.0)
    factors = jnp.stack(
        [
            jnp.exp(-TIME_STEP / relax_time),
            jnp.exp(-TIME_STEP / (1.5 * relax_time)),
            0.4 * jnp.exp(2.0 * (parcel_rows[1] - 1.0)),
        ],
        axis=0,
    )
    vmem = pl.BlockSpec(memory_space=pltpu.VMEM)
    smem = pl.BlockSpec(memory_space=pltpu.SMEM)
    lanes = GROUP * block_parcels
    kept_rows, outbox_rows, deposit_rows = pl.pallas_call(
        functools.partial(coupling_kernel, span_y=span_y, span_z=span_z),
        out_shape=(
            jax.ShapeDtypeStruct(parcel_rows.shape, jnp.float32),
            jax.ShapeDtypeStruct((parcel_fields, 27 * SLOTS, block_parcels), jnp.float32),
            jax.ShapeDtypeStruct((fields * DEPTH_ROWS, PAIR_LANES), jnp.float32),
        ),
        in_specs=[smem, smem] + [vmem] * 5,
        out_specs=(vmem, vmem, vmem),
        scratch_shapes=[
            pltpu.VMEM((PAIR_LANES, lanes), jnp.float32),
            pltpu.VMEM((DEPTH_ROWS, lanes), jnp.float32),
            pltpu.VMEM((fields * DEPTH_ROWS, lanes), jnp.float32),
            pltpu.VMEM(parcel_rows.shape, jnp.float32),
            pltpu.SMEM((32,), jnp.int32),
            pltpu.VMEM(table.shape, jnp.bfloat16),
            pltpu.VMEM(table.shape, jnp.bfloat16),
            pltpu.VMEM((PAIR_LANES, fields * DEPTH_ROWS), jnp.float32),
            pltpu.VMEM((fields * DEPTH_ROWS, 3 * PAIR_LANES), jnp.bfloat16),
            pltpu.VMEM((3 * PAIR_LANES, lanes), jnp.bfloat16),
            pltpu.VMEM((fields * DEPTH_ROWS, 3 * lanes), jnp.bfloat16),
        ],
    )(live_blocks, destination, table, parcel_rows, parcel_cells, offset_rows, factors)
    kept = jnp.transpose(kept_rows, (1, 0, 2))
    deposit = deposit_rows.reshape(fields, DEPTH_ROWS, PAIR_LANES)[:, :span_z, :pair_count]
    deposit = jnp.transpose(deposit.reshape(fields, span_z, span_x, span_y), (0, 2, 3, 1))
    cell_sources = fold_ghosts(deposit, (("gx", 1), ("gy", 2), ("gz", 3)))
    kappa = jnp.array(DIFFUSION, jnp.float32)[:, None, None, None]
    gas_next = gas_state + kappa * laplacian(padded) + COUPLING * cell_sources
    outbox = outbox_rows.reshape((parcel_fields, 3, 3, 3, SLOTS, block_parcels))
    widened = with_halo(outbox, (("gx", 1), ("gy", 2), ("gz", 3)), 1)
    arrived_boxes = widened[:, 0::2, 0::2, 0::2]
    arrived = jnp.transpose(
        arrived_boxes.reshape((parcel_fields, 27 * SLOTS, block_parcels)), (1, 0, 2)
    )
    return (gas_next, kept, arrived)


def solution(mesh):
    placed = (
        P(None, "gx", "gy", "gz"),
        P(("gx", "gy", "gz"), None, None),
        P(("gx", "gy", "gz"), None),
        P(("gx", "gy", "gz"), None, None),
        P(("gx", "gy", "gz")),
        P(("gx", "gy", "gz")),
    )
    return jax.shard_map(
        local,
        mesh=mesh,
        in_specs=placed,
        out_specs=(
            P(None, "gx", "gy", "gz"),
            P(("gx", "gy", "gz"), None, None),
            P(("gx", "gy", "gz"), None, None),
        ),
        check_vma=False,
    )
```

```python
import functools

import jax
import jax.numpy as jnp
from jax import lax
from jax.sharding import PartitionSpec as P
from jax.experimental import pallas as pl
from jax.experimental.pallas import tpu as pltpu

SLOTS = 4


DIFFUSION = (0.06, 0.1, 0.12, 0.12, 0.12)
TIME_STEP = 0.5
COUPLING = 0.5
PHASE_CHANGE_COST = 0.5


def with_halo(block, sides, width):
    for axis, dim in sides:
        count = lax.axis_size(axis)
        forward = [(i, i + 1) for i in range(count - 1)]
        backward = [(target, source) for source, target in forward]
        low = lax.ppermute(
            lax.slice_in_dim(block, block.shape[dim] - width, None, axis=dim), axis, forward
        )
        high = lax.ppermute(lax.slice_in_dim(block, 0, width, axis=dim), axis, backward)
        block = jnp.concatenate([low, block, high], axis=dim)
    return block


def fold_ghosts(block, sides):
    for axis, dim in sides:
        count = lax.axis_size(axis)
        forward = [(i, i + 1) for i in range(count - 1)]
        backward = [(target, source) for source, target in forward]
        span = block.shape[dim]
        below = lax.ppermute(lax.slice_in_dim(block, span - 1, span, axis=dim), axis, forward)
        above = lax.ppermute(lax.slice_in_dim(block, 0, 1, axis=dim), axis, backward)
        inner = lax.slice_in_dim(block, 1, span - 1, axis=dim)
        low_pad = [(0, 0)] * block.ndim
        high_pad = [(0, 0)] * block.ndim
        low_pad[dim] = (0, span - 3)
        high_pad[dim] = (span - 3, 0)
        block = inner + jnp.pad(below, low_pad) + jnp.pad(above, high_pad)
    return block


def parcel_update(current_condition, local_air_sample):
    particle_weights_list = current_condition[:, 0]
    parcel_hotness_measure = current_condition[:, 1]
    particle_speed_vector = current_condition[:, 2:5]
    relax_time = 0.4 * particle_weights_list ** (2.0 / 3.0)
    keep_velocity = jnp.exp(-TIME_STEP / relax_time)
    residual_heat_content = jnp.exp(-TIME_STEP / (1.5 * relax_time))
    equilibrium_steam_load = 0.4 * jnp.exp(2.0 * (parcel_hotness_measure - 1.0))
    evaporated_share = 1.0 - jnp.exp(
        -0.3 * jax.nn.softplus(4.0 * (equilibrium_steam_load - local_air_sample[:, 0]))
    )
    evaporated = particle_weights_list * evaporated_share
    ambient_heat_content = local_air_sample[:, 1]
    gas_velocity = local_air_sample[:, 2:5]
    adjusted_heat_content = (
        ambient_heat_content
        + (parcel_hotness_measure - ambient_heat_content) * residual_heat_content
        - PHASE_CHANGE_COST * evaporated_share
    )
    velocity_new = gas_velocity + (particle_speed_vector - gas_velocity) * keep_velocity[:, None]
    enthalpy_injection = (
        0.5 * particle_weights_list * (parcel_hotness_measure - adjusted_heat_content)
    )
    push_source = particle_weights_list[:, None] * (particle_speed_vector - velocity_new)
    updated = jnp.concatenate(
        [
            (particle_weights_list - evaporated)[:, None],
            adjusted_heat_content[:, None],
            velocity_new,
        ],
        axis=1,
    )
    sources = jnp.concatenate(
        [evaporated[:, None], enthalpy_injection[:, None], push_source], axis=1
    )
    return (updated, sources)


def laplacian(padded):
    centre = padded[:, 1:-1, 1:-1, 1:-1]
    beside = padded[:, 2:, 1:-1, 1:-1] + padded[:, :-2, 1:-1, 1:-1]
    beside = beside + padded[:, 1:-1, 2:, 1:-1] + padded[:, 1:-1, :-2, 1:-1]
    beside = beside + padded[:, 1:-1, 1:-1, 2:] + padded[:, 1:-1, 1:-1, :-2]
    return beside - 6.0 * centre


PAIR_LANES = 256
PAIR_ROWS = 192
DEPTH_ROWS = 136


def split_bf16(value):
    high = value.astype(jnp.bfloat16)
    low = (value - high.astype(jnp.float32)).astype(jnp.bfloat16)
    return high, low


def three_pass(a, b, dims):
    a_high, a_low = split_bf16(a)
    b_high, b_low = split_bf16(b)
    out = None
    for x, y in ((a_high, b_high), (a_high, b_low), (a_low, b_high)):
        part = lax.dot_general(x, y, (dims, ((), ())), preferred_element_type=jnp.float32)
        out = part if out is None else out + part
    return out


GROUP = 8


def coupling_kernel(
    live_ref, dest_ref, table_ref, parcel_ref, cell_ref, offset_ref, factor_ref,
    kept_ref, outbox_ref, deposit_ref,
    weight_scr, depth_scr, spread_scr, updated_scr, count_scr, table_high_ref, table_low_ref,
    total_scr, stack_scr, weight_rows_scr, spread_rows_scr, *, span_y, span_z,
):
    fields = parcel_ref.shape[0]
    blocks = parcel_ref.shape[1]
    lanes = parcel_ref.shape[2]
    plane_size = span_y * span_z
    total_scr[...] = jnp.zeros(total_scr.shape, jnp.float32)
    table_high, table_low = split_bf16(table_ref[...])
    stack_scr[:, 0:PAIR_LANES] = table_high
    stack_scr[:, PAIR_LANES:2 * PAIR_LANES] = table_high
    stack_scr[:, 2 * PAIR_LANES:3 * PAIR_LANES] = table_low
    live = live_ref[0]
    pair_iota = lax.broadcasted_iota(jnp.int32, (PAIR_ROWS, lanes), 0)
    weight_rows_scr[...] = jnp.zeros(weight_rows_scr.shape, jnp.bfloat16)
    depth_iota = lax.broadcasted_iota(jnp.int32, (DEPTH_ROWS, lanes), 0)

    def group(g, carry):
        first = pl.multiple_of(g * GROUP, GROUP)
        cells = cell_ref[pl.ds(first, GROUP), :]
        offsets = offset_ref[:, pl.ds(first, GROUP), :]
        parcels = parcel_ref[:, pl.ds(first, GROUP), :]
        factors = factor_ref[:, pl.ds(first, GROUP), :]
        flat = cells.astype(jnp.float32) + 0.5
        cell_x = jnp.floor(flat * (1.0 / plane_size))
        rest = flat - cell_x * plane_size
        cell_y = jnp.floor(rest * (1.0 / span_z))
        cell_z = (rest - cell_y * span_z).astype(jnp.int32)
        cell_x = cell_x.astype(jnp.int32)
        cell_y = cell_y.astype(jnp.int32)
        step_sign = jnp.where(offsets >= 0.0, 1, -1).astype(jnp.int32)
        far_share = jnp.abs(offsets)
        near_share = 1.0 - far_share
        for j in range(GROUP):
            weights = jnp.zeros((PAIR_ROWS, lanes), jnp.float32)
            for bit_x in range(2):
                for bit_y in range(2):
                    share = (far_share[0, j:j + 1] if bit_x else near_share[0, j:j + 1]) * (
                        far_share[1, j:j + 1] if bit_y else near_share[1, j:j + 1]
                    )
                    target = (
                        (cell_x[j:j + 1] + bit_x * step_sign[0, j:j + 1]) * span_y
                        + cell_y[j:j + 1]
                        + bit_y * step_sign[1, j:j + 1]
                    )
                    weights = weights + jnp.where(pair_iota == target, share, 0.0)
            weight_scr[:, j * lanes:(j + 1) * lanes] = weights
            depth_weights = jnp.where(
                depth_iota == cell_z[j:j + 1], near_share[2, j:j + 1], 0.0
            ) + jnp.where(
                depth_iota == cell_z[j:j + 1] + step_sign[2, j:j + 1], far_share[2, j:j + 1], 0.0
            )
            depth_scr[:, j * lanes:(j + 1) * lanes] = depth_weights
        weight_high, weight_low = split_bf16(weight_scr[...])
        width = GROUP * lanes
        weight_rows_scr[0:PAIR_ROWS, :] = weight_high
        weight_rows_scr[PAIR_LANES:PAIR_LANES + PAIR_ROWS, :] = weight_low
        weight_rows_scr[2 * PAIR_LANES:2 * PAIR_LANES + PAIR_ROWS, :] = weight_high
        mixed = jnp.dot(stack_scr[...], weight_rows_scr[...], preferred_element_type=jnp.float32)
        for j in range(GROUP):
            b = first + j
            depth_weights = depth_scr[:, j * lanes:(j + 1) * lanes]
            sample = [
                jnp.sum(
                    mixed[f * DEPTH_ROWS:(f + 1) * DEPTH_ROWS, j * lanes:(j + 1) * lanes]
                    * depth_weights,
                    axis=0,
                    keepdims=True,
                )
                for f in range(fields)
            ]
            mass = parcels[0, j:j + 1]
            heat = parcels[1, j:j + 1]
            keep_velocity = factors[0, j:j + 1]
            residual_heat = factors[1, j:j + 1]
            equilibrium = factors[2, j:j + 1]
            x = 4.0 * (equilibrium - sample[0])
            soft = jnp.maximum(x, 0.0) + jnp.log1p(jnp.exp(-jnp.abs(x)))
            share = 1.0 - jnp.exp(-0.3 * soft)
            evaporated = mass * share
            ambient = sample[1]
            adjusted = ambient + (heat - ambient) * residual_heat - PHASE_CHANGE_COST * share
            velocity = [
                sample[2 + d] + (parcels[2 + d, j:j + 1] - sample[2 + d]) * keep_velocity
                for d in range(3)
            ]
            enthalpy = 0.5 * mass * (heat - adjusted)
            push = [mass * (parcels[2 + d, j:j + 1] - velocity[d]) for d in range(3)]
            rows = [mass - evaporated, adjusted] + velocity
            for f in range(fields):
                updated_scr[f, pl.ds(b, 1), :] = rows[f]
            alive = b < live
            sources = [jnp.where(alive, s, 0.0) for s in [evaporated, enthalpy] + push]
            spread_scr[:, j * lanes:(j + 1) * lanes] = jnp.concatenate(
                [s * depth_weights for s in sources], axis=0
            )
        spread_high, spread_low = split_bf16(spread_scr[...])
        spread_rows_scr[:, 0:width] = spread_high
        spread_rows_scr[:, width:2 * width] = spread_high
        spread_rows_scr[:, 2 * width:3 * width] = spread_low
        weight_cols = jnp.concatenate([weight_high, weight_low, weight_high], axis=1)
        dims = (((1,), (1,)), ((), ()))
        total_scr[...] += lax.dot_general(
            weight_cols, spread_rows_scr[...], dims, preferred_element_type=jnp.float32
        )
        return carry

    lax.fori_loop(0, blocks // GROUP, group, 0)
    deposit_ref[...] = jnp.zeros(deposit_ref.shape, jnp.float32)
    deposit_ref[:, 0:PAIR_ROWS] = total_scr[...].T

    kept_ref[...] = jnp.zeros(kept_ref.shape, jnp.float32)
    outbox_ref[...] = jnp.zeros(outbox_ref.shape, jnp.float32)
    for d in range(27):
        count_scr[d] = 0

    def route(b, carry):
        d = jnp.minimum(jnp.maximum(dest_ref[b], 0), 26)
        alive = b < live

        @pl.when(alive & (d == 13))
        def _():
            kept_ref[:, pl.ds(b, 1), :] = updated_scr[:, pl.ds(b, 1), :]

        rank = count_scr[d]

        @pl.when(alive & (d != 13) & (rank < SLOTS))
        def _():
            outbox_ref[:, pl.ds(d * SLOTS + rank, 1), :] = updated_scr[:, pl.ds(b, 1), :]
            count_scr[d] = rank + 1

        return carry

    lax.fori_loop(0, blocks, route, 0)


def local(gas_state, parcels, parcel_cells, offsets, destination, live_blocks):
    fields, size_x, size_y, size_z = gas_state.shape
    blocks, parcel_fields, block_parcels = parcels.shape
    padded = with_halo(gas_state, (("gx", 1), ("gy", 2), ("gz", 3)), 1)
    span_x = size_x + 2
    span_y = size_y + 2
    span_z = size_z + 2
    pair_count = span_x * span_y
    assert pair_count <= PAIR_ROWS and span_z <= DEPTH_ROWS
    plane_size = span_y * span_z
    table = jnp.transpose(padded, (0, 3, 1, 2)).reshape(fields, span_z, pair_count)
    table = jnp.pad(table, ((0, 0), (0, DEPTH_ROWS - span_z), (0, PAIR_LANES - pair_count)))
    table = table.reshape(fields * DEPTH_ROWS, PAIR_LANES)
    parcel_rows = jnp.transpose(parcels, (1, 0, 2))
    offset_rows = jnp.transpose(offsets, (1, 0, 2))
    relax_time = 0.4 * parcel_rows[0] ** (2.0 / 3.0)
    factors = jnp.stack(
        [
            jnp.exp(-TIME_STEP / relax_time),
            jnp.exp(-TIME_STEP / (1.5 * relax_time)),
            0.4 * jnp.exp(2.0 * (parcel_rows[1] - 1.0)),
        ],
        axis=0,
    )
    vmem = pl.BlockSpec(memory_space=pltpu.VMEM)
    smem = pl.BlockSpec(memory_space=pltpu.SMEM)
    lanes = GROUP * block_parcels
    kept_rows, outbox_rows, deposit_rows = pl.pallas_call(
        functools.partial(coupling_kernel, span_y=span_y, span_z=span_z),
        out_shape=(
            jax.ShapeDtypeStruct(parcel_rows.shape, jnp.float32),
            jax.ShapeDtypeStruct((parcel_fields, 27 * SLOTS, block_parcels), jnp.float32),
            jax.ShapeDtypeStruct((fields * DEPTH_ROWS, PAIR_LANES), jnp.float32),
        ),
        in_specs=[smem, smem] + [vmem] * 5,
        out_specs=(vmem, vmem, vmem),
        scratch_shapes=[
            pltpu.VMEM((PAIR_ROWS, lanes), jnp.float32),
            pltpu.VMEM((DEPTH_ROWS, lanes), jnp.float32),
            pltpu.VMEM((fields * DEPTH_ROWS, lanes), jnp.float32),
            pltpu.VMEM(parcel_rows.shape, jnp.float32),
            pltpu.SMEM((32,), jnp.int32),
            pltpu.VMEM(table.shape, jnp.bfloat16),
            pltpu.VMEM(table.shape, jnp.bfloat16),
            pltpu.VMEM((PAIR_ROWS, fields * DEPTH_ROWS), jnp.float32),
            pltpu.VMEM((fields * DEPTH_ROWS, 3 * PAIR_LANES), jnp.bfloat16),
            pltpu.VMEM((3 * PAIR_LANES, lanes), jnp.bfloat16),
            pltpu.VMEM((fields * DEPTH_ROWS, 3 * lanes), jnp.bfloat16),
        ],
    )(live_blocks, destination, table, parcel_rows, parcel_cells, offset_rows, factors)
    kept = jnp.transpose(kept_rows, (1, 0, 2))
    deposit = deposit_rows.reshape(fields, DEPTH_ROWS, PAIR_LANES)[:, :span_z, :pair_count]
    deposit = jnp.transpose(deposit.reshape(fields, span_z, span_x, span_y), (0, 2, 3, 1))
    cell_sources = fold_ghosts(deposit, (("gx", 1), ("gy", 2), ("gz", 3)))
    kappa = jnp.array(DIFFUSION, jnp.float32)[:, None, None, None]
    gas_next = gas_state + kappa * laplacian(padded) + COUPLING * cell_sources
    outbox = outbox_rows.reshape((parcel_fields, 3, 3, 3, SLOTS, block_parcels))
    widened = with_halo(outbox, (("gx", 1), ("gy", 2), ("gz", 3)), 1)
    arrived_boxes = widened[:, 0::2, 0::2, 0::2]
    arrived = jnp.transpose(
        arrived_boxes.reshape((parcel_fields, 27 * SLOTS, block_parcels)), (1, 0, 2)
    )
    return (gas_next, kept, arrived)


def solution(mesh):
    placed = (
        P(None, "gx", "gy", "gz"),
        P(("gx", "gy", "gz"), None, None),
        P(("gx", "gy", "gz"), None),
        P(("gx", "gy", "gz"), None, None),
        P(("gx", "gy", "gz")),
        P(("gx", "gy", "gz")),
    )
    return jax.shard_map(
        local,
        mesh=mesh,
        in_specs=placed,
        out_specs=(
            P(None, "gx", "gy", "gz"),
            P(("gx", "gy", "gz"), None, None),
            P(("gx", "gy", "gz"), None, None),
        ),
        check_vma=False,
    )
```

```python
import functools

import jax
import jax.numpy as jnp
from jax import lax
from jax.sharding import PartitionSpec as P
from jax.experimental import pallas as pl
from jax.experimental.pallas import tpu as pltpu

SLOTS = 4


DIFFUSION = (0.06, 0.1, 0.12, 0.12, 0.12)
TIME_STEP = 0.5
COUPLING = 0.5
PHASE_CHANGE_COST = 0.5


def with_halo(block, sides, width):
    for axis, dim in sides:
        count = lax.axis_size(axis)
        forward = [(i, i + 1) for i in range(count - 1)]
        backward = [(target, source) for source, target in forward]
        low = lax.ppermute(
            lax.slice_in_dim(block, block.shape[dim] - width, None, axis=dim), axis, forward
        )
        high = lax.ppermute(lax.slice_in_dim(block, 0, width, axis=dim), axis, backward)
        block = jnp.concatenate([low, block, high], axis=dim)
    return block


def fold_ghosts(block, sides):
    for axis, dim in sides:
        count = lax.axis_size(axis)
        forward = [(i, i + 1) for i in range(count - 1)]
        backward = [(target, source) for source, target in forward]
        span = block.shape[dim]
        below = lax.ppermute(lax.slice_in_dim(block, span - 1, span, axis=dim), axis, forward)
        above = lax.ppermute(lax.slice_in_dim(block, 0, 1, axis=dim), axis, backward)
        inner = lax.slice_in_dim(block, 1, span - 1, axis=dim)
        low_pad = [(0, 0)] * block.ndim
        high_pad = [(0, 0)] * block.ndim
        low_pad[dim] = (0, span - 3)
        high_pad[dim] = (span - 3, 0)
        block = inner + jnp.pad(below, low_pad) + jnp.pad(above, high_pad)
    return block


def parcel_update(current_condition, local_air_sample):
    particle_weights_list = current_condition[:, 0]
    parcel_hotness_measure = current_condition[:, 1]
    particle_speed_vector = current_condition[:, 2:5]
    relax_time = 0.4 * particle_weights_list ** (2.0 / 3.0)
    keep_velocity = jnp.exp(-TIME_STEP / relax_time)
    residual_heat_content = jnp.exp(-TIME_STEP / (1.5 * relax_time))
    equilibrium_steam_load = 0.4 * jnp.exp(2.0 * (parcel_hotness_measure - 1.0))
    evaporated_share = 1.0 - jnp.exp(
        -0.3 * jax.nn.softplus(4.0 * (equilibrium_steam_load - local_air_sample[:, 0]))
    )
    evaporated = particle_weights_list * evaporated_share
    ambient_heat_content = local_air_sample[:, 1]
    gas_velocity = local_air_sample[:, 2:5]
    adjusted_heat_content = (
        ambient_heat_content
        + (parcel_hotness_measure - ambient_heat_content) * residual_heat_content
        - PHASE_CHANGE_COST * evaporated_share
    )
    velocity_new = gas_velocity + (particle_speed_vector - gas_velocity) * keep_velocity[:, None]
    enthalpy_injection = (
        0.5 * particle_weights_list * (parcel_hotness_measure - adjusted_heat_content)
    )
    push_source = particle_weights_list[:, None] * (particle_speed_vector - velocity_new)
    updated = jnp.concatenate(
        [
            (particle_weights_list - evaporated)[:, None],
            adjusted_heat_content[:, None],
            velocity_new,
        ],
        axis=1,
    )
    sources = jnp.concatenate(
        [evaporated[:, None], enthalpy_injection[:, None], push_source], axis=1
    )
    return (updated, sources)


def laplacian(padded):
    centre = padded[:, 1:-1, 1:-1, 1:-1]
    beside = padded[:, 2:, 1:-1, 1:-1] + padded[:, :-2, 1:-1, 1:-1]
    beside = beside + padded[:, 1:-1, 2:, 1:-1] + padded[:, 1:-1, :-2, 1:-1]
    beside = beside + padded[:, 1:-1, 1:-1, 2:] + padded[:, 1:-1, 1:-1, :-2]
    return beside - 6.0 * centre


PAIR_LANES = 256
PAIR_ROWS = 192
DEPTH_ROWS = 136


def split_bf16(value):
    high = value.astype(jnp.bfloat16)
    low = (value - high.astype(jnp.float32)).astype(jnp.bfloat16)
    return high, low


def three_pass(a, b, dims):
    a_high, a_low = split_bf16(a)
    b_high, b_low = split_bf16(b)
    out = None
    for x, y in ((a_high, b_high), (a_high, b_low), (a_low, b_high)):
        part = lax.dot_general(x, y, (dims, ((), ())), preferred_element_type=jnp.float32)
        out = part if out is None else out + part
    return out


GROUP = 16


def coupling_kernel(
    live_ref, dest_ref, table_ref, parcel_ref, cell_ref, offset_ref, factor_ref,
    kept_ref, outbox_ref, deposit_ref,
    weight_scr, depth_scr, spread_scr, updated_scr, count_scr, table_high_ref, table_low_ref,
    total_scr, stack_scr, weight_rows_scr, spread_rows_scr, *, span_y, span_z,
):
    fields = parcel_ref.shape[0]
    blocks = parcel_ref.shape[1]
    lanes = parcel_ref.shape[2]
    plane_size = span_y * span_z
    total_scr[...] = jnp.zeros(total_scr.shape, jnp.float32)
    table_high, table_low = split_bf16(table_ref[...])
    stack_scr[:, 0:PAIR_LANES] = table_high
    stack_scr[:, PAIR_LANES:2 * PAIR_LANES] = table_high
    stack_scr[:, 2 * PAIR_LANES:3 * PAIR_LANES] = table_low
    live = live_ref[0]
    pair_iota = lax.broadcasted_iota(jnp.int32, (PAIR_ROWS, lanes), 0)
    weight_rows_scr[...] = jnp.zeros(weight_rows_scr.shape, jnp.bfloat16)
    depth_iota = lax.broadcasted_iota(jnp.int32, (DEPTH_ROWS, lanes), 0)

    def group(g, carry):
        first = pl.multiple_of(g * GROUP, GROUP)
        cells = cell_ref[pl.ds(first, GROUP), :]
        offsets = offset_ref[:, pl.ds(first, GROUP), :]
        parcels = parcel_ref[:, pl.ds(first, GROUP), :]
        factors = factor_ref[:, pl.ds(first, GROUP), :]
        flat = cells.astype(jnp.float32) + 0.5
        cell_x = jnp.floor(flat * (1.0 / plane_size))
        rest = flat - cell_x * plane_size
        cell_y = jnp.floor(rest * (1.0 / span_z))
        cell_z = (rest - cell_y * span_z).astype(jnp.int32)
        cell_x = cell_x.astype(jnp.int32)
        cell_y = cell_y.astype(jnp.int32)
        step_sign = jnp.where(offsets >= 0.0, 1, -1).astype(jnp.int32)
        far_share = jnp.abs(offsets)
        near_share = 1.0 - far_share
        for j in range(GROUP):
            weights = jnp.zeros((PAIR_ROWS, lanes), jnp.float32)
            for bit_x in range(2):
                for bit_y in range(2):
                    share = (far_share[0, j:j + 1] if bit_x else near_share[0, j:j + 1]) * (
                        far_share[1, j:j + 1] if bit_y else near_share[1, j:j + 1]
                    )
                    target = (
                        (cell_x[j:j + 1] + bit_x * step_sign[0, j:j + 1]) * span_y
                        + cell_y[j:j + 1]
                        + bit_y * step_sign[1, j:j + 1]
                    )
                    weights = weights + jnp.where(pair_iota == target, share, 0.0)
            weight_scr[:, j * lanes:(j + 1) * lanes] = weights
            depth_weights = jnp.where(
                depth_iota == cell_z[j:j + 1], near_share[2, j:j + 1], 0.0
            ) + jnp.where(
                depth_iota == cell_z[j:j + 1] + step_sign[2, j:j + 1], far_share[2, j:j + 1], 0.0
            )
            depth_scr[:, j * lanes:(j + 1) * lanes] = depth_weights
        weight_high, weight_low = split_bf16(weight_scr[...])
        width = GROUP * lanes
        weight_rows_scr[0:PAIR_ROWS, :] = weight_high
        weight_rows_scr[PAIR_LANES:PAIR_LANES + PAIR_ROWS, :] = weight_low
        weight_rows_scr[2 * PAIR_LANES:2 * PAIR_LANES + PAIR_ROWS, :] = weight_high
        mixed = jnp.dot(stack_scr[...], weight_rows_scr[...], preferred_element_type=jnp.float32)
        for j in range(GROUP):
            b = first + j
            depth_weights = depth_scr[:, j * lanes:(j + 1) * lanes]
            sample = [
                jnp.sum(
                    mixed[f * DEPTH_ROWS:(f + 1) * DEPTH_ROWS, j * lanes:(j + 1) * lanes]
                    * depth_weights,
                    axis=0,
                    keepdims=True,
                )
                for f in range(fields)
            ]
            mass = parcels[0, j:j + 1]
            heat = parcels[1, j:j + 1]
            keep_velocity = factors[0, j:j + 1]
            residual_heat = factors[1, j:j + 1]
            equilibrium = factors[2, j:j + 1]
            x = 4.0 * (equilibrium - sample[0])
            soft = jnp.maximum(x, 0.0) + jnp.log1p(jnp.exp(-jnp.abs(x)))
            share = 1.0 - jnp.exp(-0.3 * soft)
            evaporated = mass * share
            ambient = sample[1]
            adjusted = ambient + (heat - ambient) * residual_heat - PHASE_CHANGE_COST * share
            velocity = [
                sample[2 + d] + (parcels[2 + d, j:j + 1] - sample[2 + d]) * keep_velocity
                for d in range(3)
            ]
            enthalpy = 0.5 * mass * (heat - adjusted)
            push = [mass * (parcels[2 + d, j:j + 1] - velocity[d]) for d in range(3)]
            rows = [mass - evaporated, adjusted] + velocity
            for f in range(fields):
                updated_scr[f, pl.ds(b, 1), :] = rows[f]
            alive = b < live
            sources = [jnp.where(alive, s, 0.0) for s in [evaporated, enthalpy] + push]
            spread_scr[:, j * lanes:(j + 1) * lanes] = jnp.concatenate(
                [s * depth_weights for s in sources], axis=0
            )
        spread_high, spread_low = split_bf16(spread_scr[...])
        spread_rows_scr[:, 0:width] = spread_high
        spread_rows_scr[:, width:2 * width] = spread_high
        spread_rows_scr[:, 2 * width:3 * width] = spread_low
        weight_cols = jnp.concatenate([weight_high, weight_low, weight_high], axis=1)
        dims = (((1,), (1,)), ((), ()))
        total_scr[...] += lax.dot_general(
            weight_cols, spread_rows_scr[...], dims, preferred_element_type=jnp.float32
        )
        return carry

    lax.fori_loop(0, blocks // GROUP, group, 0)
    deposit_ref[...] = jnp.zeros(deposit_ref.shape, jnp.float32)
    deposit_ref[:, 0:PAIR_ROWS] = total_scr[...].T

    kept_ref[...] = jnp.zeros(kept_ref.shape, jnp.float32)
    outbox_ref[...] = jnp.zeros(outbox_ref.shape, jnp.float32)
    for d in range(27):
        count_scr[d] = 0

    def route(b, carry):
        d = jnp.minimum(jnp.maximum(dest_ref[b], 0), 26)
        alive = b < live

        @pl.when(alive & (d == 13))
        def _():
            kept_ref[:, pl.ds(b, 1), :] = updated_scr[:, pl.ds(b, 1), :]

        rank = count_scr[d]

        @pl.when(alive & (d != 13) & (rank < SLOTS))
        def _():
            outbox_ref[:, pl.ds(d * SLOTS + rank, 1), :] = updated_scr[:, pl.ds(b, 1), :]
            count_scr[d] = rank + 1

        return carry

    lax.fori_loop(0, blocks, route, 0)


def local(gas_state, parcels, parcel_cells, offsets, destination, live_blocks):
    fields, size_x, size_y, size_z = gas_state.shape
    blocks, parcel_fields, block_parcels = parcels.shape
    padded = with_halo(gas_state, (("gx", 1), ("gy", 2), ("gz", 3)), 1)
    span_x = size_x + 2
    span_y = size_y + 2
    span_z = size_z + 2
    pair_count = span_x * span_y
    assert pair_count <= PAIR_ROWS and span_z <= DEPTH_ROWS
    plane_size = span_y * span_z
    table = jnp.transpose(padded, (0, 3, 1, 2)).reshape(fields, span_z, pair_count)
    table = jnp.pad(table, ((0, 0), (0, DEPTH_ROWS - span_z), (0, PAIR_LANES - pair_count)))
    table = table.reshape(fields * DEPTH_ROWS, PAIR_LANES)
    parcel_rows = jnp.transpose(parcels, (1, 0, 2))
    offset_rows = jnp.transpose(offsets, (1, 0, 2))
    relax_time = 0.4 * parcel_rows[0] ** (2.0 / 3.0)
    factors = jnp.stack(
        [
            jnp.exp(-TIME_STEP / relax_time),
            jnp.exp(-TIME_STEP / (1.5 * relax_time)),
            0.4 * jnp.exp(2.0 * (parcel_rows[1] - 1.0)),
        ],
        axis=0,
    )
    vmem = pl.BlockSpec(memory_space=pltpu.VMEM)
    smem = pl.BlockSpec(memory_space=pltpu.SMEM)
    lanes = GROUP * block_parcels
    kept_rows, outbox_rows, deposit_rows = pl.pallas_call(
        functools.partial(coupling_kernel, span_y=span_y, span_z=span_z),
        out_shape=(
            jax.ShapeDtypeStruct(parcel_rows.shape, jnp.float32),
            jax.ShapeDtypeStruct((parcel_fields, 27 * SLOTS, block_parcels), jnp.float32),
            jax.ShapeDtypeStruct((fields * DEPTH_ROWS, PAIR_LANES), jnp.float32),
        ),
        in_specs=[smem, smem] + [vmem] * 5,
        out_specs=(vmem, vmem, vmem),
        scratch_shapes=[
            pltpu.VMEM((PAIR_ROWS, lanes), jnp.float32),
            pltpu.VMEM((DEPTH_ROWS, lanes), jnp.float32),
            pltpu.VMEM((fields * DEPTH_ROWS, lanes), jnp.float32),
            pltpu.VMEM(parcel_rows.shape, jnp.float32),
            pltpu.SMEM((32,), jnp.int32),
            pltpu.VMEM(table.shape, jnp.bfloat16),
            pltpu.VMEM(table.shape, jnp.bfloat16),
            pltpu.VMEM((PAIR_ROWS, fields * DEPTH_ROWS), jnp.float32),
            pltpu.VMEM((fields * DEPTH_ROWS, 3 * PAIR_LANES), jnp.bfloat16),
            pltpu.VMEM((3 * PAIR_LANES, lanes), jnp.bfloat16),
            pltpu.VMEM((fields * DEPTH_ROWS, 3 * lanes), jnp.bfloat16),
        ],
    )(live_blocks, destination, table, parcel_rows, parcel_cells, offset_rows, factors)
    kept = jnp.transpose(kept_rows, (1, 0, 2))
    deposit = deposit_rows.reshape(fields, DEPTH_ROWS, PAIR_LANES)[:, :span_z, :pair_count]
    deposit = jnp.transpose(deposit.reshape(fields, span_z, span_x, span_y), (0, 2, 3, 1))
    cell_sources = fold_ghosts(deposit, (("gx", 1), ("gy", 2), ("gz", 3)))
    kappa = jnp.array(DIFFUSION, jnp.float32)[:, None, None, None]
    gas_next = gas_state + kappa * laplacian(padded) + COUPLING * cell_sources
    outbox = outbox_rows.reshape((parcel_fields, 3, 3, 3, SLOTS, block_parcels))
    widened = with_halo(outbox, (("gx", 1), ("gy", 2), ("gz", 3)), 1)
    arrived_boxes = widened[:, 0::2, 0::2, 0::2]
    arrived = jnp.transpose(
        arrived_boxes.reshape((parcel_fields, 27 * SLOTS, block_parcels)), (1, 0, 2)
    )
    return (gas_next, kept, arrived)


def solution(mesh):
    placed = (
        P(None, "gx", "gy", "gz"),
        P(("gx", "gy", "gz"), None, None),
        P(("gx", "gy", "gz"), None),
        P(("gx", "gy", "gz"), None, None),
        P(("gx", "gy", "gz")),
        P(("gx", "gy", "gz")),
    )
    return jax.shard_map(
        local,
        mesh=mesh,
        in_specs=placed,
        out_specs=(
            P(None, "gx", "gy", "gz"),
            P(("gx", "gy", "gz"), None, None),
            P(("gx", "gy", "gz"), None, None),
        ),
        check_vma=False,
    )
```

```python
import functools

import jax
import jax.numpy as jnp
from jax import lax
from jax.sharding import PartitionSpec as P
from jax.experimental import pallas as pl
from jax.experimental.pallas import tpu as pltpu

SLOTS = 4


DIFFUSION = (0.06, 0.1, 0.12, 0.12, 0.12)
TIME_STEP = 0.5
COUPLING = 0.5
PHASE_CHANGE_COST = 0.5


def with_halo(block, sides, width):
    for axis, dim in sides:
        count = lax.axis_size(axis)
        forward = [(i, i + 1) for i in range(count - 1)]
        backward = [(target, source) for source, target in forward]
        low = lax.ppermute(
            lax.slice_in_dim(block, block.shape[dim] - width, None, axis=dim), axis, forward
        )
        high = lax.ppermute(lax.slice_in_dim(block, 0, width, axis=dim), axis, backward)
        block = jnp.concatenate([low, block, high], axis=dim)
    return block


def fold_ghosts(block, sides):
    for axis, dim in sides:
        count = lax.axis_size(axis)
        forward = [(i, i + 1) for i in range(count - 1)]
        backward = [(target, source) for source, target in forward]
        span = block.shape[dim]
        below = lax.ppermute(lax.slice_in_dim(block, span - 1, span, axis=dim), axis, forward)
        above = lax.ppermute(lax.slice_in_dim(block, 0, 1, axis=dim), axis, backward)
        inner = lax.slice_in_dim(block, 1, span - 1, axis=dim)
        low_pad = [(0, 0)] * block.ndim
        high_pad = [(0, 0)] * block.ndim
        low_pad[dim] = (0, span - 3)
        high_pad[dim] = (span - 3, 0)
        block = inner + jnp.pad(below, low_pad) + jnp.pad(above, high_pad)
    return block


def parcel_update(current_condition, local_air_sample):
    particle_weights_list = current_condition[:, 0]
    parcel_hotness_measure = current_condition[:, 1]
    particle_speed_vector = current_condition[:, 2:5]
    relax_time = 0.4 * particle_weights_list ** (2.0 / 3.0)
    keep_velocity = jnp.exp(-TIME_STEP / relax_time)
    residual_heat_content = jnp.exp(-TIME_STEP / (1.5 * relax_time))
    equilibrium_steam_load = 0.4 * jnp.exp(2.0 * (parcel_hotness_measure - 1.0))
    evaporated_share = 1.0 - jnp.exp(
        -0.3 * jax.nn.softplus(4.0 * (equilibrium_steam_load - local_air_sample[:, 0]))
    )
    evaporated = particle_weights_list * evaporated_share
    ambient_heat_content = local_air_sample[:, 1]
    gas_velocity = local_air_sample[:, 2:5]
    adjusted_heat_content = (
        ambient_heat_content
        + (parcel_hotness_measure - ambient_heat_content) * residual_heat_content
        - PHASE_CHANGE_COST * evaporated_share
    )
    velocity_new = gas_velocity + (particle_speed_vector - gas_velocity) * keep_velocity[:, None]
    enthalpy_injection = (
        0.5 * particle_weights_list * (parcel_hotness_measure - adjusted_heat_content)
    )
    push_source = particle_weights_list[:, None] * (particle_speed_vector - velocity_new)
    updated = jnp.concatenate(
        [
            (particle_weights_list - evaporated)[:, None],
            adjusted_heat_content[:, None],
            velocity_new,
        ],
        axis=1,
    )
    sources = jnp.concatenate(
        [evaporated[:, None], enthalpy_injection[:, None], push_source], axis=1
    )
    return (updated, sources)


def laplacian(padded):
    centre = padded[:, 1:-1, 1:-1, 1:-1]
    beside = padded[:, 2:, 1:-1, 1:-1] + padded[:, :-2, 1:-1, 1:-1]
    beside = beside + padded[:, 1:-1, 2:, 1:-1] + padded[:, 1:-1, :-2, 1:-1]
    beside = beside + padded[:, 1:-1, 1:-1, 2:] + padded[:, 1:-1, 1:-1, :-2]
    return beside - 6.0 * centre


PAIR_LANES = 256
PAIR_ROWS = 192
DEPTH_ROWS = 136


def split_bf16(value):
    high = value.astype(jnp.bfloat16)
    low = (value - high.astype(jnp.float32)).astype(jnp.bfloat16)
    return high, low


def three_pass(a, b, dims):
    a_high, a_low = split_bf16(a)
    b_high, b_low = split_bf16(b)
    out = None
    for x, y in ((a_high, b_high), (a_high, b_low), (a_low, b_high)):
        part = lax.dot_general(x, y, (dims, ((), ())), preferred_element_type=jnp.float32)
        out = part if out is None else out + part
    return out


GROUP = 32


def coupling_kernel(
    live_ref, dest_ref, table_ref, parcel_ref, cell_ref, offset_ref, factor_ref,
    kept_ref, outbox_ref, deposit_ref,
    weight_scr, depth_scr, spread_scr, updated_scr, count_scr, table_high_ref, table_low_ref,
    total_scr, stack_scr, weight_rows_scr, spread_rows_scr, *, span_y, span_z,
):
    fields = parcel_ref.shape[0]
    blocks = parcel_ref.shape[1]
    lanes = parcel_ref.shape[2]
    plane_size = span_y * span_z
    total_scr[...] = jnp.zeros(total_scr.shape, jnp.float32)
    table_high, table_low = split_bf16(table_ref[...])
    stack_scr[:, 0:PAIR_LANES] = table_high
    stack_scr[:, PAIR_LANES:2 * PAIR_LANES] = table_high
    stack_scr[:, 2 * PAIR_LANES:3 * PAIR_LANES] = table_low
    live = live_ref[0]
    pair_iota = lax.broadcasted_iota(jnp.int32, (PAIR_ROWS, lanes), 0)
    weight_rows_scr[...] = jnp.zeros(weight_rows_scr.shape, jnp.bfloat16)
    depth_iota = lax.broadcasted_iota(jnp.int32, (DEPTH_ROWS, lanes), 0)

    def group(g, carry):
        first = pl.multiple_of(g * GROUP, GROUP)
        cells = cell_ref[pl.ds(first, GROUP), :]
        offsets = offset_ref[:, pl.ds(first, GROUP), :]
        parcels = parcel_ref[:, pl.ds(first, GROUP), :]
        factors = factor_ref[:, pl.ds(first, GROUP), :]
        flat = cells.astype(jnp.float32) + 0.5
        cell_x = jnp.floor(flat * (1.0 / plane_size))
        rest = flat - cell_x * plane_size
        cell_y = jnp.floor(rest * (1.0 / span_z))
        cell_z = (rest - cell_y * span_z).astype(jnp.int32)
        cell_x = cell_x.astype(jnp.int32)
        cell_y = cell_y.astype(jnp.int32)
        step_sign = jnp.where(offsets >= 0.0, 1, -1).astype(jnp.int32)
        far_share = jnp.abs(offsets)
        near_share = 1.0 - far_share
        for j in range(GROUP):
            weights = jnp.zeros((PAIR_ROWS, lanes), jnp.float32)
            for bit_x in range(2):
                for bit_y in range(2):
                    share = (far_share[0, j:j + 1] if bit_x else near_share[0, j:j + 1]) * (
                        far_share[1, j:j + 1] if bit_y else near_share[1, j:j + 1]
                    )
                    target = (
                        (cell_x[j:j + 1] + bit_x * step_sign[0, j:j + 1]) * span_y
                        + cell_y[j:j + 1]
                        + bit_y * step_sign[1, j:j + 1]
                    )
                    weights = weights + jnp.where(pair_iota == target, share, 0.0)
            weight_scr[:, j * lanes:(j + 1) * lanes] = weights
            depth_weights = jnp.where(
                depth_iota == cell_z[j:j + 1], near_share[2, j:j + 1], 0.0
            ) + jnp.where(
                depth_iota == cell_z[j:j + 1] + step_sign[2, j:j + 1], far_share[2, j:j + 1], 0.0
            )
            depth_scr[:, j * lanes:(j + 1) * lanes] = depth_weights
        weight_high, weight_low = split_bf16(weight_scr[...])
        width = GROUP * lanes
        weight_rows_scr[0:PAIR_ROWS, :] = weight_high
        weight_rows_scr[PAIR_LANES:PAIR_LANES + PAIR_ROWS, :] = weight_low
        weight_rows_scr[2 * PAIR_LANES:2 * PAIR_LANES + PAIR_ROWS, :] = weight_high
        mixed = jnp.dot(stack_scr[...], weight_rows_scr[...], preferred_element_type=jnp.float32)
        for j in range(GROUP):
            b = first + j
            depth_weights = depth_scr[:, j * lanes:(j + 1) * lanes]
            sample = [
                jnp.sum(
                    mixed[f * DEPTH_ROWS:(f + 1) * DEPTH_ROWS, j * lanes:(j + 1) * lanes]
                    * depth_weights,
                    axis=0,
                    keepdims=True,
                )
                for f in range(fields)
            ]
            mass = parcels[0, j:j + 1]
            heat = parcels[1, j:j + 1]
            keep_velocity = factors[0, j:j + 1]
            residual_heat = factors[1, j:j + 1]
            equilibrium = factors[2, j:j + 1]
            x = 4.0 * (equilibrium - sample[0])
            soft = jnp.maximum(x, 0.0) + jnp.log1p(jnp.exp(-jnp.abs(x)))
            share = 1.0 - jnp.exp(-0.3 * soft)
            evaporated = mass * share
            ambient = sample[1]
            adjusted = ambient + (heat - ambient) * residual_heat - PHASE_CHANGE_COST * share
            velocity = [
                sample[2 + d] + (parcels[2 + d, j:j + 1] - sample[2 + d]) * keep_velocity
                for d in range(3)
            ]
            enthalpy = 0.5 * mass * (heat - adjusted)
            push = [mass * (parcels[2 + d, j:j + 1] - velocity[d]) for d in range(3)]
            rows = [mass - evaporated, adjusted] + velocity
            for f in range(fields):
                updated_scr[f, pl.ds(b, 1), :] = rows[f]
            alive = b < live
            sources = [jnp.where(alive, s, 0.0) for s in [evaporated, enthalpy] + push]
            spread_scr[:, j * lanes:(j + 1) * lanes] = jnp.concatenate(
                [s * depth_weights for s in sources], axis=0
            )
        spread_high, spread_low = split_bf16(spread_scr[...])
        spread_rows_scr[:, 0:width] = spread_high
        spread_rows_scr[:, width:2 * width] = spread_high
        spread_rows_scr[:, 2 * width:3 * width] = spread_low
        weight_cols = jnp.concatenate([weight_high, weight_low, weight_high], axis=1)
        dims = (((1,), (1,)), ((), ()))
        total_scr[...] += lax.dot_general(
            weight_cols, spread_rows_scr[...], dims, preferred_element_type=jnp.float32
        )
        return carry

    lax.fori_loop(0, blocks // GROUP, group, 0)
    deposit_ref[...] = jnp.zeros(deposit_ref.shape, jnp.float32)
    deposit_ref[:, 0:PAIR_ROWS] = total_scr[...].T

    kept_ref[...] = jnp.zeros(kept_ref.shape, jnp.float32)
    outbox_ref[...] = jnp.zeros(outbox_ref.shape, jnp.float32)
    for d in range(27):
        count_scr[d] = 0

    def route(b, carry):
        d = jnp.minimum(jnp.maximum(dest_ref[b], 0), 26)
        alive = b < live

        @pl.when(alive & (d == 13))
        def _():
            kept_ref[:, pl.ds(b, 1), :] = updated_scr[:, pl.ds(b, 1), :]

        rank = count_scr[d]

        @pl.when(alive & (d != 13) & (rank < SLOTS))
        def _():
            outbox_ref[:, pl.ds(d * SLOTS + rank, 1), :] = updated_scr[:, pl.ds(b, 1), :]
            count_scr[d] = rank + 1

        return carry

    lax.fori_loop(0, blocks, route, 0)


def local(gas_state, parcels, parcel_cells, offsets, destination, live_blocks):
    fields, size_x, size_y, size_z = gas_state.shape
    blocks, parcel_fields, block_parcels = parcels.shape
    padded = with_halo(gas_state, (("gx", 1), ("gy", 2), ("gz", 3)), 1)
    span_x = size_x + 2
    span_y = size_y + 2
    span_z = size_z + 2
    pair_count = span_x * span_y
    assert pair_count <= PAIR_ROWS and span_z <= DEPTH_ROWS
    plane_size = span_y * span_z
    table = jnp.transpose(padded, (0, 3, 1, 2)).reshape(fields, span_z, pair_count)
    table = jnp.pad(table, ((0, 0), (0, DEPTH_ROWS - span_z), (0, PAIR_LANES - pair_count)))
    table = table.reshape(fields * DEPTH_ROWS, PAIR_LANES)
    parcel_rows = jnp.transpose(parcels, (1, 0, 2))
    offset_rows = jnp.transpose(offsets, (1, 0, 2))
    relax_time = 0.4 * parcel_rows[0] ** (2.0 / 3.0)
    factors = jnp.stack(
        [
            jnp.exp(-TIME_STEP / relax_time),
            jnp.exp(-TIME_STEP / (1.5 * relax_time)),
            0.4 * jnp.exp(2.0 * (parcel_rows[1] - 1.0)),
        ],
        axis=0,
    )
    vmem = pl.BlockSpec(memory_space=pltpu.VMEM)
    smem = pl.BlockSpec(memory_space=pltpu.SMEM)
    lanes = GROUP * block_parcels
    kept_rows, outbox_rows, deposit_rows = pl.pallas_call(
        functools.partial(coupling_kernel, span_y=span_y, span_z=span_z),
        out_shape=(
            jax.ShapeDtypeStruct(parcel_rows.shape, jnp.float32),
            jax.ShapeDtypeStruct((parcel_fields, 27 * SLOTS, block_parcels), jnp.float32),
            jax.ShapeDtypeStruct((fields * DEPTH_ROWS, PAIR_LANES), jnp.float32),
        ),
        in_specs=[smem, smem] + [vmem] * 5,
        out_specs=(vmem, vmem, vmem),
        scratch_shapes=[
            pltpu.VMEM((PAIR_ROWS, lanes), jnp.float32),
            pltpu.VMEM((DEPTH_ROWS, lanes), jnp.float32),
            pltpu.VMEM((fields * DEPTH_ROWS, lanes), jnp.float32),
            pltpu.VMEM(parcel_rows.shape, jnp.float32),
            pltpu.SMEM((32,), jnp.int32),
            pltpu.VMEM(table.shape, jnp.bfloat16),
            pltpu.VMEM(table.shape, jnp.bfloat16),
            pltpu.VMEM((PAIR_ROWS, fields * DEPTH_ROWS), jnp.float32),
            pltpu.VMEM((fields * DEPTH_ROWS, 3 * PAIR_LANES), jnp.bfloat16),
            pltpu.VMEM((3 * PAIR_LANES, lanes), jnp.bfloat16),
            pltpu.VMEM((fields * DEPTH_ROWS, 3 * lanes), jnp.bfloat16),
        ],
    )(live_blocks, destination, table, parcel_rows, parcel_cells, offset_rows, factors)
    kept = jnp.transpose(kept_rows, (1, 0, 2))
    deposit = deposit_rows.reshape(fields, DEPTH_ROWS, PAIR_LANES)[:, :span_z, :pair_count]
    deposit = jnp.transpose(deposit.reshape(fields, span_z, span_x, span_y), (0, 2, 3, 1))
    cell_sources = fold_ghosts(deposit, (("gx", 1), ("gy", 2), ("gz", 3)))
    kappa = jnp.array(DIFFUSION, jnp.float32)[:, None, None, None]
    gas_next = gas_state + kappa * laplacian(padded) + COUPLING * cell_sources
    outbox = outbox_rows.reshape((parcel_fields, 3, 3, 3, SLOTS, block_parcels))
    widened = with_halo(outbox, (("gx", 1), ("gy", 2), ("gz", 3)), 1)
    arrived_boxes = widened[:, 0::2, 0::2, 0::2]
    arrived = jnp.transpose(
        arrived_boxes.reshape((parcel_fields, 27 * SLOTS, block_parcels)), (1, 0, 2)
    )
    return (gas_next, kept, arrived)


def solution(mesh):
    placed = (
        P(None, "gx", "gy", "gz"),
        P(("gx", "gy", "gz"), None, None),
        P(("gx", "gy", "gz"), None),
        P(("gx", "gy", "gz"), None, None),
        P(("gx", "gy", "gz")),
        P(("gx", "gy", "gz")),
    )
    return jax.shard_map(
        local,
        mesh=mesh,
        in_specs=placed,
        out_specs=(
            P(None, "gx", "gy", "gz"),
            P(("gx", "gy", "gz"), None, None),
            P(("gx", "gy", "gz"), None, None),
        ),
        check_vma=False,
    )
```
